32 devices in a mesh: mem: 8 (over z, x), tp: 4 (over y, core).
Axes of the slice: x: 2, y: 2, z: 4, core: 2. Of those that a mesh axis runs over, the one named last changes fastest.
Arguments:
- tokens: bfloat16 [3072, 2560], P(('mem', 'tp')), may hold values from -48 to 48
- input_weight: bfloat16 [2560, 6144], P(None, 'tp'), may hold values from -0.125 to 0.125
- output_weight: bfloat16 [2048, 2560], P('tp'), may hold values from -0.125 to 0.125
- gate_logit: float32 [16], P('tp'), may hold values from -2 to 2
- memory: bfloat16 [2, 32768, 2048], P(None, 'mem', 'tp'), may hold values from -48 to 48
- retrieved: int32 [24, 16], P('mem'), may hold values from 0 to 255, as said below
- block_home: int32 [256], replicated, may hold values from 0 to 255, as said below
Outputs:
- mixed: bfloat16 [3072, 2560], P(('mem', 'tp'))
The draws below stay inside these ranges and needn't reach their ends.
Inputs may be any that keep to these rules, and one draw needn't show every extreme that they name: `block_home`: A permutation: each logical block names one stored block; stored block s lies with index s // 32 of mem, as its block s % 32. `retrieved`: each row names 16 different logical blocks; rows i * 3 to i * 3 + 2 are the query blocks of index i of mem. A row names at most 2 blocks held by one index of mem, and all rows of one index of mem together name at most 2 different blocks held by one index of mem.
All inputs are finite; a program needn't handle non-finite values.
Results may differ from the reference program's by a relative error of at most 0.023.
Values may be sent and summed in bfloat16 or wider, within the bound.
No kernel may reach another device: no remote copies, remote signals or barrier semaphores. Data moves between devices by JAX's collectives and lax.ppermute only.
A program may use at most 128 MiB of HBM per device.

```python
import jax
import jax.numpy as jnp
from jax import lax

D = 2560
HEADS = 16
HD = 128
BLK = 128
TOPB = 16
CAP = 2
MB_DEV = 32
QB_DEV = 3
POOL = 16
TOKENS = 3072
QBLOCKS = 24
MEMBLK = 256
MEMTOK = 32768
N_TP = 4


def retrieval_tables(key):
    key = jax.random.fold_in(key, 77)
    keys_split = jax.random.split(key, 7)
    holder_count = MEMBLK // MB_DEV
    home = jax.random.permutation(keys_split[0], MEMBLK).astype(jnp.int32)
    block_of_slot = jnp.argsort(home).astype(jnp.int32)
    most_popular = jax.random.randint(keys_split[1], (), 0, holder_count)
    popularity = jax.random.permutation(keys_split[2], holder_count).astype(jnp.int32)
    candidate_blocks = holder_count * CAP
    candidate_holder = jnp.arange(candidate_blocks, dtype=jnp.int32) // CAP
    random_jitter = jax.random.randint(keys_split[3], (holder_count, candidate_blocks), 0, holder_count)
    slight_tilt = (holder_count - popularity[candidate_holder]) // 2
    extra_credit = jnp.where(candidate_holder == most_popular, 4 * holder_count, 0)
    block_ranking = (random_jitter + slight_tilt[None, :] + extra_credit[None, :]) * candidate_blocks + jnp.arange(candidate_blocks, dtype=jnp.int32)[None, :]
    chosen = jnp.argsort(-block_ranking, axis=1)[:, :POOL].astype(jnp.int32)
    pool_owner = chosen // CAP
    pool_member = chosen % CAP
    starting = jax.random.randint(keys_split[4], (holder_count, holder_count), 0, MB_DEV)
    pool_local = (jnp.take_along_axis(starting, pool_owner, axis=1) + pool_member) % MB_DEV
    pool_block = block_of_slot[pool_owner * MB_DEV + pool_local]
    rest = POOL - CAP
    pick_score = jax.random.randint(keys_split[5], (QBLOCKS, rest), 0, 1 << 20) * rest + jnp.arange(rest, dtype=jnp.int32)[None, :]
    picked = jnp.argsort(-pick_score, axis=1)[:, :TOPB - CAP].astype(jnp.int32) + CAP
    leading = jnp.broadcast_to(jnp.arange(CAP, dtype=jnp.int32)[None, :], (QBLOCKS, CAP))
    positions = jnp.concatenate([leading, picked], axis=1)
    order_score = jax.random.randint(keys_split[6], (QBLOCKS, TOPB), 0, 1 << 20) * TOPB + jnp.arange(TOPB, dtype=jnp.int32)[None, :]
    shuffle = jnp.argsort(order_score, axis=1).astype(jnp.int32)
    positions = jnp.take_along_axis(positions, shuffle, axis=1)
    device_of_row = jnp.arange(QBLOCKS, dtype=jnp.int32) // QB_DEV
    lists = jnp.take_along_axis(pool_block[device_of_row], positions, axis=1)
    return (home, lists.astype(jnp.int32))


def draw_retrieved(key, part):
    return retrieval_tables(key)[1]


def draw_block_home(key, part):
    return retrieval_tables(key)[0]


def draw_tokens(key, part):
    values = jnp.clip(jax.random.normal(key, (TOKENS, D), jnp.float32), -6.0, 6.0)
    return values.astype(jnp.bfloat16)


def draw_memory(key, part):
    values = jnp.clip(jax.random.normal(key, (2, MEMTOK, HEADS * HD), jnp.float32), -6.0, 6.0)
    return values.astype(jnp.bfloat16)


def block_scale(key, dims, pieces, low, largest):
    def one(position, parts):
        draws = jax.random.uniform(jax.random.fold_in(jax.random.fold_in(key, 6), position), (parts,), jnp.float32, low / len(pieces), largest / len(pieces))
        return jnp.repeat(jnp.exp(draws), dims[position] // parts).reshape((-1,) + (1,) * (len(dims) - position - 1))

    loudness = one(*pieces[0])
    for cut in pieces[1:]:
        loudness = loudness * one(*cut)
    return loudness


def scatter_about(rng, extent, scale, limit, pieces=(), held_as=jnp.bfloat16):
    level = block_scale(rng, extent, pieces, -0.22, 0.18) if pieces else 1.0
    entries = jax.random.normal(rng, extent, jnp.float32) * scale * level
    return jnp.minimum(jnp.maximum(entries, -limit), limit).astype(held_as)


def setup_inputs(seed: int = 0) -> dict:
    arg_keys = jax.random.split(jax.random.key(seed), 8)
    tokens = draw_tokens(jax.random.fold_in(arg_keys[7], 71), 0)
    input_weight = scatter_about(arg_keys[1], (D, HEADS * 3 * HD), D ** -0.5, 0.125, ((1, 4),))
    output_weight = scatter_about(arg_keys[2], (HEADS * HD, D), (HEADS * HD) ** -0.5, 0.125, ((0, 4),))
    gate_logit = jnp.clip(jax.random.uniform(arg_keys[3], (HEADS,), jnp.float32, -2.0, 2.0) * block_scale(arg_keys[3], (HEADS,), ((0, 4),), -0.4, 0.0), -2.0, 2.0)
    memory = draw_memory(jax.random.fold_in(arg_keys[7], 71), 0)
    retrieved = draw_retrieved(jax.random.fold_in(arg_keys[7], 71), 0)
    block_home = draw_block_home(jax.random.fold_in(arg_keys[7], 71), 0)
    return dict(tokens=tokens, input_weight=input_weight, output_weight=output_weight, gate_logit=gate_logit, memory=memory, retrieved=retrieved, block_home=block_home)


NEG_FILL = -1e30


def softmax_rows(scores, allowed):
    row_peak = jnp.max(jnp.where(allowed, scores, NEG_FILL), axis=-1, keepdims=True)
    weights = jnp.where(allowed, jnp.exp(scores - row_peak), 0.0)
    return (weights / jnp.sum(weights, axis=-1, keepdims=True)).astype(jnp.bfloat16)


def reference(tokens, input_weight, output_weight, gate_logit, memory, retrieved, block_home):
    score_scale = HD ** -0.5
    projected = jnp.dot(tokens, input_weight, preferred_element_type=jnp.float32).astype(jnp.bfloat16)
    projected = projected.reshape(TOKENS, HEADS, 3, HD)
    queries = projected[:, :, 0]
    key_rows = projected[:, :, 1]
    value_rows = projected[:, :, 2]
    zero_rows = jnp.zeros((BLK, HEADS, HD), jnp.bfloat16)
    padded_keys = jnp.concatenate([zero_rows, key_rows], axis=0)
    padded_values = jnp.concatenate([zero_rows, value_rows], axis=0)
    store = memory.reshape(2, MEMBLK, BLK, HEADS, HD)
    mixing = jax.nn.sigmoid(gate_logit)[None, :, None]
    query_index = lax.broadcasted_iota(jnp.int32, (BLK, 2 * BLK), 0)
    key_index = lax.broadcasted_iota(jnp.int32, (BLK, 2 * BLK), 1)

    def one_block(block):
        first_row = (block * BLK).astype(jnp.int32)
        block_queries = lax.dynamic_slice_in_dim(queries, first_row, BLK, 0).astype(jnp.float32)
        near_keys = lax.dynamic_slice_in_dim(padded_keys, first_row, 2 * BLK, 0).astype(jnp.float32)
        near_values = lax.dynamic_slice_in_dim(padded_values, first_row, 2 * BLK, 0).astype(jnp.float32)
        near_scores = jnp.einsum("qhd,khd->hqk", block_queries, near_keys) * score_scale
        allowed = (key_index > query_index) & (key_index <= query_index + BLK) & (key_index + first_row - BLK >= 0)
        near_probs = softmax_rows(near_scores, allowed[None]).astype(jnp.float32)
        near_out = jnp.einsum("hqk,khd->qhd", near_probs, near_values)
        home_slots = jnp.take(block_home, retrieved[block]).astype(jnp.int32)
        far_pairs = jnp.take(store, home_slots, axis=1).reshape(2, TOPB * BLK, HEADS, HD).astype(jnp.float32)
        far_scores = jnp.einsum("qhd,khd->hqk", block_queries, far_pairs[0]) * score_scale
        far_probs = softmax_rows(far_scores, True).astype(jnp.float32)
        far_out = jnp.einsum("hqk,khd->qhd", far_probs, far_pairs[1])
        return (mixing * far_out + (1.0 - mixing) * near_out).astype(jnp.bfloat16)

    attended = lax.map(one_block, jnp.arange(QBLOCKS, dtype=jnp.int32)).reshape(TOKENS, HEADS * HD)
    head_group = HEADS // N_TP
    grouped = attended.reshape(TOKENS, N_TP, head_group * HD)
    weight_groups = output_weight.reshape(N_TP, head_group * HD, D)

    def add_group(total, member):
        term = jnp.dot(grouped[:, member], weight_groups[member], preferred_element_type=jnp.float32)
        rounded = lax.optimization_barrier(term.astype(jnp.bfloat16)).astype(jnp.float32)
        return total + rounded, None

    total, unused = lax.scan(add_group, jnp.zeros((TOKENS, D), jnp.float32), jnp.arange(N_TP, dtype=jnp.int32))
    return total.astype(jnp.bfloat16)
```

```python
import jax
import jax.numpy as jnp
from jax import lax
from jax.sharding import PartitionSpec as P

HD = 128
BLK = 128
TOPB = 16
CAP = 2


NEG_FILL = -1e30


def from_behind(value, axis, steps):
    count = lax.axis_size(axis)
    initial, last = (max(0, -steps), min(count, count - steps))
    return lax.ppermute(value, axis, [(source, source + steps) for source in range(initial, last)])


def softmax_rows(scores, allowed):
    row_peak = jnp.max(jnp.where(allowed, scores, NEG_FILL), axis=-1, keepdims=True)
    weights = jnp.where(allowed, jnp.exp(scores - row_peak), 0.0)
    return (weights / jnp.sum(weights, axis=-1, keepdims=True)).astype(jnp.bfloat16)


def local(tokens, input_weight, output_weight, gate_logit, memory, retrieved, block_home):
    holder_count = lax.axis_size("mem")
    share_rows = tokens.shape[0]
    local_rows = share_rows * lax.axis_size("tp")
    groups = output_weight.shape[0] // HD
    score_scale = HD ** (-0.5)
    projected = jnp.dot(
        lax.all_gather(tokens, "tp", axis=0, tiled=True),
        input_weight,
        preferred_element_type=jnp.float32,
    )
    projected = projected.astype(jnp.bfloat16).reshape(local_rows, groups, 3, HD)
    queries = projected[:, :, 0]
    key_rows = projected[:, :, 1]
    value_rows = projected[:, :, 2]
    last_rows = jnp.stack([key_rows[-BLK:], value_rows[-BLK:]]).reshape(2, BLK, groups * HD)
    before = from_behind(last_rows, "mem", 1).reshape(2, BLK, groups, HD)
    near_keys = jnp.concatenate([before[0], key_rows], axis=0)
    near_values = jnp.concatenate([before[1], value_rows], axis=0)
    near_scores = (
        jnp.einsum("qgd,kgd->gqk", queries, near_keys, preferred_element_type=jnp.float32)
        * score_scale
    )
    query_index = lax.broadcasted_iota(jnp.int32, (local_rows, local_rows + BLK), 0)
    key_index = lax.broadcasted_iota(jnp.int32, (local_rows, local_rows + BLK), 1)
    first_key = lax.axis_index("mem") * local_rows - BLK
    allowed = (
        (key_index > query_index) & (key_index <= query_index + BLK) & (key_index + first_key >= 0)
    )
    near_probs = softmax_rows(near_scores, allowed[None])
    near_out = jnp.einsum(
        "gqk,kgd->qgd", near_probs, near_values, preferred_element_type=jnp.float32
    )
    blocks_here = retrieved.shape[0]
    entries = blocks_here * TOPB
    local_blocks = memory.shape[1] // BLK
    flat_blocks = retrieved.reshape(entries)
    home_slot = jnp.take(block_home, flat_blocks)
    holder = home_slot // local_blocks
    local_block = home_slot % local_blocks
    local_store = memory.reshape(2, local_blocks, BLK, groups * HD)
    entry_order = jnp.arange(entries)
    earlier = entry_order[None, :] < entry_order[:, None]
    same_owner = holder[:, None] == holder[None, :]
    same_block = home_slot[:, None] == home_slot[None, :]
    first = jnp.sum(same_block & earlier, axis=1) == 0
    first_entry = jnp.argmax(same_block, axis=1)
    before_first = entry_order[None, :] < first_entry[:, None]
    slot_of = jnp.sum(same_owner & before_first & first[None, :], axis=1)
    wanted_ids = (
        jnp.zeros((holder_count, CAP), jnp.int32).at[holder, slot_of].set(local_block)
    )
    picked = jnp.take(
        local_store,
        lax.all_to_all(wanted_ids, "mem", split_axis=0, concat_axis=0, tiled=True).reshape(
            holder_count * CAP
        ),
        axis=1,
    )
    fetched = lax.all_to_all(picked, "mem", split_axis=1, concat_axis=1, tiled=True)
    pool = holder_count * CAP
    far_keys = fetched[0].reshape(pool * BLK, groups, HD)
    far_values = fetched[1].reshape(pool * BLK, groups, HD)
    row_of = entry_order // TOPB
    member = (
        jnp.zeros((blocks_here, pool), jnp.bool_).at[row_of, holder * CAP + slot_of].set(True)
    )
    far_allowed = jnp.repeat(member, BLK, axis=1)[:, None, None, :]
    block_queries = queries.reshape(blocks_here, BLK, groups, HD)
    far_scores = (
        jnp.einsum(
            "bqgd,kgd->bgqk", block_queries, far_keys, preferred_element_type=jnp.float32
        )
        * score_scale
    )
    far_probs = softmax_rows(far_scores, far_allowed)
    far_out = jnp.einsum(
        "bgqk,kgd->bqgd", far_probs, far_values, preferred_element_type=jnp.float32
    )
    far_out = far_out.reshape(local_rows, groups, HD)
    mixing = jax.nn.sigmoid(gate_logit)[None, :, None]
    attended = (
        (mixing * far_out + (1.0 - mixing) * near_out)
        .astype(jnp.bfloat16)
        .reshape(local_rows, groups * HD)
    )
    return lax.psum_scatter(
        jnp.dot(attended, output_weight, preferred_element_type=jnp.float32).astype(jnp.bfloat16),
        "tp",
        scatter_dimension=0,
        tiled=True,
    )


def solution(mesh):
    placed = (
        P(("mem", "tp"), None),
        P(None, "tp"),
        P("tp", None),
        P("tp"),
        P(None, "mem", "tp"),
        P("mem", None),
        P(),
    )
    return jax.shard_map(
        local, mesh=mesh, in_specs=placed, out_specs=P(("mem", "tp"), None), check_vma=False
    )
```

```python
import jax
import jax.numpy as jnp
from jax import lax
from jax.sharding import PartitionSpec as P
from jax.experimental import pallas as pl
from jax.experimental.pallas import tpu as pltpu

HD = 128
BLK = 128
TOPB = 16
CAP = 2


NEG_FILL = -1e30


def from_behind(value, axis, steps):
    count = lax.axis_size(axis)
    initial, last = (max(0, -steps), min(count, count - steps))
    return lax.ppermute(value, axis, [(source, source + steps) for source in range(initial, last)])


def softmax_rows(scores, allowed):
    row_peak = jnp.max(jnp.where(allowed, scores, NEG_FILL), axis=-1, keepdims=True)
    weights = jnp.where(allowed, jnp.exp(scores - row_peak), 0.0)
    return (weights / jnp.sum(weights, axis=-1, keepdims=True)).astype(jnp.bfloat16)


def far_kernel(q_ref, k_ref, v_ref, allow_ref, o_ref):
    pool = k_ref.shape[1]
    keys = k_ref[0].reshape(pool * BLK, HD)
    values = v_ref[0].reshape(pool * BLK, HD)
    scores = lax.dot_general(
        q_ref[...], keys, (((1,), (1,)), ((), ())), preferred_element_type=jnp.float32
    ) * (HD ** (-0.5))
    allowed = allow_ref[0] > 0
    peak = jnp.max(jnp.where(allowed, scores, NEG_FILL), axis=-1, keepdims=True)
    weights = jnp.where(allowed, jnp.exp(scores - peak), 0.0)
    probs = (weights / jnp.sum(weights, axis=-1, keepdims=True)).astype(jnp.bfloat16)
    o_ref[...] = jnp.dot(probs, values, preferred_element_type=jnp.float32)


def far_attention(projected, fetched, allow):
    rows = projected.shape[0]
    blocks = rows // BLK
    pool = fetched.shape[1]
    groups = fetched.shape[3] // HD
    steps = groups * blocks
    return pl.pallas_call(
        far_kernel,
        grid=(groups, blocks),
        in_specs=[
            pl.BlockSpec((BLK, HD), lambda h, b: (b, h * 3)),
            pl.BlockSpec((1, pool, BLK, HD), lambda h, b: (0, 0, 0, h)),
            pl.BlockSpec((1, pool, BLK, HD), lambda h, b: (1, 0, 0, h)),
            pl.BlockSpec((1, 1, pool * BLK), lambda h, b: (b, 0, 0)),
        ],
        out_specs=pl.BlockSpec((BLK, HD), lambda h, b: (b, h)),
        out_shape=jax.ShapeDtypeStruct((rows, groups * HD), jnp.float32),
        cost_estimate=pl.CostEstimate(
            flops=steps * 4 * BLK * pool * BLK * HD,
            transcendentals=steps * BLK * pool * BLK,
            bytes_accessed=fetched.size * 2 + rows * groups * HD * 6,
        ),
    )(projected, fetched, fetched, allow)


def local(tokens, input_weight, output_weight, gate_logit, memory, retrieved, block_home):
    holder_count = lax.axis_size("mem")
    share_rows = tokens.shape[0]
    local_rows = share_rows * lax.axis_size("tp")
    groups = output_weight.shape[0] // HD
    score_scale = HD ** (-0.5)
    projected = jnp.dot(
        lax.all_gather(tokens, "tp", axis=0, tiled=True),
        input_weight,
        preferred_element_type=jnp.float32,
    )
    projected_flat = projected.astype(jnp.bfloat16)
    projected = projected_flat.reshape(local_rows, groups, 3, HD)
    queries = projected[:, :, 0]
    key_rows = projected[:, :, 1]
    value_rows = projected[:, :, 2]
    last_rows = jnp.stack([key_rows[-BLK:], value_rows[-BLK:]]).reshape(2, BLK, groups * HD)
    before = from_behind(last_rows, "mem", 1).reshape(2, BLK, groups, HD)
    near_keys = jnp.concatenate([before[0], key_rows], axis=0)
    near_values = jnp.concatenate([before[1], value_rows], axis=0)
    near_scores = (
        jnp.einsum("qgd,kgd->gqk", queries, near_keys, preferred_element_type=jnp.float32)
        * score_scale
    )
    query_index = lax.broadcasted_iota(jnp.int32, (local_rows, local_rows + BLK), 0)
    key_index = lax.broadcasted_iota(jnp.int32, (local_rows, local_rows + BLK), 1)
    first_key = lax.axis_index("mem") * local_rows - BLK
    allowed = (
        (key_index > query_index) & (key_index <= query_index + BLK) & (key_index + first_key >= 0)
    )
    near_probs = softmax_rows(near_scores, allowed[None])
    near_out = jnp.einsum(
        "gqk,kgd->qgd", near_probs, near_values, preferred_element_type=jnp.float32
    )
    blocks_here = retrieved.shape[0]
    entries = blocks_here * TOPB
    local_blocks = memory.shape[1] // BLK
    flat_blocks = retrieved.reshape(entries)
    home_slot = jnp.take(block_home, flat_blocks)
    holder = home_slot // local_blocks
    local_block = home_slot % local_blocks
    local_store = memory.reshape(2, local_blocks, BLK, groups * HD)
    entry_order = jnp.arange(entries)
    earlier = entry_order[None, :] < entry_order[:, None]
    same_owner = holder[:, None] == holder[None, :]
    same_block = home_slot[:, None] == home_slot[None, :]
    first = jnp.sum(same_block & earlier, axis=1) == 0
    first_entry = jnp.argmax(same_block, axis=1)
    before_first = entry_order[None, :] < first_entry[:, None]
    slot_of = jnp.sum(same_owner & before_first & first[None, :], axis=1)
    wanted_ids = (
        jnp.zeros((holder_count, CAP), jnp.int32).at[holder, slot_of].set(local_block)
    )
    picked = jnp.take(
        local_store,
        lax.all_to_all(wanted_ids, "mem", split_axis=0, concat_axis=0, tiled=True).reshape(
            holder_count * CAP
        ),
        axis=1,
        mode="clip",
    )
    fetched = lax.all_to_all(picked, "mem", split_axis=1, concat_axis=1, tiled=True)
    pool = holder_count * CAP
    row_of = entry_order // TOPB
    member = (
        jnp.zeros((blocks_here, pool), jnp.float32).at[row_of, holder * CAP + slot_of].set(1.0)
    )
    allow = jnp.repeat(member, BLK, axis=1).reshape(blocks_here, 1, pool * BLK)
    far_out = far_attention(projected_flat, fetched, allow).reshape(local_rows, groups, HD)
    mixing = jax.nn.sigmoid(gate_logit)[None, :, None]
    attended = (
        (mixing * far_out + (1.0 - mixing) * near_out)
        .astype(jnp.bfloat16)
        .reshape(local_rows, groups * HD)
    )
    return lax.psum_scatter(
        jnp.dot(attended, output_weight, preferred_element_type=jnp.float32).astype(jnp.bfloat16),
        "tp",
        scatter_dimension=0,
        tiled=True,
    )


def solution(mesh):
    placed = (
        P(("mem", "tp"), None),
        P(None, "tp"),
        P("tp", None),
        P("tp"),
        P(None, "mem", "tp"),
        P("mem", None),
        P(),
    )
    return jax.shard_map(
        local, mesh=mesh, in_specs=placed, out_specs=P(("mem", "tp"), None), check_vma=False
    )
```

```python
import jax
import jax.numpy as jnp
from jax import lax
from jax.sharding import PartitionSpec as P
from jax.experimental import pallas as pl
from jax.experimental.pallas import tpu as pltpu

HD = 128
BLK = 128
TOPB = 16
CAP = 2


NEG_FILL = -1e30


def from_behind(value, axis, steps):
    count = lax.axis_size(axis)
    initial, last = (max(0, -steps), min(count, count - steps))
    return lax.ppermute(value, axis, [(source, source + steps) for source in range(initial, last)])


def softmax_rows(scores, allowed):
    row_peak = jnp.max(jnp.where(allowed, scores, NEG_FILL), axis=-1, keepdims=True)
    weights = jnp.where(allowed, jnp.exp(scores - row_peak), 0.0)
    return (weights / jnp.sum(weights, axis=-1, keepdims=True)).astype(jnp.bfloat16)


def far_kernel(q_ref, k_ref, v_ref, allow_ref, o_ref):
    pool = k_ref.shape[1]
    keys = k_ref[0].reshape(pool * BLK, HD)
    values = v_ref[0].reshape(pool * BLK, HD)
    scores = lax.dot_general(
        q_ref[...], keys, (((1,), (1,)), ((), ())), preferred_element_type=jnp.float32
    ) * (HD ** (-0.5))
    allowed = allow_ref[0] > 0
    peak = jnp.max(jnp.where(allowed, scores, NEG_FILL), axis=-1, keepdims=True)
    weights = jnp.where(allowed, jnp.exp(scores - peak), 0.0)
    probs = (weights / jnp.sum(weights, axis=-1, keepdims=True)).astype(jnp.bfloat16)
    o_ref[...] = jnp.dot(probs, values, preferred_element_type=jnp.float32)


def far_attention(projected, fetched, allow):
    rows = projected.shape[0]
    blocks = rows // BLK
    pool = fetched.shape[1]
    groups = fetched.shape[3] // HD
    steps = groups * blocks
    return pl.pallas_call(
        far_kernel,
        grid=(groups, blocks),
        in_specs=[
            pl.BlockSpec((BLK, HD), lambda h, b: (b, h * 3)),
            pl.BlockSpec((1, pool, BLK, HD), lambda h, b: (0, 0, 0, h)),
            pl.BlockSpec((1, pool, BLK, HD), lambda h, b: (1, 0, 0, h)),
            pl.BlockSpec((1, 1, pool * BLK), lambda h, b: (b, 0, 0)),
        ],
        out_specs=pl.BlockSpec((BLK, HD), lambda h, b: (b, h)),
        out_shape=jax.ShapeDtypeStruct((rows, groups * HD), jnp.float32),
        cost_estimate=pl.CostEstimate(
            flops=steps * 4 * BLK * pool * BLK * HD,
            transcendentals=steps * BLK * pool * BLK,
            bytes_accessed=fetched.size * 2 + rows * groups * HD * 6,
        ),
    )(projected, fetched, fetched, allow)


def local(tokens, input_weight, output_weight, gate_logit, memory, retrieved, block_home):
    holder_count = lax.axis_size("mem")
    share_rows = tokens.shape[0]
    local_rows = share_rows * lax.axis_size("tp")
    groups = output_weight.shape[0] // HD
    score_scale = HD ** (-0.5)
    projected = jnp.dot(
        lax.all_gather(tokens, "tp", axis=0, tiled=True),
        input_weight,
        preferred_element_type=jnp.float32,
    )
    projected_flat = projected.astype(jnp.bfloat16)
    projected = projected_flat.reshape(local_rows, groups, 3, HD)
    queries = projected[:, :, 0]
    key_rows = projected[:, :, 1]
    value_rows = projected[:, :, 2]
    last_rows = jnp.stack([key_rows[-BLK:], value_rows[-BLK:]]).reshape(2, BLK, groups * HD)
    before = from_behind(last_rows, "mem", 1).reshape(2, BLK, groups, HD)
    near_keys = jnp.concatenate([before[0], key_rows], axis=0)
    near_values = jnp.concatenate([before[1], value_rows], axis=0)
    near_scores = (
        jnp.einsum("qgd,kgd->gqk", queries, near_keys, preferred_element_type=jnp.float32)
        * score_scale
    )
    query_index = lax.broadcasted_iota(jnp.int32, (local_rows, local_rows + BLK), 0)
    key_index = lax.broadcasted_iota(jnp.int32, (local_rows, local_rows + BLK), 1)
    first_key = lax.axis_index("mem") * local_rows - BLK
    allowed = (
        (key_index > query_index) & (key_index <= query_index + BLK) & (key_index + first_key >= 0)
    )
    near_probs = softmax_rows(near_scores, allowed[None])
    near_out = jnp.einsum(
        "gqk,kgd->qgd", near_probs, near_values, preferred_element_type=jnp.float32
    )
    blocks_here = retrieved.shape[0]
    entries = blocks_here * TOPB
    local_blocks = memory.shape[1] // BLK
    flat_blocks = retrieved.reshape(entries)
    home_slot = jnp.take(block_home, flat_blocks)
    holder = home_slot // local_blocks
    local_block = home_slot % local_blocks
    local_store = memory.reshape(2, local_blocks, BLK, groups * HD)
    entry_order = jnp.arange(entries)
    earlier = entry_order[None, :] < entry_order[:, None]
    same_owner = holder[:, None] == holder[None, :]
    same_block = home_slot[:, None] == home_slot[None, :]
    first = jnp.sum(same_block & earlier, axis=1) == 0
    first_entry = jnp.argmax(same_block, axis=1)
    before_first = entry_order[None, :] < first_entry[:, None]
    slot_of = jnp.sum(same_owner & before_first & first[None, :], axis=1)
    wanted_ids = (
        jnp.zeros((holder_count, CAP), jnp.int32).at[holder, slot_of].set(local_block)
    )
    picked = jnp.take(
        local_store,
        lax.all_to_all(wanted_ids, "mem", split_axis=0, concat_axis=0, tiled=True).reshape(
            holder_count * CAP
        ),
        axis=1,
        mode="clip",
    )
    fetched = lax.all_to_all(picked, "mem", split_axis=1, concat_axis=1, tiled=True)
    pool = holder_count * CAP
    row_of = entry_order // TOPB
    member = (
        jnp.zeros((blocks_here, pool), jnp.float32).at[row_of, holder * CAP + slot_of].set(1.0)
    )
    allow = jnp.repeat(member, BLK, axis=1).reshape(blocks_here, 1, pool * BLK)
    far_out = far_attention(projected_flat, fetched, allow).reshape(local_rows, groups, HD)
    mixing = jax.nn.sigmoid(gate_logit)[None, :, None]
    attended = (
        (mixing * far_out + (1.0 - mixing) * near_out)
        .astype(jnp.bfloat16)
        .reshape(local_rows, groups * HD)
    )
    partial = jnp.dot(attended, output_weight, preferred_element_type=jnp.float32)
    return reduce_over_tp(partial).astype(jnp.bfloat16)


def reduce_over_tp(partial):
    count = lax.axis_size("tp")
    chips = count // 2
    share = partial.shape[0] // count
    me = lax.axis_index("tp")
    core = me % 2
    chip = me // 2
    split = partial.reshape(chips, 2, share, partial.shape[1])
    mine = lax.dynamic_index_in_dim(split, core, axis=1, keepdims=False)
    other = lax.dynamic_index_in_dim(split, 1 - core, axis=1, keepdims=False)
    arrived = lax.ppermute(
        other.astype(jnp.bfloat16), "tp", [(t, t ^ 1) for t in range(count)]
    )
    chip_sum = mine + arrived.astype(jnp.float32)
    total = lax.dynamic_index_in_dim(chip_sum, chip, axis=0, keepdims=False)
    for shift in range(1, chips):
        outgoing = lax.dynamic_index_in_dim(chip_sum, (chip + shift) % chips, axis=0, keepdims=False)
        pairs = [(t, ((t // 2 + shift) % chips) * 2 + t % 2) for t in range(count)]
        total = total + lax.ppermute(outgoing.astype(jnp.bfloat16), "tp", pairs).astype(jnp.float32)
    return total

def solution(mesh):
    placed = (
        P(("mem", "tp"), None),
        P(None, "tp"),
        P("tp", None),
        P("tp"),
        P(None, "mem", "tp"),
        P("mem", None),
        P(),
    )
    return jax.shard_map(
        local, mesh=mesh, in_specs=placed, out_specs=P(("mem", "tp"), None), check_vma=False
    )
```

```python
import jax
import jax.numpy as jnp
from jax import lax
from jax.sharding import PartitionSpec as P
from jax.experimental import pallas as pl
from jax.experimental.pallas import tpu as pltpu

HD = 128
BLK = 128
TOPB = 16
CAP = 2


NEG_FILL = -1e30


def from_behind(value, axis, steps):
    count = lax.axis_size(axis)
    initial, last = (max(0, -steps), min(count, count - steps))
    return lax.ppermute(value, axis, [(source, source + steps) for source in range(initial, last)])


def softmax_rows(scores, allowed):
    row_peak = jnp.max(jnp.where(allowed, scores, NEG_FILL), axis=-1, keepdims=True)
    weights = jnp.where(allowed, jnp.exp(scores - row_peak), 0.0)
    return (weights / jnp.sum(weights, axis=-1, keepdims=True)).astype(jnp.bfloat16)


def far_kernel(q_ref, k_ref, v_ref, bias_ref, o_ref):
    pool = k_ref.shape[0]
    keys = k_ref[:, 0].reshape(pool * BLK, HD)
    values = v_ref[:, 0].reshape(pool * BLK, HD)
    scores = lax.dot_general(
        q_ref[...], keys, (((1,), (1,)), ((), ())), preferred_element_type=jnp.float32
    ) * (HD ** (-0.5)) + bias_ref[0]
    peak = jnp.max(scores, axis=-1, keepdims=True)
    weights = jnp.exp(scores - peak)
    scale = 1.0 / jnp.sum(weights, axis=-1, keepdims=True)
    probs = (weights * scale).astype(jnp.bfloat16)
    o_ref[...] = jnp.dot(probs, values, preferred_element_type=jnp.float32)


def far_attention(projected, fetched, bias):
    rows = projected.shape[0]
    blocks = rows // BLK
    pool = fetched.shape[0]
    groups = fetched.shape[3] // HD
    steps = groups * blocks
    return pl.pallas_call(
        far_kernel,
        grid=(groups, blocks),
        in_specs=[
            pl.BlockSpec((BLK, HD), lambda h, b: (b, h * 3)),
            pl.BlockSpec((pool, 1, BLK, HD), lambda h, b: (0, 0, 0, h)),
            pl.BlockSpec((pool, 1, BLK, HD), lambda h, b: (0, 1, 0, h)),
            pl.BlockSpec((1, 1, pool * BLK), lambda h, b: (b, 0, 0)),
        ],
        out_specs=pl.BlockSpec((BLK, HD), lambda h, b: (b, h)),
        out_shape=jax.ShapeDtypeStruct((rows, groups * HD), jnp.float32),
        cost_estimate=pl.CostEstimate(
            flops=steps * 4 * BLK * pool * BLK * HD,
            transcendentals=steps * BLK * pool * BLK,
            bytes_accessed=fetched.size * 2 + rows * groups * HD * 6,
        ),
    )(projected, fetched, fetched, bias)


def gather_tp(part):
    count = lax.axis_size("tp")
    me = lax.axis_index("tp")
    arrived = [part] + [
        lax.ppermute(part, "tp", [(t, (t + shift) % count) for t in range(count)])
        for shift in range(1, count)
    ]
    order = (me - jnp.arange(count)) % count
    return jnp.take(jnp.stack(arrived), order, axis=0, mode="clip").reshape(
        count * part.shape[0], part.shape[1]
    )

def local(tokens, input_weight, output_weight, gate_logit, memory, retrieved, block_home):
    holder_count = lax.axis_size("mem")
    share_rows = tokens.shape[0]
    local_rows = share_rows * lax.axis_size("tp")
    groups = output_weight.shape[0] // HD
    score_scale = HD ** (-0.5)
    projected = jnp.dot(
        gather_tp(tokens),
        input_weight,
        preferred_element_type=jnp.float32,
    )
    projected_flat = projected.astype(jnp.bfloat16)
    projected = projected_flat.reshape(local_rows, groups, 3, HD)
    queries = projected[:, :, 0]
    key_rows = projected[:, :, 1]
    value_rows = projected[:, :, 2]
    last_rows = jnp.stack([key_rows[-BLK:], value_rows[-BLK:]]).reshape(2, BLK, groups * HD)
    before = from_behind(last_rows, "mem", 1).reshape(2, BLK, groups, HD)
    near_keys = jnp.concatenate([before[0], key_rows], axis=0)
    near_values = jnp.concatenate([before[1], value_rows], axis=0)
    near_scores = (
        jnp.einsum("qgd,kgd->gqk", queries, near_keys, preferred_element_type=jnp.float32)
        * score_scale
    )
    query_index = lax.broadcasted_iota(jnp.int32, (local_rows, local_rows + BLK), 0)
    key_index = lax.broadcasted_iota(jnp.int32, (local_rows, local_rows + BLK), 1)
    first_key = lax.axis_index("mem") * local_rows - BLK
    allowed = (
        (key_index > query_index) & (key_index <= query_index + BLK) & (key_index + first_key >= 0)
    )
    near_probs = softmax_rows(near_scores, allowed[None])
    near_out = jnp.einsum(
        "gqk,kgd->qgd", near_probs, near_values, preferred_element_type=jnp.float32
    )
    blocks_here = retrieved.shape[0]
    entries = blocks_here * TOPB
    local_blocks = memory.shape[1] // BLK
    flat_blocks = retrieved.reshape(entries)
    home_slot = jnp.take(block_home, flat_blocks)
    holder = home_slot // local_blocks
    local_block = home_slot % local_blocks
    local_store = memory.reshape(2, local_blocks, BLK, groups * HD)
    entry_order = jnp.arange(entries)
    earlier = entry_order[None, :] < entry_order[:, None]
    same_owner = holder[:, None] == holder[None, :]
    same_block = home_slot[:, None] == home_slot[None, :]
    first = jnp.sum(same_block & earlier, axis=1) == 0
    first_entry = jnp.argmax(same_block, axis=1)
    before_first = entry_order[None, :] < first_entry[:, None]
    slot_of = jnp.sum(same_owner & before_first & first[None, :], axis=1)
    wanted_ids = (
        jnp.zeros((holder_count, CAP), jnp.int32).at[holder, slot_of].set(local_block)
    )
    picked = jnp.take(
        local_store,
        lax.all_to_all(wanted_ids, "mem", split_axis=0, concat_axis=0, tiled=True).reshape(
            holder_count * CAP
        ),
        axis=1,
        mode="clip",
    ).transpose(1, 0, 2, 3)
    fetched = lax.all_to_all(picked, "mem", split_axis=0, concat_axis=0, tiled=True)
    pool = holder_count * CAP
    row_of = entry_order // TOPB
    member = (
        jnp.zeros((blocks_here, pool), jnp.bool_).at[row_of, holder * CAP + slot_of].set(True)
    )
    bias = jnp.where(jnp.repeat(member, BLK, axis=1), 0.0, NEG_FILL).reshape(
        blocks_here, 1, pool * BLK
    )
    far_out = far_attention(projected_flat, fetched, bias).reshape(local_rows, groups, HD)
    mixing = jax.nn.sigmoid(gate_logit)[None, :, None]
    attended = (
        (mixing * far_out + (1.0 - mixing) * near_out)
        .astype(jnp.bfloat16)
        .reshape(local_rows, groups * HD)
    )
    partial = jnp.dot(attended, output_weight, preferred_element_type=jnp.float32)
    return reduce_over_tp(partial).astype(jnp.bfloat16)


def reduce_over_tp(partial):
    count = lax.axis_size("tp")
    chips = count // 2
    share = partial.shape[0] // count
    me = lax.axis_index("tp")
    core = me % 2
    chip = me // 2
    split = partial.reshape(chips, 2, share, partial.shape[1])
    mine = lax.dynamic_index_in_dim(split, core, axis=1, keepdims=False)
    other = lax.dynamic_index_in_dim(split, 1 - core, axis=1, keepdims=False)
    arrived = lax.ppermute(
        other.astype(jnp.bfloat16), "tp", [(t, t ^ 1) for t in range(count)]
    )
    chip_sum = mine + arrived.astype(jnp.float32)
    total = lax.dynamic_index_in_dim(chip_sum, chip, axis=0, keepdims=False)
    for shift in range(1, chips):
        outgoing = lax.dynamic_index_in_dim(chip_sum, (chip + shift) % chips, axis=0, keepdims=False)
        pairs = [(t, ((t // 2 + shift) % chips) * 2 + t % 2) for t in range(count)]
        total = total + lax.ppermute(outgoing.astype(jnp.bfloat16), "tp", pairs).astype(jnp.float32)
    return total

def solution(mesh):
    placed = (
        P(("mem", "tp"), None),
        P(None, "tp"),
        P("tp", None),
        P("tp"),
        P(None, "mem", "tp"),
        P("mem", None),
        P(),
    )
    return jax.shard_map(
        local, mesh=mesh, in_specs=placed, out_specs=P(("mem", "tp"), None), check_vma=False
    )
```

```python
import jax
import jax.numpy as jnp
from jax import lax
from jax.sharding import PartitionSpec as P
from jax.experimental import pallas as pl
from jax.experimental.pallas import tpu as pltpu

HD = 128
BLK = 128
TOPB = 16
CAP = 2


NEG_FILL = -1e30


def from_behind(value, axis, steps):
    count = lax.axis_size(axis)
    initial, last = (max(0, -steps), min(count, count - steps))
    return lax.ppermute(value, axis, [(source, source + steps) for source in range(initial, last)])


def softmax_rows(scores, allowed):
    row_peak = jnp.max(jnp.where(allowed, scores, NEG_FILL), axis=-1, keepdims=True)
    weights = jnp.where(allowed, jnp.exp(scores - row_peak), 0.0)
    return (weights / jnp.sum(weights, axis=-1, keepdims=True)).astype(jnp.bfloat16)


def near_part(block_queries, window_keys, window_values, first_key):
    scores = (
        jnp.einsum(
            "nqgd,nkgd->ngqk", block_queries, window_keys, preferred_element_type=jnp.float32
        )
        * (HD ** (-0.5))
    )
    query_index = lax.broadcasted_iota(jnp.int32, (BLK, 2 * BLK), 0)
    key_index = lax.broadcasted_iota(jnp.int32, (BLK, 2 * BLK), 1)
    allowed = (
        (key_index > query_index)[None]
        & (key_index <= query_index + BLK)[None]
        & (key_index[None] + first_key[:, None, None] >= 0)
    )
    probs = softmax_rows(scores, allowed[:, None])
    return jnp.einsum(
        "ngqk,nkgd->nqgd", probs, window_values, preferred_element_type=jnp.float32
    )


def far_kernel(q_ref, k_ref, v_ref, bias_ref, o_ref):
    pool = k_ref.shape[0]
    keys = k_ref[:, 0].reshape(pool * BLK, HD)
    values = v_ref[:, 0].reshape(pool * BLK, HD)
    scores = lax.dot_general(
        q_ref[...], keys, (((1,), (1,)), ((), ())), preferred_element_type=jnp.float32
    ) * (HD ** (-0.5)) + bias_ref[0]
    peak = jnp.max(scores, axis=-1, keepdims=True)
    weights = jnp.exp(scores - peak)
    scale = 1.0 / jnp.sum(weights, axis=-1, keepdims=True)
    probs = (weights * scale).astype(jnp.bfloat16)
    o_ref[...] = jnp.dot(probs, values, preferred_element_type=jnp.float32)


def far_attention(projected, fetched, bias):
    rows = projected.shape[0]
    blocks = rows // BLK
    pool = fetched.shape[0]
    groups = fetched.shape[3] // HD
    steps = groups * blocks
    return pl.pallas_call(
        far_kernel,
        grid=(groups, blocks),
        in_specs=[
            pl.BlockSpec((BLK, HD), lambda h, b: (b, h * 3)),
            pl.BlockSpec((pool, 1, BLK, HD), lambda h, b: (0, 0, 0, h)),
            pl.BlockSpec((pool, 1, BLK, HD), lambda h, b: (0, 1, 0, h)),
            pl.BlockSpec((1, 1, pool * BLK), lambda h, b: (b, 0, 0)),
        ],
        out_specs=pl.BlockSpec((BLK, HD), lambda h, b: (b, h)),
        out_shape=jax.ShapeDtypeStruct((rows, groups * HD), jnp.float32),
        cost_estimate=pl.CostEstimate(
            flops=steps * 4 * BLK * pool * BLK * HD,
            transcendentals=steps * BLK * pool * BLK,
            bytes_accessed=fetched.size * 2 + rows * groups * HD * 6,
        ),
    )(projected, fetched, fetched, bias)


def gather_tp(part):
    count = lax.axis_size("tp")
    me = lax.axis_index("tp")
    arrived = [part] + [
        lax.ppermute(part, "tp", [(t, (t + shift) % count) for t in range(count)])
        for shift in range(1, count)
    ]
    order = (me - jnp.arange(count)) % count
    return jnp.take(jnp.stack(arrived), order, axis=0, mode="clip").reshape(
        count * part.shape[0], part.shape[1]
    )

def local(tokens, input_weight, output_weight, gate_logit, memory, retrieved, block_home):
    holder_count = lax.axis_size("mem")
    share_rows = tokens.shape[0]
    local_rows = share_rows * lax.axis_size("tp")
    groups = output_weight.shape[0] // HD
    score_scale = HD ** (-0.5)
    projected = jnp.dot(
        gather_tp(tokens),
        input_weight,
        preferred_element_type=jnp.float32,
    )
    projected_flat = projected.astype(jnp.bfloat16)
    projected = projected_flat.reshape(local_rows, groups, 3, HD)
    queries = projected[:, :, 0]
    key_rows = projected[:, :, 1]
    value_rows = projected[:, :, 2]
    last_rows = jnp.stack([key_rows[-BLK:], value_rows[-BLK:]]).reshape(2, BLK, groups * HD)
    before = from_behind(last_rows, "mem", 1).reshape(2, BLK, groups, HD)
    blocks_here = local_rows // BLK
    query_blocks = queries.reshape(blocks_here, BLK, groups, HD)
    key_blocks = key_rows.reshape(blocks_here, BLK, groups, HD)
    value_blocks = value_rows.reshape(blocks_here, BLK, groups, HD)
    first_row = lax.axis_index("mem") * local_rows + jnp.arange(blocks_here) * BLK
    later = near_part(
        query_blocks[1:],
        jnp.concatenate([key_blocks[:-1], key_blocks[1:]], axis=1),
        jnp.concatenate([value_blocks[:-1], value_blocks[1:]], axis=1),
        first_row[1:] - BLK,
    )
    opening = near_part(
        query_blocks[:1],
        jnp.concatenate([before[0][None], key_blocks[:1]], axis=1),
        jnp.concatenate([before[1][None], value_blocks[:1]], axis=1),
        first_row[:1] - BLK,
    )
    near_out = jnp.concatenate([opening, later], axis=0).reshape(local_rows, groups, HD)
    blocks_here = retrieved.shape[0]
    entries = blocks_here * TOPB
    local_blocks = memory.shape[1] // BLK
    flat_blocks = retrieved.reshape(entries)
    home_slot = jnp.take(block_home, flat_blocks)
    holder = home_slot // local_blocks
    local_block = home_slot % local_blocks
    local_store = memory.reshape(2, local_blocks, BLK, groups * HD)
    entry_order = jnp.arange(entries)
    earlier = entry_order[None, :] < entry_order[:, None]
    same_owner = holder[:, None] == holder[None, :]
    same_block = home_slot[:, None] == home_slot[None, :]
    first = jnp.sum(same_block & earlier, axis=1) == 0
    first_entry = jnp.argmax(same_block, axis=1)
    before_first = entry_order[None, :] < first_entry[:, None]
    slot_of = jnp.sum(same_owner & before_first & first[None, :], axis=1)
    wanted_ids = (
        jnp.zeros((holder_count, CAP), jnp.int32).at[holder, slot_of].set(local_block)
    )
    picked = jnp.take(
        local_store,
        lax.all_to_all(wanted_ids, "mem", split_axis=0, concat_axis=0, tiled=True).reshape(
            holder_count * CAP
        ),
        axis=1,
        mode="clip",
    ).transpose(1, 0, 2, 3)
    fetched = lax.all_to_all(picked, "mem", split_axis=0, concat_axis=0, tiled=True)
    pool = holder_count * CAP
    row_of = entry_order // TOPB
    member = (
        jnp.zeros((blocks_here, pool), jnp.bool_).at[row_of, holder * CAP + slot_of].set(True)
    )
    bias = jnp.where(jnp.repeat(member, BLK, axis=1), 0.0, NEG_FILL).reshape(
        blocks_here, 1, pool * BLK
    )
    far_out = far_attention(projected_flat, fetched, bias).reshape(local_rows, groups, HD)
    mixing = jax.nn.sigmoid(gate_logit)[None, :, None]
    attended = (
        (mixing * far_out + (1.0 - mixing) * near_out)
        .astype(jnp.bfloat16)
        .reshape(local_rows, groups * HD)
    )
    partial = jnp.dot(attended, output_weight, preferred_element_type=jnp.float32)
    return reduce_over_tp(partial).astype(jnp.bfloat16)


def reduce_over_tp(partial):
    count = lax.axis_size("tp")
    chips = count // 2
    share = partial.shape[0] // count
    me = lax.axis_index("tp")
    core = me % 2
    chip = me // 2
    split = partial.reshape(chips, 2, share, partial.shape[1])
    mine = lax.dynamic_index_in_dim(split, core, axis=1, keepdims=False)
    other = lax.dynamic_index_in_dim(split, 1 - core, axis=1, keepdims=False)
    arrived = lax.ppermute(
        other.astype(jnp.bfloat16), "tp", [(t, t ^ 1) for t in range(count)]
    )
    chip_sum = mine + arrived.astype(jnp.float32)
    total = lax.dynamic_index_in_dim(chip_sum, chip, axis=0, keepdims=False)
    for shift in range(1, chips):
        outgoing = lax.dynamic_index_in_dim(chip_sum, (chip + shift) % chips, axis=0, keepdims=False)
        pairs = [(t, ((t // 2 + shift) % chips) * 2 + t % 2) for t in range(count)]
        total = total + lax.ppermute(outgoing.astype(jnp.bfloat16), "tp", pairs).astype(jnp.float32)
    return total

def solution(mesh):
    placed = (
        P(("mem", "tp"), None),
        P(None, "tp"),
        P("tp", None),
        P("tp"),
        P(None, "mem", "tp"),
        P("mem", None),
        P(),
    )
    return jax.shard_map(
        local, mesh=mesh, in_specs=placed, out_specs=P(("mem", "tp"), None), check_vma=False
    )
```

```python
import jax
import jax.numpy as jnp
from jax import lax
from jax.sharding import PartitionSpec as P
from jax.experimental import pallas as pl
from jax.experimental.pallas import tpu as pltpu

HD = 128
BLK = 128
TOPB = 16
CAP = 2


NEG_FILL = -1e30


def from_behind(value, axis, steps):
    count = lax.axis_size(axis)
    initial, last = (max(0, -steps), min(count, count - steps))
    return lax.ppermute(value, axis, [(source, source + steps) for source in range(initial, last)])


def softmax_rows(scores, allowed):
    row_peak = jnp.max(jnp.where(allowed, scores, NEG_FILL), axis=-1, keepdims=True)
    weights = jnp.where(allowed, jnp.exp(scores - row_peak), 0.0)
    return (weights / jnp.sum(weights, axis=-1, keepdims=True)).astype(jnp.bfloat16)


def near_part(block_queries, window_keys, window_values, first_key):
    scores = (
        jnp.einsum(
            "nqgd,nkgd->ngqk", block_queries, window_keys, preferred_element_type=jnp.float32
        )
        * (HD ** (-0.5))
    )
    query_index = lax.broadcasted_iota(jnp.int32, (BLK, 2 * BLK), 0)
    key_index = lax.broadcasted_iota(jnp.int32, (BLK, 2 * BLK), 1)
    allowed = (
        (key_index > query_index)[None]
        & (key_index <= query_index + BLK)[None]
        & (key_index[None] + first_key[:, None, None] >= 0)
    )
    probs = softmax_rows(scores, allowed[:, None])
    return jnp.einsum(
        "ngqk,nkgd->nqgd", probs, window_values, preferred_element_type=jnp.float32
    )


def far_kernel(q_ref, k_ref, v_ref, bias_ref, o_ref):
    pool = k_ref.shape[0]
    keys = k_ref[:, 0].reshape(pool * BLK, HD)
    values = v_ref[:, 0].reshape(pool * BLK, HD)
    scores = lax.dot_general(
        q_ref[...], keys, (((1,), (1,)), ((), ())), preferred_element_type=jnp.float32
    ) * (HD ** (-0.5)) + bias_ref[0]
    peak = jnp.max(scores, axis=-1, keepdims=True)
    weights = jnp.exp(scores - peak)
    scale = 1.0 / jnp.sum(weights, axis=-1, keepdims=True)
    probs = (weights * scale).astype(jnp.bfloat16)
    o_ref[...] = jnp.dot(probs, values, preferred_element_type=jnp.float32)


def far_attention(projected, fetched, bias):
    rows = projected.shape[0]
    blocks = rows // BLK
    pool = fetched.shape[0]
    groups = fetched.shape[3] // HD
    steps = groups * blocks
    return pl.pallas_call(
        far_kernel,
        grid=(groups, blocks),
        in_specs=[
            pl.BlockSpec((BLK, HD), lambda h, b: (b, h * 3)),
            pl.BlockSpec((pool, 1, BLK, HD), lambda h, b: (0, 0, 0, h)),
            pl.BlockSpec((pool, 1, BLK, HD), lambda h, b: (0, 1, 0, h)),
            pl.BlockSpec((1, 1, pool * BLK), lambda h, b: (b, 0, 0)),
        ],
        out_specs=pl.BlockSpec((BLK, HD), lambda h, b: (b, h)),
        out_shape=jax.ShapeDtypeStruct((rows, groups * HD), jnp.float32),
        cost_estimate=pl.CostEstimate(
            flops=steps * 4 * BLK * pool * BLK * HD,
            transcendentals=steps * BLK * pool * BLK,
            bytes_accessed=fetched.size * 2 + rows * groups * HD * 6,
        ),
    )(projected, fetched, fetched, bias)


def gather_tp(part):
    count = lax.axis_size("tp")
    me = lax.axis_index("tp")
    arrived = [part] + [
        lax.ppermute(part, "tp", [(t, (t + shift) % count) for t in range(count)])
        for shift in range(1, count)
    ]
    order = (me - jnp.arange(count)) % count
    return jnp.take(jnp.stack(arrived), order, axis=0, mode="clip").reshape(
        count * part.shape[0], part.shape[1]
    )

def local(tokens, input_weight, output_weight, gate_logit, memory, retrieved, block_home):
    holder_count = lax.axis_size("mem")
    share_rows = tokens.shape[0]
    local_rows = share_rows * lax.axis_size("tp")
    groups = output_weight.shape[0] // HD
    score_scale = HD ** (-0.5)
    projected = jnp.dot(
        gather_tp(tokens),
        input_weight,
        preferred_element_type=jnp.float32,
    )
    projected_flat = projected.astype(jnp.bfloat16)
    projected = projected_flat.reshape(local_rows, groups, 3, HD)
    queries = projected[:, :, 0]
    key_rows = projected[:, :, 1]
    value_rows = projected[:, :, 2]
    last_rows = jnp.stack([key_rows[-BLK:], value_rows[-BLK:]]).reshape(2, BLK, groups * HD)
    before = from_behind(last_rows, "mem", 1).reshape(2, BLK, groups, HD)
    blocks_here = local_rows // BLK
    query_blocks = queries.reshape(blocks_here, BLK, groups, HD)
    key_blocks = key_rows.reshape(blocks_here, BLK, groups, HD)
    value_blocks = value_rows.reshape(blocks_here, BLK, groups, HD)
    first_row = lax.axis_index("mem") * local_rows + jnp.arange(blocks_here) * BLK
    later = near_part(
        query_blocks[1:],
        jnp.concatenate([key_blocks[:-1], key_blocks[1:]], axis=1),
        jnp.concatenate([value_blocks[:-1], value_blocks[1:]], axis=1),
        first_row[1:] - BLK,
    )
    opening = near_part(
        query_blocks[:1],
        jnp.concatenate([before[0][None], key_blocks[:1]], axis=1),
        jnp.concatenate([before[1][None], value_blocks[:1]], axis=1),
        first_row[:1] - BLK,
    )
    near_out = jnp.concatenate([opening, later], axis=0).reshape(local_rows, groups, HD)
    blocks_here = retrieved.shape[0]
    entries = blocks_here * TOPB
    local_blocks = memory.shape[1] // BLK
    flat_blocks = retrieved.reshape(entries)
    home_slot = jnp.take(block_home, flat_blocks)
    holder = home_slot // local_blocks
    local_block = home_slot % local_blocks
    local_store = memory.reshape(2, local_blocks, BLK, groups * HD)
    entry_order = jnp.arange(entries)
    earlier = entry_order[None, :] < entry_order[:, None]
    same_owner = holder[:, None] == holder[None, :]
    same_block = home_slot[:, None] == home_slot[None, :]
    first = jnp.sum(same_block & earlier, axis=1) == 0
    first_entry = jnp.argmax(same_block, axis=1)
    before_first = entry_order[None, :] < first_entry[:, None]
    slot_of = jnp.sum(same_owner & before_first & first[None, :], axis=1)
    wanted_ids = (
        jnp.zeros((holder_count, CAP), jnp.int32).at[holder, slot_of].set(local_block)
    )
    picked = jnp.take(
        local_store,
        lax.all_to_all(wanted_ids, "mem", split_axis=0, concat_axis=0, tiled=True).reshape(
            holder_count * CAP
        ),
        axis=1,
        mode="clip",
    ).transpose(1, 0, 2, 3)
    fetched = lax.all_to_all(picked, "mem", split_axis=0, concat_axis=0, tiled=True)
    pool = holder_count * CAP
    row_of = entry_order // TOPB
    member = (
        jnp.zeros((blocks_here, pool), jnp.bool_).at[row_of, holder * CAP + slot_of].set(True)
    )
    bias = jnp.where(jnp.repeat(member, BLK, axis=1), 0.0, NEG_FILL).reshape(
        blocks_here, 1, pool * BLK
    )
    far_out = far_attention(projected_flat, fetched, bias).reshape(local_rows, groups, HD)
    mixing = jax.nn.sigmoid(gate_logit)[None, :, None]
    attended = (
        (mixing * far_out + (1.0 - mixing) * near_out)
        .astype(jnp.bfloat16)
        .reshape(local_rows, groups * HD)
    )
    count = lax.axis_size("tp")
    share = local_rows // count
    all_weights = gather_tp(output_weight).reshape(count, groups * HD, output_weight.shape[1])
    owned = exchange_tp(attended.reshape(count, share, groups * HD))
    mixed = jnp.einsum("jrc,jcd->rd", owned, all_weights, preferred_element_type=jnp.float32)
    return mixed.astype(jnp.bfloat16)


def exchange_tp(pieces):
    count = lax.axis_size("tp")
    me = lax.axis_index("tp")
    arrived = [lax.dynamic_index_in_dim(pieces, me, 0, keepdims=False)]
    for shift in range(1, count):
        outgoing = lax.dynamic_index_in_dim(pieces, (me + shift) % count, 0, keepdims=False)
        arrived.append(
            lax.ppermute(outgoing, "tp", [(t, (t + shift) % count) for t in range(count)])
        )
    order = (me - jnp.arange(count)) % count
    return jnp.take(jnp.stack(arrived), order, axis=0, mode="clip")

def solution(mesh):
    placed = (
        P(("mem", "tp"), None),
        P(None, "tp"),
        P("tp", None),
        P("tp"),
        P(None, "mem", "tp"),
        P("mem", None),
        P(),
    )
    return jax.shard_map(
        local, mesh=mesh, in_specs=placed, out_specs=P(("mem", "tp"), None), check_vma=False
    )
```

```python
import jax
import jax.numpy as jnp
from jax import lax
from jax.sharding import PartitionSpec as P
from jax.experimental import pallas as pl
from jax.experimental.pallas import tpu as pltpu

HD = 128
BLK = 128
TOPB = 16
CAP = 2


NEG_FILL = -1e30


def from_behind(value, axis, steps):
    count = lax.axis_size(axis)
    initial, last = (max(0, -steps), min(count, count - steps))
    return lax.ppermute(value, axis, [(source, source + steps) for source in range(initial, last)])


def softmax_rows(scores, allowed):
    row_peak = jnp.max(jnp.where(allowed, scores, NEG_FILL), axis=-1, keepdims=True)
    weights = jnp.where(allowed, jnp.exp(scores - row_peak), 0.0)
    return (weights / jnp.sum(weights, axis=-1, keepdims=True)).astype(jnp.bfloat16)


def near_part(block_queries, window_keys, window_values, first_key):
    scores = (
        jnp.einsum(
            "nqgd,nkgd->ngqk", block_queries, window_keys, preferred_element_type=jnp.float32
        )
        * (HD ** (-0.5))
    )
    query_index = lax.broadcasted_iota(jnp.int32, (BLK, 2 * BLK), 0)
    key_index = lax.broadcasted_iota(jnp.int32, (BLK, 2 * BLK), 1)
    allowed = (
        (key_index > query_index)[None]
        & (key_index <= query_index + BLK)[None]
        & (key_index[None] + first_key[:, None, None] >= 0)
    )
    probs = softmax_rows(scores, allowed[:, None])
    return jnp.einsum(
        "ngqk,nkgd->nqgd", probs, window_values, preferred_element_type=jnp.float32
    )


def far_kernel(*refs):
    q_ref, bias_ref, o_ref = refs[0], refs[-2], refs[-1]
    pieces = (len(refs) - 3) // 2
    span = refs[1].shape[0] * BLK
    query = q_ref[...]
    scores = []
    for piece in range(pieces):
        keys = refs[1 + piece][:, 0].reshape(span, HD)
        scores.append(
            lax.dot_general(
                query, keys, (((1,), (1,)), ((), ())), preferred_element_type=jnp.float32
            )
            * (HD ** (-0.5))
            + bias_ref[0, :, piece * span:(piece + 1) * span]
        )
    peak = scores[0].max(axis=-1, keepdims=True)
    for piece in range(1, pieces):
        peak = jnp.maximum(peak, scores[piece].max(axis=-1, keepdims=True))
    weights = [jnp.exp(part - peak) for part in scores]
    total = weights[0].sum(axis=-1, keepdims=True)
    for piece in range(1, pieces):
        total = total + weights[piece].sum(axis=-1, keepdims=True)
    scale = 1.0 / total
    out = None
    for piece in range(pieces):
        values = refs[1 + pieces + piece][:, 0].reshape(span, HD)
        term = jnp.dot(
            (weights[piece] * scale).astype(jnp.bfloat16), values, preferred_element_type=jnp.float32
        )
        out = term if out is None else out + term
    o_ref[...] = out


def far_attention(projected, pieces, bias):
    rows = projected.shape[0]
    blocks = rows // BLK
    slots = pieces[0].shape[0]
    groups = pieces[0].shape[3] // HD
    steps = groups * blocks
    pool = slots * len(pieces)
    kv_spec = [pl.BlockSpec((slots, 1, BLK, HD), lambda h, b, c=c: (0, c, 0, h)) for c in (0, 1)]
    return pl.pallas_call(
        far_kernel,
        grid=(groups, blocks),
        in_specs=[pl.BlockSpec((BLK, HD), lambda h, b: (b, h * 3))]
        + [kv_spec[0]] * len(pieces)
        + [kv_spec[1]] * len(pieces)
        + [pl.BlockSpec((1, 1, pool * BLK), lambda h, b: (b, 0, 0))],
        out_specs=pl.BlockSpec((BLK, HD), lambda h, b: (b, h)),
        out_shape=jax.ShapeDtypeStruct((rows, groups * HD), jnp.float32),
        cost_estimate=pl.CostEstimate(
            flops=steps * 4 * BLK * pool * BLK * HD,
            transcendentals=steps * BLK * pool * BLK,
            bytes_accessed=sum(p.size for p in pieces) * 2 + rows * groups * HD * 6,
        ),
    )(projected, *pieces, *pieces, bias)


def exchange_mem(pieces):
    count = lax.axis_size("mem")
    me = lax.axis_index("mem")
    arrived = [pieces(me)]
    for shift in range(1, count):
        arrived.append(
            lax.ppermute(
                pieces((me + shift) % count), "mem", [(t, (t + shift) % count) for t in range(count)]
            )
        )
    return arrived

def gather_tp(part):
    count = lax.axis_size("tp")
    me = lax.axis_index("tp")
    arrived = [part] + [
        lax.ppermute(part, "tp", [(t, (t + shift) % count) for t in range(count)])
        for shift in range(1, count)
    ]
    order = (me - jnp.arange(count)) % count
    return jnp.take(jnp.stack(arrived), order, axis=0, mode="clip").reshape(
        count * part.shape[0], part.shape[1]
    )

def local(tokens, input_weight, output_weight, gate_logit, memory, retrieved, block_home):
    holder_count = lax.axis_size("mem")
    share_rows = tokens.shape[0]
    local_rows = share_rows * lax.axis_size("tp")
    groups = output_weight.shape[0] // HD
    score_scale = HD ** (-0.5)
    projected = jnp.dot(
        gather_tp(tokens),
        input_weight,
        preferred_element_type=jnp.float32,
    )
    projected_flat = projected.astype(jnp.bfloat16)
    projected = projected_flat.reshape(local_rows, groups, 3, HD)
    queries = projected[:, :, 0]
    key_rows = projected[:, :, 1]
    value_rows = projected[:, :, 2]
    last_rows = jnp.stack([key_rows[-BLK:], value_rows[-BLK:]]).reshape(2, BLK, groups * HD)
    before = from_behind(last_rows, "mem", 1).reshape(2, BLK, groups, HD)
    blocks_here = local_rows // BLK
    query_blocks = queries.reshape(blocks_here, BLK, groups, HD)
    key_blocks = key_rows.reshape(blocks_here, BLK, groups, HD)
    value_blocks = value_rows.reshape(blocks_here, BLK, groups, HD)
    first_row = lax.axis_index("mem") * local_rows + jnp.arange(blocks_here) * BLK
    later = near_part(
        query_blocks[1:],
        jnp.concatenate([key_blocks[:-1], key_blocks[1:]], axis=1),
        jnp.concatenate([value_blocks[:-1], value_blocks[1:]], axis=1),
        first_row[1:] - BLK,
    )
    opening = near_part(
        query_blocks[:1],
        jnp.concatenate([before[0][None], key_blocks[:1]], axis=1),
        jnp.concatenate([before[1][None], value_blocks[:1]], axis=1),
        first_row[:1] - BLK,
    )
    near_out = jnp.concatenate([opening, later], axis=0).reshape(local_rows, groups, HD)
    blocks_here = retrieved.shape[0]
    entries = blocks_here * TOPB
    local_blocks = memory.shape[1] // BLK
    flat_blocks = retrieved.reshape(entries)
    home_slot = jnp.take(block_home, flat_blocks)
    holder = home_slot // local_blocks
    local_block = home_slot % local_blocks
    local_store = memory.reshape(2, local_blocks, BLK, groups * HD)
    entry_order = jnp.arange(entries)
    earlier = entry_order[None, :] < entry_order[:, None]
    same_owner = holder[:, None] == holder[None, :]
    same_block = home_slot[:, None] == home_slot[None, :]
    first = jnp.sum(same_block & earlier, axis=1) == 0
    first_entry = jnp.argmax(same_block, axis=1)
    before_first = entry_order[None, :] < first_entry[:, None]
    slot_of = jnp.sum(same_owner & before_first & first[None, :], axis=1)
    pool = holder_count * CAP
    slot_index = lax.broadcasted_iota(jnp.int32, (holder_count, CAP, entries), 1)
    holder_index = lax.broadcasted_iota(jnp.int32, (holder_count, CAP, entries), 0)
    wanted_ids = jnp.max(
        jnp.where(
            (holder_index == holder[None, None, :]) & (slot_index == slot_of[None, None, :]),
            local_block[None, None, :],
            0,
        ),
        axis=2,
    )
    asked = exchange_mem(lambda target: lax.dynamic_index_in_dim(wanted_ids, target, 0, keepdims=False))
    me_mem = lax.axis_index("mem")
    pieces = exchange_mem(
        lambda target: jnp.take(
            local_store,
            lax.dynamic_index_in_dim(jnp.stack(asked), (me_mem - target) % holder_count, 0, keepdims=False),
            axis=1,
            mode="clip",
        ).transpose(1, 0, 2, 3)
    )
    row_of = entry_order // TOPB
    arrival = (me_mem - holder) % holder_count
    pool_slot = arrival * CAP + slot_of
    pool_index = lax.broadcasted_iota(jnp.int32, (blocks_here, pool, entries), 1)
    row_index = lax.broadcasted_iota(jnp.int32, (blocks_here, pool, entries), 0)
    member = jnp.any(
        (pool_index == pool_slot[None, None, :]) & (row_index == row_of[None, None, :]), axis=2
    )
    bias = jnp.where(jnp.repeat(member, BLK, axis=1), 0.0, NEG_FILL).reshape(
        blocks_here, 1, pool * BLK
    )
    far_out = far_attention(projected_flat, pieces, bias).reshape(local_rows, groups, HD)
    mixing = jax.nn.sigmoid(gate_logit)[None, :, None]
    attended = (
        (mixing * far_out + (1.0 - mixing) * near_out)
        .astype(jnp.bfloat16)
        .reshape(local_rows, groups * HD)
    )
    partial = jnp.dot(attended, output_weight, preferred_element_type=jnp.float32)
    return reduce_over_tp(partial).astype(jnp.bfloat16)


def reduce_over_tp(partial):
    count = lax.axis_size("tp")
    chips = count // 2
    share = partial.shape[0] // count
    me = lax.axis_index("tp")
    core = me % 2
    chip = me // 2
    split = partial.reshape(chips, 2, share, partial.shape[1])
    mine = lax.dynamic_index_in_dim(split, core, axis=1, keepdims=False)
    other = lax.dynamic_index_in_dim(split, 1 - core, axis=1, keepdims=False)
    arrived = lax.ppermute(
        other.astype(jnp.bfloat16), "tp", [(t, t ^ 1) for t in range(count)]
    )
    chip_sum = mine + arrived.astype(jnp.float32)
    total = lax.dynamic_index_in_dim(chip_sum, chip, axis=0, keepdims=False)
    for shift in range(1, chips):
        outgoing = lax.dynamic_index_in_dim(chip_sum, (chip + shift) % chips, axis=0, keepdims=False)
        pairs = [(t, ((t // 2 + shift) % chips) * 2 + t % 2) for t in range(count)]
        total = total + lax.ppermute(outgoing.astype(jnp.bfloat16), "tp", pairs).astype(jnp.float32)
    return total

def solution(mesh):
    placed = (
        P(("mem", "tp"), None),
        P(None, "tp"),
        P("tp", None),
        P("tp"),
        P(None, "mem", "tp"),
        P("mem", None),
        P(),
    )
    return jax.shard_map(
        local, mesh=mesh, in_specs=placed, out_specs=P(("mem", "tp"), None), check_vma=False
    )
```

```python
import jax
import jax.numpy as jnp
from jax import lax
from jax.sharding import PartitionSpec as P
from jax.experimental import pallas as pl
from jax.experimental.pallas import tpu as pltpu

HD = 128
BLK = 128
TOPB = 16
CAP = 2


NEG_FILL = -1e30


def from_behind(value, axis, steps):
    count = lax.axis_size(axis)
    initial, last = (max(0, -steps), min(count, count - steps))
    return lax.ppermute(value, axis, [(source, source + steps) for source in range(initial, last)])


def softmax_rows(scores, allowed):
    row_peak = jnp.max(jnp.where(allowed, scores, NEG_FILL), axis=-1, keepdims=True)
    weights = jnp.where(allowed, jnp.exp(scores - row_peak), 0.0)
    return (weights / jnp.sum(weights, axis=-1, keepdims=True)).astype(jnp.bfloat16)


def near_part(block_queries, window_keys, window_values, first_key):
    scores = (
        jnp.einsum(
            "nqgd,nkgd->ngqk", block_queries, window_keys, preferred_element_type=jnp.float32
        )
        * (HD ** (-0.5))
    )
    query_index = lax.broadcasted_iota(jnp.int32, (BLK, 2 * BLK), 0)
    key_index = lax.broadcasted_iota(jnp.int32, (BLK, 2 * BLK), 1)
    allowed = (
        (key_index > query_index)[None]
        & (key_index <= query_index + BLK)[None]
        & (key_index[None] + first_key[:, None, None] >= 0)
    )
    probs = softmax_rows(scores, allowed[:, None])
    return jnp.einsum(
        "ngqk,nkgd->nqgd", probs, window_values, preferred_element_type=jnp.float32
    )


def far_kernel(q_ref, k_ref, v_ref, bias_ref, o_ref):
    pool = k_ref.shape[0]
    keys = k_ref[:, 0].reshape(pool * BLK, HD)
    values = v_ref[:, 0].reshape(pool * BLK, HD)
    scores = lax.dot_general(
        q_ref[...], keys, (((1,), (1,)), ((), ())), preferred_element_type=jnp.float32
    ) + bias_ref[0]
    peak = jnp.max(scores, axis=-1, keepdims=True)
    weights = jnp.exp((scores - peak) * (HD ** (-0.5)))
    scale = 1.0 / jnp.sum(weights, axis=-1, keepdims=True)
    out = jnp.dot(weights.astype(jnp.bfloat16), values, preferred_element_type=jnp.float32)
    o_ref[...] = out * scale


def far_attention(projected, fetched, bias):
    rows = projected.shape[0]
    blocks = rows // BLK
    pool = fetched.shape[0]
    groups = fetched.shape[3] // HD
    steps = groups * blocks
    return pl.pallas_call(
        far_kernel,
        grid=(groups, blocks),
        in_specs=[
            pl.BlockSpec((BLK, HD), lambda h, b: (b, h * 3)),
            pl.BlockSpec((pool, 1, BLK, HD), lambda h, b: (0, 0, 0, h)),
            pl.BlockSpec((pool, 1, BLK, HD), lambda h, b: (0, 1, 0, h)),
            pl.BlockSpec((1, 1, pool * BLK), lambda h, b: (b, 0, 0)),
        ],
        out_specs=pl.BlockSpec((BLK, HD), lambda h, b: (b, h)),
        out_shape=jax.ShapeDtypeStruct((rows, groups * HD), jnp.float32),
        cost_estimate=pl.CostEstimate(
            flops=steps * 4 * BLK * pool * BLK * HD,
            transcendentals=steps * BLK * pool * BLK,
            bytes_accessed=fetched.size * 2 + rows * groups * HD * 6,
        ),
    )(projected, fetched, fetched, bias)


def gather_tp(part):
    count = lax.axis_size("tp")
    me = lax.axis_index("tp")
    arrived = [part] + [
        lax.ppermute(part, "tp", [(t, (t + shift) % count) for t in range(count)])
        for shift in range(1, count)
    ]
    order = (me - jnp.arange(count)) % count
    return jnp.take(jnp.stack(arrived), order, axis=0, mode="clip").reshape(
        count * part.shape[0], part.shape[1]
    )

def local(tokens, input_weight, output_weight, gate_logit, memory, retrieved, block_home):
    holder_count = lax.axis_size("mem")
    share_rows = tokens.shape[0]
    local_rows = share_rows * lax.axis_size("tp")
    groups = output_weight.shape[0] // HD
    score_scale = HD ** (-0.5)
    projected = jnp.dot(
        gather_tp(tokens),
        input_weight,
        preferred_element_type=jnp.float32,
    )
    projected_flat = projected.astype(jnp.bfloat16)
    projected = projected_flat.reshape(local_rows, groups, 3, HD)
    queries = projected[:, :, 0]
    key_rows = projected[:, :, 1]
    value_rows = projected[:, :, 2]
    last_rows = jnp.stack([key_rows[-BLK:], value_rows[-BLK:]]).reshape(2, BLK, groups * HD)
    before = from_behind(last_rows, "mem", 1).reshape(2, BLK, groups, HD)
    blocks_here = local_rows // BLK
    query_blocks = queries.reshape(blocks_here, BLK, groups, HD)
    key_blocks = key_rows.reshape(blocks_here, BLK, groups, HD)
    value_blocks = value_rows.reshape(blocks_here, BLK, groups, HD)
    first_row = lax.axis_index("mem") * local_rows + jnp.arange(blocks_here) * BLK
    later = near_part(
        query_blocks[1:],
        jnp.concatenate([key_blocks[:-1], key_blocks[1:]], axis=1),
        jnp.concatenate([value_blocks[:-1], value_blocks[1:]], axis=1),
        first_row[1:] - BLK,
    )
    opening = near_part(
        query_blocks[:1],
        jnp.concatenate([before[0][None], key_blocks[:1]], axis=1),
        jnp.concatenate([before[1][None], value_blocks[:1]], axis=1),
        first_row[:1] - BLK,
    )
    near_out = jnp.concatenate([opening, later], axis=0).reshape(local_rows, groups, HD)
    blocks_here = retrieved.shape[0]
    entries = blocks_here * TOPB
    local_blocks = memory.shape[1] // BLK
    flat_blocks = retrieved.reshape(entries)
    block_index = lax.broadcasted_iota(jnp.int32, (entries, block_home.shape[0]), 1)
    home_slot = jnp.sum(
        jnp.where(block_index == flat_blocks[:, None], block_home[None, :], 0), axis=1
    )
    holder = home_slot // local_blocks
    local_block = home_slot % local_blocks
    local_store = memory.reshape(2, local_blocks, BLK, groups * HD)
    entry_order = jnp.arange(entries)
    earlier = entry_order[None, :] < entry_order[:, None]
    same_owner = holder[:, None] == holder[None, :]
    same_block = home_slot[:, None] == home_slot[None, :]
    first = jnp.sum(same_block & earlier, axis=1) == 0
    first_entry = jnp.argmax(same_block, axis=1)
    before_first = entry_order[None, :] < first_entry[:, None]
    slot_of = jnp.sum(same_owner & before_first & first[None, :], axis=1)
    slot_index = lax.broadcasted_iota(jnp.int32, (holder_count, CAP, entries), 1)
    holder_index = lax.broadcasted_iota(jnp.int32, (holder_count, CAP, entries), 0)
    wanted_ids = jnp.max(
        jnp.where(
            (holder_index == holder[None, None, :]) & (slot_index == slot_of[None, None, :]),
            local_block[None, None, :],
            0,
        ),
        axis=2,
    )
    picked = jnp.take(
        local_store,
        lax.all_to_all(wanted_ids, "mem", split_axis=0, concat_axis=0, tiled=True).reshape(
            holder_count * CAP
        ),
        axis=1,
        mode="clip",
    ).transpose(1, 0, 2, 3)
    fetched = lax.all_to_all(picked, "mem", split_axis=0, concat_axis=0, tiled=True)
    pool = holder_count * CAP
    row_of = entry_order // TOPB
    member = (
        jnp.zeros((blocks_here, pool), jnp.bool_).at[row_of, holder * CAP + slot_of].set(True)
    )
    bias = jnp.where(jnp.repeat(member, BLK, axis=1), 0.0, NEG_FILL).reshape(
        blocks_here, 1, pool * BLK
    )
    far_out = far_attention(projected_flat, fetched, bias).reshape(local_rows, groups, HD)
    mixing = jax.nn.sigmoid(gate_logit)[None, :, None]
    attended = (
        (mixing * far_out + (1.0 - mixing) * near_out)
        .astype(jnp.bfloat16)
        .reshape(local_rows, groups * HD)
    )
    partial = jnp.dot(attended, output_weight, preferred_element_type=jnp.float32)
    return reduce_over_tp(partial).astype(jnp.bfloat16)


def reduce_over_tp(partial):
    count = lax.axis_size("tp")
    chips = count // 2
    share = partial.shape[0] // count
    me = lax.axis_index("tp")
    core = me % 2
    chip = me // 2
    split = partial.reshape(chips, 2, share, partial.shape[1])
    mine = lax.dynamic_index_in_dim(split, core, axis=1, keepdims=False)
    other = lax.dynamic_index_in_dim(split, 1 - core, axis=1, keepdims=False)
    arrived = lax.ppermute(
        other.astype(jnp.bfloat16), "tp", [(t, t ^ 1) for t in range(count)]
    )
    chip_sum = mine + arrived.astype(jnp.float32)
    total = lax.dynamic_index_in_dim(chip_sum, chip, axis=0, keepdims=False)
    for shift in range(1, chips):
        outgoing = lax.dynamic_index_in_dim(chip_sum, (chip + shift) % chips, axis=0, keepdims=False)
        pairs = [(t, ((t // 2 + shift) % chips) * 2 + t % 2) for t in range(count)]
        total = total + lax.ppermute(outgoing.astype(jnp.bfloat16), "tp", pairs).astype(jnp.float32)
    return total

def solution(mesh):
    placed = (
        P(("mem", "tp"), None),
        P(None, "tp"),
        P("tp", None),
        P("tp"),
        P(None, "mem", "tp"),
        P("mem", None),
        P(),
    )
    return jax.shard_map(
        local, mesh=mesh, in_specs=placed, out_specs=P(("mem", "tp"), None), check_vma=False
    )
```

```python
import jax
import jax.numpy as jnp
from jax import lax
from jax.sharding import PartitionSpec as P
from jax.experimental import pallas as pl
from jax.experimental.pallas import tpu as pltpu

HD = 128
BLK = 128
TOPB = 16
CAP = 2


NEG_FILL = -1e30


def from_behind(value, axis, steps):
    count = lax.axis_size(axis)
    initial, last = (max(0, -steps), min(count, count - steps))
    return lax.ppermute(value, axis, [(source, source + steps) for source in range(initial, last)])


def softmax_rows(scores, allowed):
    row_peak = jnp.max(jnp.where(allowed, scores, NEG_FILL), axis=-1, keepdims=True)
    weights = jnp.where(allowed, jnp.exp(scores - row_peak), 0.0)
    return (weights / jnp.sum(weights, axis=-1, keepdims=True)).astype(jnp.bfloat16)


def near_part(block_queries, window_keys, window_values, first_key):
    scores = (
        jnp.einsum(
            "nqgd,nkgd->ngqk", block_queries, window_keys, preferred_element_type=jnp.float32
        )
        * (HD ** (-0.5))
    )
    query_index = lax.broadcasted_iota(jnp.int32, (BLK, 2 * BLK), 0)
    key_index = lax.broadcasted_iota(jnp.int32, (BLK, 2 * BLK), 1)
    allowed = (
        (key_index > query_index)[None]
        & (key_index <= query_index + BLK)[None]
        & (key_index[None] + first_key[:, None, None] >= 0)
    )
    probs = softmax_rows(scores, allowed[:, None])
    return jnp.einsum(
        "ngqk,nkgd->nqgd", probs, window_values, preferred_element_type=jnp.float32
    )


def far_kernel(q_ref, k_ref, v_ref, bias_ref, near_ref, mix_ref, o_ref):
    pool = k_ref.shape[0]
    keys = k_ref[:, 0].reshape(pool * BLK, HD)
    values = v_ref[:, 0].reshape(pool * BLK, HD)
    mix = mix_ref[...]
    for block in range(q_ref.shape[0] // BLK):
        rows = slice(block * BLK, (block + 1) * BLK)
        scores = lax.dot_general(
            q_ref[rows, :], keys, (((1,), (1,)), ((), ())), preferred_element_type=jnp.float32
        ) + bias_ref[block]
        peak = jnp.max(scores, axis=-1, keepdims=True)
        weights = jnp.exp((scores - peak) * (HD ** (-0.5)))
        scale = 1.0 / jnp.sum(weights, axis=-1, keepdims=True)
        far = jnp.dot(weights.astype(jnp.bfloat16), values, preferred_element_type=jnp.float32)
        o_ref[rows, :] = (mix * (far * scale) + (1.0 - mix) * near_ref[rows, :]).astype(o_ref.dtype)


def far_attention(projected, fetched, bias, near_out, mixing):
    rows = projected.shape[0]
    blocks = rows // BLK
    pool = fetched.shape[0]
    groups = fetched.shape[3] // HD
    return pl.pallas_call(
        far_kernel,
        grid=(groups,),
        in_specs=[
            pl.BlockSpec((rows, HD), lambda h: (0, h * 3)),
            pl.BlockSpec((pool, 1, BLK, HD), lambda h: (0, 0, 0, h)),
            pl.BlockSpec((pool, 1, BLK, HD), lambda h: (0, 1, 0, h)),
            pl.BlockSpec((blocks, 1, pool * BLK), lambda h: (0, 0, 0)),
            pl.BlockSpec((rows, HD), lambda h: (0, h)),
            pl.BlockSpec((1, HD), lambda h: (0, h)),
        ],
        out_specs=pl.BlockSpec((rows, HD), lambda h: (0, h)),
        out_shape=jax.ShapeDtypeStruct((rows, groups * HD), jnp.bfloat16),
        cost_estimate=pl.CostEstimate(
            flops=groups * blocks * 4 * BLK * pool * BLK * HD,
            transcendentals=groups * blocks * BLK * pool * BLK,
            bytes_accessed=fetched.size * 2 + rows * groups * HD * 8,
        ),
    )(projected, fetched, fetched, bias, near_out, mixing)

def gather_tp(part):
    count = lax.axis_size("tp")
    me = lax.axis_index("tp")
    arrived = [part] + [
        lax.ppermute(part, "tp", [(t, (t + shift) % count) for t in range(count)])
        for shift in range(1, count)
    ]
    order = (me - jnp.arange(count)) % count
    return jnp.take(jnp.stack(arrived), order, axis=0, mode="clip").reshape(
        count * part.shape[0], part.shape[1]
    )

def local(tokens, input_weight, output_weight, gate_logit, memory, retrieved, block_home):
    holder_count = lax.axis_size("mem")
    share_rows = tokens.shape[0]
    local_rows = share_rows * lax.axis_size("tp")
    groups = output_weight.shape[0] // HD
    score_scale = HD ** (-0.5)
    projected = jnp.dot(
        gather_tp(tokens),
        input_weight,
        preferred_element_type=jnp.float32,
    )
    projected_flat = projected.astype(jnp.bfloat16)
    projected = projected_flat.reshape(local_rows, groups, 3, HD)
    queries = projected[:, :, 0]
    key_rows = projected[:, :, 1]
    value_rows = projected[:, :, 2]
    last_rows = jnp.stack([key_rows[-BLK:], value_rows[-BLK:]]).reshape(2, BLK, groups * HD)
    before = from_behind(last_rows, "mem", 1).reshape(2, BLK, groups, HD)
    blocks_here = local_rows // BLK
    query_blocks = queries.reshape(blocks_here, BLK, groups, HD)
    key_blocks = key_rows.reshape(blocks_here, BLK, groups, HD)
    value_blocks = value_rows.reshape(blocks_here, BLK, groups, HD)
    first_row = lax.axis_index("mem") * local_rows + jnp.arange(blocks_here) * BLK
    later = near_part(
        query_blocks[1:],
        jnp.concatenate([key_blocks[:-1], key_blocks[1:]], axis=1),
        jnp.concatenate([value_blocks[:-1], value_blocks[1:]], axis=1),
        first_row[1:] - BLK,
    )
    opening = near_part(
        query_blocks[:1],
        jnp.concatenate([before[0][None], key_blocks[:1]], axis=1),
        jnp.concatenate([before[1][None], value_blocks[:1]], axis=1),
        first_row[:1] - BLK,
    )
    near_out = jnp.concatenate([opening, later], axis=0).reshape(local_rows, groups, HD)
    blocks_here = retrieved.shape[0]
    entries = blocks_here * TOPB
    local_blocks = memory.shape[1] // BLK
    flat_blocks = retrieved.reshape(entries)
    block_index = lax.broadcasted_iota(jnp.int32, (entries, block_home.shape[0]), 1)
    home_slot = jnp.sum(
        jnp.where(block_index == flat_blocks[:, None], block_home[None, :], 0), axis=1
    )
    holder = home_slot // local_blocks
    local_block = home_slot % local_blocks
    local_store = memory.reshape(2, local_blocks, BLK, groups * HD)
    entry_order = jnp.arange(entries)
    earlier = entry_order[None, :] < entry_order[:, None]
    same_owner = holder[:, None] == holder[None, :]
    same_block = home_slot[:, None] == home_slot[None, :]
    first = jnp.sum(same_block & earlier, axis=1) == 0
    first_entry = jnp.argmax(same_block, axis=1)
    before_first = entry_order[None, :] < first_entry[:, None]
    slot_of = jnp.sum(same_owner & before_first & first[None, :], axis=1)
    slot_index = lax.broadcasted_iota(jnp.int32, (holder_count, CAP, entries), 1)
    holder_index = lax.broadcasted_iota(jnp.int32, (holder_count, CAP, entries), 0)
    wanted_ids = jnp.max(
        jnp.where(
            (holder_index == holder[None, None, :]) & (slot_index == slot_of[None, None, :]),
            local_block[None, None, :],
            0,
        ),
        axis=2,
    )
    picked = jnp.take(
        local_store,
        lax.all_to_all(wanted_ids, "mem", split_axis=0, concat_axis=0, tiled=True).reshape(
            holder_count * CAP
        ),
        axis=1,
        mode="clip",
    ).transpose(1, 0, 2, 3)
    fetched = lax.all_to_all(picked, "mem", split_axis=0, concat_axis=0, tiled=True)
    pool = holder_count * CAP
    row_of = entry_order // TOPB
    member = (
        jnp.zeros((blocks_here, pool), jnp.bool_).at[row_of, holder * CAP + slot_of].set(True)
    )
    bias = jnp.where(jnp.repeat(member, BLK, axis=1), 0.0, NEG_FILL).reshape(
        blocks_here, 1, pool * BLK
    )
    mixing = jnp.repeat(jax.nn.sigmoid(gate_logit), HD).reshape(1, groups * HD)
    attended = far_attention(
        projected_flat, fetched, bias, near_out.reshape(local_rows, groups * HD), mixing
    )
    partial = jnp.dot(attended, output_weight, preferred_element_type=jnp.float32)
    return reduce_over_tp(partial).astype(jnp.bfloat16)


def reduce_over_tp(partial):
    count = lax.axis_size("tp")
    chips = count // 2
    share = partial.shape[0] // count
    me = lax.axis_index("tp")
    core = me % 2
    chip = me // 2
    split = partial.reshape(chips, 2, share, partial.shape[1])
    mine = lax.dynamic_index_in_dim(split, core, axis=1, keepdims=False)
    other = lax.dynamic_index_in_dim(split, 1 - core, axis=1, keepdims=False)
    arrived = lax.ppermute(
        other.astype(jnp.bfloat16), "tp", [(t, t ^ 1) for t in range(count)]
    )
    chip_sum = mine + arrived.astype(jnp.float32)
    total = lax.dynamic_index_in_dim(chip_sum, chip, axis=0, keepdims=False)
    for shift in range(1, chips):
        outgoing = lax.dynamic_index_in_dim(chip_sum, (chip + shift) % chips, axis=0, keepdims=False)
        pairs = [(t, ((t // 2 + shift) % chips) * 2 + t % 2) for t in range(count)]
        total = total + lax.ppermute(outgoing.astype(jnp.bfloat16), "tp", pairs).astype(jnp.float32)
    return total

def solution(mesh):
    placed = (
        P(("mem", "tp"), None),
        P(None, "tp"),
        P("tp", None),
        P("tp"),
        P(None, "mem", "tp"),
        P("mem", None),
        P(),
    )
    return jax.shard_map(
        local, mesh=mesh, in_specs=placed, out_specs=P(("mem", "tp"), None), check_vma=False
    )
```

```python
import jax
import jax.numpy as jnp
from jax import lax
from jax.sharding import PartitionSpec as P
from jax.experimental import pallas as pl
from jax.experimental.pallas import tpu as pltpu

HD = 128
BLK = 128
TOPB = 16
CAP = 2


NEG_FILL = -1e30


def from_behind(value, axis, steps):
    count = lax.axis_size(axis)
    initial, last = (max(0, -steps), min(count, count - steps))
    return lax.ppermute(value, axis, [(source, source + steps) for source in range(initial, last)])


def softmax_rows(scores, allowed):
    row_peak = jnp.max(jnp.where(allowed, scores, NEG_FILL), axis=-1, keepdims=True)
    weights = jnp.where(allowed, jnp.exp(scores - row_peak), 0.0)
    return (weights / jnp.sum(weights, axis=-1, keepdims=True)).astype(jnp.bfloat16)


def near_part(block_queries, window_keys, window_values, first_key):
    scores = (
        jnp.einsum(
            "nqgd,nkgd->ngqk", block_queries, window_keys, preferred_element_type=jnp.float32
        )
        * (HD ** (-0.5))
    )
    query_index = lax.broadcasted_iota(jnp.int32, (BLK, 2 * BLK), 0)
    key_index = lax.broadcasted_iota(jnp.int32, (BLK, 2 * BLK), 1)
    allowed = (
        (key_index > query_index)[None]
        & (key_index <= query_index + BLK)[None]
        & (key_index[None] + first_key[:, None, None] >= 0)
    )
    probs = softmax_rows(scores, allowed[:, None])
    return jnp.einsum(
        "ngqk,nkgd->ngqd", probs, window_values, preferred_element_type=jnp.float32
    )


def far_kernel(q_ref, k_ref, v_ref, bias_ref, near_ref, mix_ref, o_ref):
    pool = k_ref.shape[0]
    keys = k_ref[:, 0].reshape(pool * BLK, HD)
    values = v_ref[:, 0].reshape(pool * BLK, HD)
    mix = mix_ref[...]
    for block in range(q_ref.shape[0] // BLK):
        rows = slice(block * BLK, (block + 1) * BLK)
        scores = lax.dot_general(
            q_ref[rows, :], keys, (((1,), (1,)), ((), ())), preferred_element_type=jnp.float32
        ) + bias_ref[block]
        peak = jnp.max(scores, axis=-1, keepdims=True)
        weights = jnp.exp((scores - peak) * (HD ** (-0.5)))
        scale = 1.0 / jnp.sum(weights, axis=-1, keepdims=True)
        far = jnp.dot(weights.astype(jnp.bfloat16), values, preferred_element_type=jnp.float32)
        o_ref[rows, :] = (mix * (far * scale) + (1.0 - mix) * near_ref[block, 0]).astype(o_ref.dtype)


def far_attention(projected, fetched, bias, near_out, mixing):
    rows = projected.shape[0]
    blocks = rows // BLK
    pool = fetched.shape[0]
    groups = fetched.shape[3] // HD
    return pl.pallas_call(
        far_kernel,
        grid=(groups,),
        in_specs=[
            pl.BlockSpec((rows, HD), lambda h: (0, h * 3)),
            pl.BlockSpec((pool, 1, BLK, HD), lambda h: (0, 0, 0, h)),
            pl.BlockSpec((pool, 1, BLK, HD), lambda h: (0, 1, 0, h)),
            pl.BlockSpec((blocks, 1, pool * BLK), lambda h: (0, 0, 0)),
            pl.BlockSpec((blocks, 1, BLK, HD), lambda h: (0, h, 0, 0)),
            pl.BlockSpec((1, HD), lambda h: (0, h)),
        ],
        out_specs=pl.BlockSpec((rows, HD), lambda h: (0, h)),
        out_shape=jax.ShapeDtypeStruct((rows, groups * HD), jnp.bfloat16),
        cost_estimate=pl.CostEstimate(
            flops=groups * blocks * 4 * BLK * pool * BLK * HD,
            transcendentals=groups * blocks * BLK * pool * BLK,
            bytes_accessed=fetched.size * 2 + rows * groups * HD * 8,
        ),
    )(projected, fetched, fetched, bias, near_out, mixing)

def gather_tp(part):
    count = lax.axis_size("tp")
    me = lax.axis_index("tp")
    arrived = [part] + [
        lax.ppermute(part, "tp", [(t, (t + shift) % count) for t in range(count)])
        for shift in range(1, count)
    ]
    order = (me - jnp.arange(count)) % count
    return jnp.take(jnp.stack(arrived), order, axis=0, mode="clip").reshape(
        count * part.shape[0], part.shape[1]
    )

def local(tokens, input_weight, output_weight, gate_logit, memory, retrieved, block_home):
    holder_count = lax.axis_size("mem")
    share_rows = tokens.shape[0]
    local_rows = share_rows * lax.axis_size("tp")
    groups = output_weight.shape[0] // HD
    score_scale = HD ** (-0.5)
    projected = jnp.dot(
        gather_tp(tokens),
        input_weight,
        preferred_element_type=jnp.float32,
    )
    projected_flat = projected.astype(jnp.bfloat16)
    projected = projected_flat.reshape(local_rows, groups, 3, HD)
    queries = projected[:, :, 0]
    key_rows = projected[:, :, 1]
    value_rows = projected[:, :, 2]
    last_rows = jnp.stack([key_rows[-BLK:], value_rows[-BLK:]]).reshape(2, BLK, groups * HD)
    before = from_behind(last_rows, "mem", 1).reshape(2, BLK, groups, HD)
    blocks_here = local_rows // BLK
    query_blocks = queries.reshape(blocks_here, BLK, groups, HD)
    key_blocks = key_rows.reshape(blocks_here, BLK, groups, HD)
    value_blocks = value_rows.reshape(blocks_here, BLK, groups, HD)
    first_row = lax.axis_index("mem") * local_rows + jnp.arange(blocks_here) * BLK
    later = near_part(
        query_blocks[1:],
        jnp.concatenate([key_blocks[:-1], key_blocks[1:]], axis=1),
        jnp.concatenate([value_blocks[:-1], value_blocks[1:]], axis=1),
        first_row[1:] - BLK,
    )
    opening = near_part(
        query_blocks[:1],
        jnp.concatenate([before[0][None], key_blocks[:1]], axis=1),
        jnp.concatenate([before[1][None], value_blocks[:1]], axis=1),
        first_row[:1] - BLK,
    )
    near_out = jnp.concatenate([opening, later], axis=0)
    blocks_here = retrieved.shape[0]
    entries = blocks_here * TOPB
    local_blocks = memory.shape[1] // BLK
    flat_blocks = retrieved.reshape(entries)
    block_index = lax.broadcasted_iota(jnp.int32, (entries, block_home.shape[0]), 1)
    home_slot = jnp.sum(
        jnp.where(block_index == flat_blocks[:, None], block_home[None, :], 0), axis=1
    )
    holder = home_slot // local_blocks
    local_block = home_slot % local_blocks
    local_store = memory.reshape(2, local_blocks, BLK, groups * HD)
    entry_order = jnp.arange(entries)
    earlier = entry_order[None, :] < entry_order[:, None]
    same_owner = holder[:, None] == holder[None, :]
    same_block = home_slot[:, None] == home_slot[None, :]
    first = jnp.sum(same_block & earlier, axis=1) == 0
    first_entry = jnp.argmax(same_block, axis=1)
    before_first = entry_order[None, :] < first_entry[:, None]
    slot_of = jnp.sum(same_owner & before_first & first[None, :], axis=1)
    slot_index = lax.broadcasted_iota(jnp.int32, (holder_count, CAP, entries), 1)
    holder_index = lax.broadcasted_iota(jnp.int32, (holder_count, CAP, entries), 0)
    wanted_ids = jnp.max(
        jnp.where(
            (holder_index == holder[None, None, :]) & (slot_index == slot_of[None, None, :]),
            local_block[None, None, :],
            0,
        ),
        axis=2,
    )
    picked = jnp.take(
        local_store,
        lax.all_to_all(wanted_ids, "mem", split_axis=0, concat_axis=0, tiled=True).reshape(
            holder_count * CAP
        ),
        axis=1,
        mode="clip",
    ).transpose(1, 0, 2, 3)
    fetched = lax.all_to_all(picked, "mem", split_axis=0, concat_axis=0, tiled=True)
    pool = holder_count * CAP
    row_of = entry_order // TOPB
    member = (
        jnp.zeros((blocks_here, pool), jnp.bool_).at[row_of, holder * CAP + slot_of].set(True)
    )
    bias = jnp.where(jnp.repeat(member, BLK, axis=1), 0.0, NEG_FILL).reshape(
        blocks_here, 1, pool * BLK
    )
    mixing = jnp.repeat(jax.nn.sigmoid(gate_logit), HD).reshape(1, groups * HD)
    attended = far_attention(
        projected_flat, fetched, bias, near_out, mixing
    )
    partial = jnp.dot(attended, output_weight, preferred_element_type=jnp.float32)
    half = partial.shape[1] // 2
    return jnp.concatenate(
        [reduce_over_tp(partial[:, :half]), reduce_over_tp(partial[:, half:])], axis=1
    ).astype(jnp.bfloat16)


def reduce_over_tp(partial):
    count = lax.axis_size("tp")
    chips = count // 2
    share = partial.shape[0] // count
    me = lax.axis_index("tp")
    core = me % 2
    chip = me // 2
    split = partial.reshape(chips, 2, share, partial.shape[1])
    mine = lax.dynamic_index_in_dim(split, core, axis=1, keepdims=False)
    other = lax.dynamic_index_in_dim(split, 1 - core, axis=1, keepdims=False)
    arrived = lax.ppermute(
        other.astype(jnp.bfloat16), "tp", [(t, t ^ 1) for t in range(count)]
    )
    chip_sum = mine + arrived.astype(jnp.float32)
    total = lax.dynamic_index_in_dim(chip_sum, chip, axis=0, keepdims=False)
    for shift in range(1, chips):
        outgoing = lax.dynamic_index_in_dim(chip_sum, (chip + shift) % chips, axis=0, keepdims=False)
        pairs = [(t, ((t // 2 + shift) % chips) * 2 + t % 2) for t in range(count)]
        total = total + lax.ppermute(outgoing.astype(jnp.bfloat16), "tp", pairs).astype(jnp.float32)
    return total

def solution(mesh):
    placed = (
        P(("mem", "tp"), None),
        P(None, "tp"),
        P("tp", None),
        P("tp"),
        P(None, "mem", "tp"),
        P("mem", None),
        P(),
    )
    return jax.shard_map(
        local, mesh=mesh, in_specs=placed, out_specs=P(("mem", "tp"), None), check_vma=False
    )
```

```python
import jax
import jax.numpy as jnp
from jax import lax
from jax.sharding import PartitionSpec as P
from jax.experimental import pallas as pl
from jax.experimental.pallas import tpu as pltpu

HD = 128
BLK = 128
TOPB = 16
CAP = 2


NEG_FILL = -1e30


def from_behind(value, axis, steps):
    count = lax.axis_size(axis)
    initial, last = (max(0, -steps), min(count, count - steps))
    return lax.ppermute(value, axis, [(source, source + steps) for source in range(initial, last)])


def softmax_rows(scores, allowed):
    row_peak = jnp.max(jnp.where(allowed, scores, NEG_FILL), axis=-1, keepdims=True)
    weights = jnp.where(allowed, jnp.exp(scores - row_peak), 0.0)
    return (weights / jnp.sum(weights, axis=-1, keepdims=True)).astype(jnp.bfloat16)


def near_part(block_queries, window_keys, window_values, first_key):
    scores = (
        jnp.einsum(
            "nqgd,nkgd->ngqk", block_queries, window_keys, preferred_element_type=jnp.float32
        )
        * (HD ** (-0.5))
    )
    query_index = lax.broadcasted_iota(jnp.int32, (BLK, 2 * BLK), 0)
    key_index = lax.broadcasted_iota(jnp.int32, (BLK, 2 * BLK), 1)
    allowed = (
        (key_index > query_index)[None]
        & (key_index <= query_index + BLK)[None]
        & (key_index[None] + first_key[:, None, None] >= 0)
    )
    probs = softmax_rows(scores, allowed[:, None])
    return jnp.einsum(
        "ngqk,nkgd->ngqd", probs, window_values, preferred_element_type=jnp.float32
    )


def far_kernel(
    q_ref, k0_ref, v0_ref, bk_ref, bv_ref, k_ref, v_ref, bias_ref, near_ref, start_ref, mix_ref, o_ref
):
    pool = k_ref.shape[0]
    keys = k_ref[:, 0].reshape(pool * BLK, HD)
    values = v_ref[:, 0].reshape(pool * BLK, HD)
    mix = mix_ref[...]
    contract = (((1,), (1,)), ((), ()))
    first_query = q_ref[0:BLK, :]
    query_index = lax.broadcasted_iota(jnp.int32, (BLK, BLK), 0)
    key_index = lax.broadcasted_iota(jnp.int32, (BLK, BLK), 1)
    allow_before = (key_index > query_index) & (start_ref[...] > 0.5)
    allow_local = key_index <= query_index
    score_before = lax.dot_general(
        first_query, bk_ref[0], contract, preferred_element_type=jnp.float32
    ) * (HD ** (-0.5))
    score_local = lax.dot_general(
        first_query, k0_ref[...], contract, preferred_element_type=jnp.float32
    ) * (HD ** (-0.5))
    near_peak = jnp.maximum(
        jnp.max(jnp.where(allow_before, score_before, NEG_FILL), axis=-1, keepdims=True),
        jnp.max(jnp.where(allow_local, score_local, NEG_FILL), axis=-1, keepdims=True),
    )
    weight_before = jnp.where(allow_before, jnp.exp(score_before - near_peak), 0.0)
    weight_local = jnp.where(allow_local, jnp.exp(score_local - near_peak), 0.0)
    near_total = jnp.sum(weight_before, axis=-1, keepdims=True) + jnp.sum(
        weight_local, axis=-1, keepdims=True
    )
    first_near = jnp.dot(
        (weight_before / near_total).astype(jnp.bfloat16), bv_ref[0],
        preferred_element_type=jnp.float32,
    ) + jnp.dot(
        (weight_local / near_total).astype(jnp.bfloat16), v0_ref[...],
        preferred_element_type=jnp.float32,
    )
    for block in range(q_ref.shape[0] // BLK):
        rows = slice(block * BLK, (block + 1) * BLK)
        scores = lax.dot_general(
            q_ref[rows, :], keys, contract, preferred_element_type=jnp.float32
        ) + bias_ref[block]
        peak = jnp.max(scores, axis=-1, keepdims=True)
        weights = jnp.exp((scores - peak) * (HD ** (-0.5)))
        scale = 1.0 / jnp.sum(weights, axis=-1, keepdims=True)
        far = jnp.dot(weights.astype(jnp.bfloat16), values, preferred_element_type=jnp.float32)
        near = first_near if block == 0 else near_ref[block - 1, 0]
        o_ref[rows, :] = (mix * (far * scale) + (1.0 - mix) * near).astype(o_ref.dtype)


def far_attention(projected, before, fetched, bias, later, start, mixing):
    rows = projected.shape[0]
    blocks = rows // BLK
    pool = fetched.shape[0]
    groups = fetched.shape[3] // HD
    return pl.pallas_call(
        far_kernel,
        grid=(groups,),
        in_specs=[
            pl.BlockSpec((rows, HD), lambda h: (0, h * 3)),
            pl.BlockSpec((BLK, HD), lambda h: (0, h * 3 + 1)),
            pl.BlockSpec((BLK, HD), lambda h: (0, h * 3 + 2)),
            pl.BlockSpec((1, BLK, HD), lambda h: (0, 0, h)),
            pl.BlockSpec((1, BLK, HD), lambda h: (1, 0, h)),
            pl.BlockSpec((pool, 1, BLK, HD), lambda h: (0, 0, 0, h)),
            pl.BlockSpec((pool, 1, BLK, HD), lambda h: (0, 1, 0, h)),
            pl.BlockSpec((blocks, 1, pool * BLK), lambda h: (0, 0, 0)),
            pl.BlockSpec((blocks - 1, 1, BLK, HD), lambda h: (0, h, 0, 0)),
            pl.BlockSpec((1, BLK), lambda h: (0, 0)),
            pl.BlockSpec((1, HD), lambda h: (0, h)),
        ],
        out_specs=pl.BlockSpec((rows, HD), lambda h: (0, h)),
        out_shape=jax.ShapeDtypeStruct((rows, groups * HD), jnp.bfloat16),
        cost_estimate=pl.CostEstimate(
            flops=groups * (blocks * pool + 2) * 4 * BLK * BLK * HD,
            transcendentals=groups * (blocks * pool + 2) * BLK * BLK,
            bytes_accessed=fetched.size * 2 + rows * groups * HD * 8,
        ),
    )(projected, projected, projected, before, before, fetched, fetched, bias, later, start, mixing)

def gather_tp(part):
    count = lax.axis_size("tp")
    me = lax.axis_index("tp")
    arrived = [part] + [
        lax.ppermute(part, "tp", [(t, (t + shift) % count) for t in range(count)])
        for shift in range(1, count)
    ]
    order = (me - jnp.arange(count)) % count
    return jnp.take(jnp.stack(arrived), order, axis=0, mode="clip").reshape(
        count * part.shape[0], part.shape[1]
    )

def local(tokens, input_weight, output_weight, gate_logit, memory, retrieved, block_home):
    holder_count = lax.axis_size("mem")
    share_rows = tokens.shape[0]
    local_rows = share_rows * lax.axis_size("tp")
    groups = output_weight.shape[0] // HD
    score_scale = HD ** (-0.5)
    projected = jnp.dot(
        gather_tp(tokens),
        input_weight,
        preferred_element_type=jnp.float32,
    )
    projected_flat = projected.astype(jnp.bfloat16)
    projected = projected_flat.reshape(local_rows, groups, 3, HD)
    queries = projected[:, :, 0]
    key_rows = projected[:, :, 1]
    value_rows = projected[:, :, 2]
    last_rows = jnp.stack([key_rows[-BLK:], value_rows[-BLK:]]).reshape(2, BLK, groups * HD)
    before = from_behind(last_rows, "mem", 1)
    blocks_here = local_rows // BLK
    query_blocks = queries.reshape(blocks_here, BLK, groups, HD)
    key_blocks = key_rows.reshape(blocks_here, BLK, groups, HD)
    value_blocks = value_rows.reshape(blocks_here, BLK, groups, HD)
    first_row = lax.axis_index("mem") * local_rows + jnp.arange(blocks_here) * BLK
    later = near_part(
        query_blocks[1:],
        jnp.concatenate([key_blocks[:-1], key_blocks[1:]], axis=1),
        jnp.concatenate([value_blocks[:-1], value_blocks[1:]], axis=1),
        first_row[1:] - BLK,
    )
    blocks_here = retrieved.shape[0]
    entries = blocks_here * TOPB
    local_blocks = memory.shape[1] // BLK
    flat_blocks = retrieved.reshape(entries)
    block_index = lax.broadcasted_iota(jnp.int32, (entries, block_home.shape[0]), 1)
    home_slot = jnp.sum(
        jnp.where(block_index == flat_blocks[:, None], block_home[None, :], 0), axis=1
    )
    holder = home_slot // local_blocks
    local_block = home_slot % local_blocks
    local_store = memory.reshape(2, local_blocks, BLK, groups * HD)
    entry_order = jnp.arange(entries)
    earlier = entry_order[None, :] < entry_order[:, None]
    same_owner = holder[:, None] == holder[None, :]
    same_block = home_slot[:, None] == home_slot[None, :]
    first = jnp.sum(same_block & earlier, axis=1) == 0
    first_entry = jnp.argmax(same_block, axis=1)
    before_first = entry_order[None, :] < first_entry[:, None]
    slot_of = jnp.sum(same_owner & before_first & first[None, :], axis=1)
    slot_index = lax.broadcasted_iota(jnp.int32, (holder_count, CAP, entries), 1)
    holder_index = lax.broadcasted_iota(jnp.int32, (holder_count, CAP, entries), 0)
    wanted_ids = jnp.max(
        jnp.where(
            (holder_index == holder[None, None, :]) & (slot_index == slot_of[None, None, :]),
            local_block[None, None, :],
            0,
        ),
        axis=2,
    )
    asked = lax.all_to_all(wanted_ids, "mem", split_axis=0, concat_axis=0, tiled=True).reshape(
        holder_count * CAP
    )
    picked = jnp.stack(
        [
            lax.dynamic_index_in_dim(local_store, jnp.clip(asked[slot], 0, local_blocks - 1), 1, False)
            for slot in range(holder_count * CAP)
        ]
    )
    fetched = lax.all_to_all(picked, "mem", split_axis=0, concat_axis=0, tiled=True)
    pool = holder_count * CAP
    row_of = entry_order // TOPB
    member = (
        jnp.zeros((blocks_here, pool), jnp.bool_).at[row_of, holder * CAP + slot_of].set(True)
    )
    bias = jnp.where(jnp.repeat(member, BLK, axis=1), 0.0, NEG_FILL).reshape(
        blocks_here, 1, pool * BLK
    )
    mixing = jnp.repeat(jax.nn.sigmoid(gate_logit), HD).reshape(1, groups * HD)
    attended = far_attention(
        projected_flat,
        before,
        fetched,
        bias,
        later,
        jnp.full((1, BLK), jnp.where(lax.axis_index("mem") > 0, 1.0, 0.0), jnp.float32),
        mixing,
    )
    partial = jnp.dot(attended, output_weight, preferred_element_type=jnp.float32)
    half = partial.shape[1] // 2
    return jnp.concatenate(
        [reduce_over_tp(partial[:, :half]), reduce_over_tp(partial[:, half:])], axis=1
    ).astype(jnp.bfloat16)


def reduce_over_tp(partial):
    count = lax.axis_size("tp")
    chips = count // 2
    share = partial.shape[0] // count
    me = lax.axis_index("tp")
    core = me % 2
    chip = me // 2
    split = partial.reshape(chips, 2, share, partial.shape[1])
    mine = lax.dynamic_index_in_dim(split, core, axis=1, keepdims=False)
    other = lax.dynamic_index_in_dim(split, 1 - core, axis=1, keepdims=False)
    arrived = lax.ppermute(
        other.astype(jnp.bfloat16), "tp", [(t, t ^ 1) for t in range(count)]
    )
    chip_sum = mine + arrived.astype(jnp.float32)
    total = lax.dynamic_index_in_dim(chip_sum, chip, axis=0, keepdims=False)
    for shift in range(1, chips):
        outgoing = lax.dynamic_index_in_dim(chip_sum, (chip + shift) % chips, axis=0, keepdims=False)
        pairs = [(t, ((t // 2 + shift) % chips) * 2 + t % 2) for t in range(count)]
        total = total + lax.ppermute(outgoing.astype(jnp.bfloat16), "tp", pairs).astype(jnp.float32)
    return total

def solution(mesh):
    placed = (
        P(("mem", "tp"), None),
        P(None, "tp"),
        P("tp", None),
        P("tp"),
        P(None, "mem", "tp"),
        P("mem", None),
        P(),
    )
    return jax.shard_map(
        local, mesh=mesh, in_specs=placed, out_specs=P(("mem", "tp"), None), check_vma=False
    )
```

```python
import jax
import jax.numpy as jnp
from jax import lax
from jax.sharding import PartitionSpec as P
from jax.experimental import pallas as pl
from jax.experimental.pallas import tpu as pltpu

HD = 128
BLK = 128
TOPB = 16
CAP = 2


NEG_FILL = -1e30


def from_behind(value, axis, steps):
    count = lax.axis_size(axis)
    initial, last = (max(0, -steps), min(count, count - steps))
    return lax.ppermute(value, axis, [(source, source + steps) for source in range(initial, last)])


def softmax_rows(scores, allowed):
    row_peak = jnp.max(jnp.where(allowed, scores, NEG_FILL), axis=-1, keepdims=True)
    weights = jnp.where(allowed, jnp.exp(scores - row_peak), 0.0)
    return (weights / jnp.sum(weights, axis=-1, keepdims=True)).astype(jnp.bfloat16)


def near_part(block_queries, window_keys, window_values, first_key):
    scores = (
        jnp.einsum(
            "nqgd,nkgd->ngqk", block_queries, window_keys, preferred_element_type=jnp.float32
        )
        * (HD ** (-0.5))
    )
    query_index = lax.broadcasted_iota(jnp.int32, (BLK, 2 * BLK), 0)
    key_index = lax.broadcasted_iota(jnp.int32, (BLK, 2 * BLK), 1)
    allowed = (
        (key_index > query_index)[None]
        & (key_index <= query_index + BLK)[None]
        & (key_index[None] + first_key[:, None, None] >= 0)
    )
    probs = softmax_rows(scores, allowed[:, None])
    return jnp.einsum(
        "ngqk,nkgd->ngqd", probs, window_values, preferred_element_type=jnp.float32
    )


def far_kernel(
    q_ref, k0_ref, v0_ref, bk_ref, bv_ref, k_ref, v_ref, bias_ref, near_ref, start_ref, mix_ref, o_ref
):
    pool = k_ref.shape[0]
    keys = k_ref[:, 0].reshape(pool * BLK, HD)
    values = v_ref[:, 0].reshape(pool * BLK, HD)
    mix = mix_ref[...]
    contract = (((1,), (1,)), ((), ()))
    first_query = q_ref[0:BLK, :]
    query_index = lax.broadcasted_iota(jnp.int32, (BLK, BLK), 0)
    key_index = lax.broadcasted_iota(jnp.int32, (BLK, BLK), 1)
    allow_before = (key_index > query_index) & (start_ref[...] > 0.5)
    allow_local = key_index <= query_index
    score_before = lax.dot_general(
        first_query, bk_ref[0], contract, preferred_element_type=jnp.float32
    ) * (HD ** (-0.5))
    score_local = lax.dot_general(
        first_query, k0_ref[...], contract, preferred_element_type=jnp.float32
    ) * (HD ** (-0.5))
    near_peak = jnp.maximum(
        jnp.max(jnp.where(allow_before, score_before, NEG_FILL), axis=-1, keepdims=True),
        jnp.max(jnp.where(allow_local, score_local, NEG_FILL), axis=-1, keepdims=True),
    )
    weight_before = jnp.where(allow_before, jnp.exp(score_before - near_peak), 0.0)
    weight_local = jnp.where(allow_local, jnp.exp(score_local - near_peak), 0.0)
    near_total = jnp.sum(weight_before, axis=-1, keepdims=True) + jnp.sum(
        weight_local, axis=-1, keepdims=True
    )
    first_near = jnp.dot(
        (weight_before / near_total).astype(jnp.bfloat16), bv_ref[0],
        preferred_element_type=jnp.float32,
    ) + jnp.dot(
        (weight_local / near_total).astype(jnp.bfloat16), v0_ref[...],
        preferred_element_type=jnp.float32,
    )
    for block in range(q_ref.shape[0] // BLK):
        rows = slice(block * BLK, (block + 1) * BLK)
        scores = lax.dot_general(
            q_ref[rows, :], keys, contract, preferred_element_type=jnp.float32
        ) + bias_ref[block]
        peak = jnp.max(scores, axis=-1, keepdims=True)
        weights = jnp.exp((scores - peak) * (HD ** (-0.5)))
        scale = 1.0 / jnp.sum(weights, axis=-1, keepdims=True)
        far = jnp.dot(weights.astype(jnp.bfloat16), values, preferred_element_type=jnp.float32)
        near = first_near if block == 0 else near_ref[block - 1, 0]
        o_ref[rows, :] = (mix * (far * scale) + (1.0 - mix) * near).astype(o_ref.dtype)


def far_attention(projected, before, fetched, bias, later, start, mixing):
    rows = projected.shape[0]
    blocks = rows // BLK
    pool = fetched.shape[0]
    groups = fetched.shape[3] // HD
    return pl.pallas_call(
        far_kernel,
        grid=(groups,),
        in_specs=[
            pl.BlockSpec((rows, HD), lambda h: (0, h * 3)),
            pl.BlockSpec((BLK, HD), lambda h: (0, h * 3 + 1)),
            pl.BlockSpec((BLK, HD), lambda h: (0, h * 3 + 2)),
            pl.BlockSpec((1, BLK, HD), lambda h: (0, 0, h)),
            pl.BlockSpec((1, BLK, HD), lambda h: (1, 0, h)),
            pl.BlockSpec((pool, 1, BLK, HD), lambda h: (0, 0, 0, h)),
            pl.BlockSpec((pool, 1, BLK, HD), lambda h: (0, 1, 0, h)),
            pl.BlockSpec((blocks, 1, pool * BLK), lambda h: (0, 0, 0)),
            pl.BlockSpec((blocks - 1, 1, BLK, HD), lambda h: (0, h, 0, 0)),
            pl.BlockSpec((1, BLK), lambda h: (0, 0)),
            pl.BlockSpec((1, HD), lambda h: (0, h)),
        ],
        out_specs=pl.BlockSpec((rows, HD), lambda h: (0, h)),
        out_shape=jax.ShapeDtypeStruct((rows, groups * HD), jnp.bfloat16),
        cost_estimate=pl.CostEstimate(
            flops=groups * (blocks * pool + 2) * 4 * BLK * BLK * HD,
            transcendentals=groups * (blocks * pool + 2) * BLK * BLK,
            bytes_accessed=fetched.size * 2 + rows * groups * HD * 8,
        ),
    )(projected, projected, projected, before, before, fetched, fetched, bias, later, start, mixing)

def gather_tp(part):
    count = lax.axis_size("tp")
    me = lax.axis_index("tp")
    arrived = [part] + [
        lax.ppermute(part, "tp", [(t, (t + shift) % count) for t in range(count)])
        for shift in range(1, count)
    ]
    order = (me - jnp.arange(count)) % count
    return jnp.take(jnp.stack(arrived), order, axis=0, mode="clip").reshape(
        count * part.shape[0], part.shape[1]
    )

def local(tokens, input_weight, output_weight, gate_logit, memory, retrieved, block_home):
    holder_count = lax.axis_size("mem")
    share_rows = tokens.shape[0]
    local_rows = share_rows * lax.axis_size("tp")
    groups = output_weight.shape[0] // HD
    score_scale = HD ** (-0.5)
    projected = jnp.dot(
        gather_tp(tokens),
        input_weight,
        preferred_element_type=jnp.float32,
    )
    projected_flat = projected.astype(jnp.bfloat16)
    projected = projected_flat.reshape(local_rows, groups, 3, HD)
    queries = projected[:, :, 0]
    key_rows = projected[:, :, 1]
    value_rows = projected[:, :, 2]
    last_rows = jnp.stack([key_rows[-BLK:], value_rows[-BLK:]]).reshape(2, BLK, groups * HD)
    before = from_behind(last_rows, "mem", 1)
    blocks_here = local_rows // BLK
    query_blocks = queries.reshape(blocks_here, BLK, groups, HD)
    key_blocks = key_rows.reshape(blocks_here, BLK, groups, HD)
    value_blocks = value_rows.reshape(blocks_here, BLK, groups, HD)
    first_row = lax.axis_index("mem") * local_rows + jnp.arange(blocks_here) * BLK
    later = near_part(
        query_blocks[1:],
        jnp.concatenate([key_blocks[:-1], key_blocks[1:]], axis=1),
        jnp.concatenate([value_blocks[:-1], value_blocks[1:]], axis=1),
        first_row[1:] - BLK,
    )
    blocks_here = retrieved.shape[0]
    entries = blocks_here * TOPB
    local_blocks = memory.shape[1] // BLK
    flat_blocks = retrieved.reshape(entries)
    block_index = lax.broadcasted_iota(jnp.int32, (entries, block_home.shape[0]), 1)
    home_slot = jnp.sum(
        jnp.where(block_index == flat_blocks[:, None], block_home[None, :], 0), axis=1
    )
    holder = home_slot // local_blocks
    local_block = home_slot % local_blocks
    local_store = memory.reshape(2, local_blocks, BLK, groups * HD)
    entry_order = jnp.arange(entries)
    earlier = entry_order[None, :] < entry_order[:, None]
    same_owner = holder[:, None] == holder[None, :]
    same_block = home_slot[:, None] == home_slot[None, :]
    first = jnp.sum(same_block & earlier, axis=1) == 0
    first_entry = jnp.argmax(same_block, axis=1)
    before_first = entry_order[None, :] < first_entry[:, None]
    slot_of = jnp.sum(same_owner & before_first & first[None, :], axis=1)
    slot_index = lax.broadcasted_iota(jnp.int32, (holder_count, CAP, entries), 1)
    holder_index = lax.broadcasted_iota(jnp.int32, (holder_count, CAP, entries), 0)
    wanted_ids = jnp.max(
        jnp.where(
            (holder_index == holder[None, None, :]) & (slot_index == slot_of[None, None, :]),
            local_block[None, None, :],
            0,
        ),
        axis=2,
    )
    picked = jnp.take(
        local_store,
        lax.all_to_all(wanted_ids, "mem", split_axis=0, concat_axis=0, tiled=True).reshape(
            holder_count * CAP
        ),
        axis=1,
        mode="clip",
    ).transpose(1, 0, 2, 3)
    fetched = lax.all_to_all(picked, "mem", split_axis=0, concat_axis=0, tiled=True)
    pool = holder_count * CAP
    row_of = entry_order // TOPB
    member = (
        jnp.zeros((blocks_here, pool), jnp.bool_).at[row_of, holder * CAP + slot_of].set(True)
    )
    bias = jnp.where(jnp.repeat(member, BLK, axis=1), 0.0, NEG_FILL).reshape(
        blocks_here, 1, pool * BLK
    )
    mixing = jnp.repeat(jax.nn.sigmoid(gate_logit), HD).reshape(1, groups * HD)
    attended = far_attention(
        projected_flat,
        before,
        fetched,
        bias,
        later,
        jnp.full((1, BLK), jnp.where(lax.axis_index("mem") > 0, 1.0, 0.0), jnp.float32),
        mixing,
    )
    partial = jnp.dot(attended, output_weight, preferred_element_type=jnp.float32)
    half = partial.shape[1] // 2
    return jnp.concatenate(
        [reduce_over_tp(partial[:, :half]), reduce_over_tp(partial[:, half:])], axis=1
    ).astype(jnp.bfloat16)


def reduce_over_tp(partial):
    count = lax.axis_size("tp")
    chips = count // 2
    share = partial.shape[0] // count
    me = lax.axis_index("tp")
    core = me % 2
    chip = me // 2
    split = partial.reshape(chips, 2, share, partial.shape[1])
    mine = lax.dynamic_index_in_dim(split, core, axis=1, keepdims=False)
    other = lax.dynamic_index_in_dim(split, 1 - core, axis=1, keepdims=False)
    arrived = lax.ppermute(
        other.astype(jnp.bfloat16), "tp", [(t, t ^ 1) for t in range(count)]
    )
    chip_sum = mine + arrived.astype(jnp.float32)
    total = lax.dynamic_index_in_dim(chip_sum, chip, axis=0, keepdims=False)
    for shift in range(1, chips):
        outgoing = lax.dynamic_index_in_dim(chip_sum, (chip + shift) % chips, axis=0, keepdims=False)
        pairs = [(t, ((t // 2 + shift) % chips) * 2 + t % 2) for t in range(count)]
        total = total + lax.ppermute(outgoing.astype(jnp.bfloat16), "tp", pairs).astype(jnp.float32)
    return total

def solution(mesh):
    placed = (
        P(("mem", "tp"), None),
        P(None, "tp"),
        P("tp", None),
        P("tp"),
        P(None, "mem", "tp"),
        P("mem", None),
        P(),
    )
    return jax.shard_map(
        local, mesh=mesh, in_specs=placed, out_specs=P(("mem", "tp"), None), check_vma=False
    )
```

```python
import jax
import jax.numpy as jnp
from jax import lax
from jax.sharding import PartitionSpec as P
from jax.experimental import pallas as pl
from jax.experimental.pallas import tpu as pltpu

HD = 128
BLK = 128
TOPB = 16
CAP = 2


NEG_FILL = -1e30


def from_behind(value, axis, steps):
    count = lax.axis_size(axis)
    initial, last = (max(0, -steps), min(count, count - steps))
    return lax.ppermute(value, axis, [(source, source + steps) for source in range(initial, last)])


def softmax_rows(scores, allowed):
    row_peak = jnp.max(jnp.where(allowed, scores, NEG_FILL), axis=-1, keepdims=True)
    weights = jnp.where(allowed, jnp.exp(scores - row_peak), 0.0)
    return (weights / jnp.sum(weights, axis=-1, keepdims=True)).astype(jnp.bfloat16)


def near_part(block_queries, window_keys, window_values, first_key):
    scores = (
        jnp.einsum(
            "nqgd,nkgd->ngqk", block_queries, window_keys, preferred_element_type=jnp.float32
        )
        * (HD ** (-0.5))
    )
    query_index = lax.broadcasted_iota(jnp.int32, (BLK, 2 * BLK), 0)
    key_index = lax.broadcasted_iota(jnp.int32, (BLK, 2 * BLK), 1)
    allowed = (
        (key_index > query_index)[None]
        & (key_index <= query_index + BLK)[None]
        & (key_index[None] + first_key[:, None, None] >= 0)
    )
    probs = softmax_rows(scores, allowed[:, None])
    return jnp.einsum(
        "ngqk,nkgd->ngqd", probs, window_values, preferred_element_type=jnp.float32
    )


def far_kernel(
    q_ref, k0_ref, v0_ref, bk_ref, bv_ref, k_ref, v_ref, bias_ref, near_ref, start_ref, mix_ref, o_ref
):
    pool = k_ref.shape[0]
    keys = k_ref[:, 0].reshape(pool * BLK, HD)
    values = v_ref[:, 0].reshape(pool * BLK, HD)
    mix = mix_ref[...]
    contract = (((1,), (1,)), ((), ()))
    first_query = q_ref[0:BLK, :]
    query_index = lax.broadcasted_iota(jnp.int32, (BLK, BLK), 0)
    key_index = lax.broadcasted_iota(jnp.int32, (BLK, BLK), 1)
    allow_before = (key_index > query_index) & (start_ref[...] > 0.5)
    allow_local = key_index <= query_index
    score_before = lax.dot_general(
        first_query, bk_ref[0], contract, preferred_element_type=jnp.float32
    ) * (HD ** (-0.5))
    score_local = lax.dot_general(
        first_query, k0_ref[...], contract, preferred_element_type=jnp.float32
    ) * (HD ** (-0.5))
    near_peak = jnp.maximum(
        jnp.max(jnp.where(allow_before, score_before, NEG_FILL), axis=-1, keepdims=True),
        jnp.max(jnp.where(allow_local, score_local, NEG_FILL), axis=-1, keepdims=True),
    )
    weight_before = jnp.where(allow_before, jnp.exp(score_before - near_peak), 0.0)
    weight_local = jnp.where(allow_local, jnp.exp(score_local - near_peak), 0.0)
    near_total = jnp.sum(weight_before, axis=-1, keepdims=True) + jnp.sum(
        weight_local, axis=-1, keepdims=True
    )
    first_near = jnp.dot(
        (weight_before / near_total).astype(jnp.bfloat16), bv_ref[0],
        preferred_element_type=jnp.float32,
    ) + jnp.dot(
        (weight_local / near_total).astype(jnp.bfloat16), v0_ref[...],
        preferred_element_type=jnp.float32,
    )
    for block in range(q_ref.shape[0] // BLK):
        rows = slice(block * BLK, (block + 1) * BLK)
        scores = lax.dot_general(
            q_ref[rows, :], keys, contract, preferred_element_type=jnp.float32
        ) + bias_ref[block]
        peak = jnp.max(scores, axis=-1, keepdims=True)
        weights = jnp.exp((scores - peak) * (HD ** (-0.5)))
        scale = 1.0 / jnp.sum(weights, axis=-1, keepdims=True)
        far = jnp.dot(weights.astype(jnp.bfloat16), values, preferred_element_type=jnp.float32)
        near = first_near if block == 0 else near_ref[block - 1, 0]
        o_ref[rows, :] = (mix * (far * scale) + (1.0 - mix) * near).astype(o_ref.dtype)


def far_attention(projected, before, fetched, bias, later, start, mixing):
    rows = projected.shape[0]
    blocks = rows // BLK
    pool = fetched.shape[0]
    groups = fetched.shape[3] // HD
    return pl.pallas_call(
        far_kernel,
        grid=(groups,),
        in_specs=[
            pl.BlockSpec((rows, HD), lambda h: (0, h * 3)),
            pl.BlockSpec((BLK, HD), lambda h: (0, h * 3 + 1)),
            pl.BlockSpec((BLK, HD), lambda h: (0, h * 3 + 2)),
            pl.BlockSpec((1, BLK, HD), lambda h: (0, 0, h)),
            pl.BlockSpec((1, BLK, HD), lambda h: (1, 0, h)),
            pl.BlockSpec((pool, 1, BLK, HD), lambda h: (0, 0, 0, h)),
            pl.BlockSpec((pool, 1, BLK, HD), lambda h: (0, 1, 0, h)),
            pl.BlockSpec((blocks, 1, pool * BLK), lambda h: (0, 0, 0)),
            pl.BlockSpec((blocks - 1, 1, BLK, HD), lambda h: (0, h, 0, 0)),
            pl.BlockSpec((1, BLK), lambda h: (0, 0)),
            pl.BlockSpec((1, HD), lambda h: (0, h)),
        ],
        out_specs=pl.BlockSpec((rows, HD), lambda h: (0, h)),
        out_shape=jax.ShapeDtypeStruct((rows, groups * HD), jnp.bfloat16),
        cost_estimate=pl.CostEstimate(
            flops=groups * (blocks * pool + 2) * 4 * BLK * BLK * HD,
            transcendentals=groups * (blocks * pool + 2) * BLK * BLK,
            bytes_accessed=fetched.size * 2 + rows * groups * HD * 8,
        ),
    )(projected, projected, projected, before, before, fetched, fetched, bias, later, start, mixing)

def gather_tp(part):
    count = lax.axis_size("tp")
    me = lax.axis_index("tp")
    arrived = [part] + [
        lax.ppermute(part, "tp", [(t, (t + shift) % count) for t in range(count)])
        for shift in range(1, count)
    ]
    order = (me - jnp.arange(count)) % count
    return jnp.take(jnp.stack(arrived), order, axis=0, mode="clip").reshape(
        count * part.shape[0], part.shape[1]
    )

def local(tokens, input_weight, output_weight, gate_logit, memory, retrieved, block_home):
    holder_count = lax.axis_size("mem")
    share_rows = tokens.shape[0]
    local_rows = share_rows * lax.axis_size("tp")
    groups = output_weight.shape[0] // HD
    score_scale = HD ** (-0.5)
    projected = jnp.dot(
        gather_tp(tokens),
        input_weight,
        preferred_element_type=jnp.float32,
    )
    projected_flat = projected.astype(jnp.bfloat16)
    projected = projected_flat.reshape(local_rows, groups, 3, HD)
    queries = projected[:, :, 0]
    key_rows = projected[:, :, 1]
    value_rows = projected[:, :, 2]
    last_rows = jnp.stack([key_rows[-BLK:], value_rows[-BLK:]]).reshape(2, BLK, groups * HD)
    before = from_behind(last_rows, "mem", 1)
    blocks_here = local_rows // BLK
    query_blocks = queries.reshape(blocks_here, BLK, groups, HD)
    key_blocks = key_rows.reshape(blocks_here, BLK, groups, HD)
    value_blocks = value_rows.reshape(blocks_here, BLK, groups, HD)
    first_row = lax.axis_index("mem") * local_rows + jnp.arange(blocks_here) * BLK
    later = near_part(
        query_blocks[1:],
        jnp.concatenate([key_blocks[:-1], key_blocks[1:]], axis=1),
        jnp.concatenate([value_blocks[:-1], value_blocks[1:]], axis=1),
        first_row[1:] - BLK,
    )
    blocks_here = retrieved.shape[0]
    entries = blocks_here * TOPB
    local_blocks = memory.shape[1] // BLK
    flat_blocks = retrieved.reshape(entries)
    block_index = lax.broadcasted_iota(jnp.int32, (entries, block_home.shape[0]), 1)
    home_slot = jnp.sum(
        jnp.where(block_index == flat_blocks[:, None], block_home[None, :], 0), axis=1
    )
    holder = home_slot // local_blocks
    local_block = home_slot % local_blocks
    local_store = memory.reshape(2, local_blocks, BLK, groups * HD)
    entry_order = jnp.arange(entries)
    earlier = entry_order[None, :] < entry_order[:, None]
    same_owner = holder[:, None] == holder[None, :]
    same_block = home_slot[:, None] == home_slot[None, :]
    first = jnp.sum(same_block & earlier, axis=1) == 0
    first_entry = jnp.argmax(same_block, axis=1)
    before_first = entry_order[None, :] < first_entry[:, None]
    slot_of = jnp.sum(same_owner & before_first & first[None, :], axis=1)
    slot_index = lax.broadcasted_iota(jnp.int32, (holder_count, CAP, entries), 1)
    holder_index = lax.broadcasted_iota(jnp.int32, (holder_count, CAP, entries), 0)
    wanted_ids = jnp.max(
        jnp.where(
            (holder_index == holder[None, None, :]) & (slot_index == slot_of[None, None, :]),
            local_block[None, None, :],
            0,
        ),
        axis=2,
    )
    picked = jnp.take(
        local_store,
        lax.all_to_all(wanted_ids, "mem", split_axis=0, concat_axis=0, tiled=True).reshape(
            holder_count * CAP
        ),
        axis=1,
        mode="clip",
    ).transpose(1, 0, 2, 3)
    fetched = lax.all_to_all(picked, "mem", split_axis=0, concat_axis=0, tiled=True)
    pool = holder_count * CAP
    row_of = entry_order // TOPB
    member = (
        jnp.zeros((blocks_here, pool), jnp.bool_).at[row_of, holder * CAP + slot_of].set(True)
    )
    bias = jnp.where(jnp.repeat(member, BLK, axis=1), 0.0, NEG_FILL).reshape(
        blocks_here, 1, pool * BLK
    )
    mixing = jnp.repeat(jax.nn.sigmoid(gate_logit), HD).reshape(1, groups * HD)
    attended = far_attention(
        projected_flat,
        before,
        fetched,
        bias,
        later,
        jnp.full((1, BLK), jnp.where(lax.axis_index("mem") > 0, 1.0, 0.0), jnp.float32),
        mixing,
    )
    partial = jnp.dot(attended, output_weight, preferred_element_type=jnp.float32)
    width = partial.shape[1] // 4
    return jnp.concatenate(
        [reduce_over_tp(partial[:, k * width:(k + 1) * width]) for k in range(4)], axis=1
    ).astype(jnp.bfloat16)


def reduce_over_tp(partial):
    count = lax.axis_size("tp")
    chips = count // 2
    share = partial.shape[0] // count
    me = lax.axis_index("tp")
    core = me % 2
    chip = me // 2
    split = partial.reshape(chips, 2, share, partial.shape[1])
    mine = lax.dynamic_index_in_dim(split, core, axis=1, keepdims=False)
    other = lax.dynamic_index_in_dim(split, 1 - core, axis=1, keepdims=False)
    arrived = lax.ppermute(
        other.astype(jnp.bfloat16), "tp", [(t, t ^ 1) for t in range(count)]
    )
    chip_sum = mine + arrived.astype(jnp.float32)
    total = lax.dynamic_index_in_dim(chip_sum, chip, axis=0, keepdims=False)
    for shift in range(1, chips):
        outgoing = lax.dynamic_index_in_dim(chip_sum, (chip + shift) % chips, axis=0, keepdims=False)
        pairs = [(t, ((t // 2 + shift) % chips) * 2 + t % 2) for t in range(count)]
        total = total + lax.ppermute(outgoing.astype(jnp.bfloat16), "tp", pairs).astype(jnp.float32)
    return total

def solution(mesh):
    placed = (
        P(("mem", "tp"), None),
        P(None, "tp"),
        P("tp", None),
        P("tp"),
        P(None, "mem", "tp"),
        P("mem", None),
        P(),
    )
    return jax.shard_map(
        local, mesh=mesh, in_specs=placed, out_specs=P(("mem", "tp"), None), check_vma=False
    )
```

```python
import jax
import jax.numpy as jnp
from jax import lax
from jax.sharding import PartitionSpec as P
from jax.experimental import pallas as pl
from jax.experimental.pallas import tpu as pltpu

HD = 128
BLK = 128
TOPB = 16
CAP = 2


NEG_FILL = -1e30


def from_behind(value, axis, steps):
    count = lax.axis_size(axis)
    initial, last = (max(0, -steps), min(count, count - steps))
    return lax.ppermute(value, axis, [(source, source + steps) for source in range(initial, last)])


def softmax_rows(scores, allowed):
    row_peak = jnp.max(jnp.where(allowed, scores, NEG_FILL), axis=-1, keepdims=True)
    weights = jnp.where(allowed, jnp.exp(scores - row_peak), 0.0)
    return (weights / jnp.sum(weights, axis=-1, keepdims=True)).astype(jnp.bfloat16)


def near_part(block_queries, window_keys, window_values, first_key):
    scores = (
        jnp.einsum(
            "nqgd,nkgd->ngqk", block_queries, window_keys, preferred_element_type=jnp.float32
        )
        * (HD ** (-0.5))
    )
    query_index = lax.broadcasted_iota(jnp.int32, (BLK, 2 * BLK), 0)
    key_index = lax.broadcasted_iota(jnp.int32, (BLK, 2 * BLK), 1)
    allowed = (
        (key_index > query_index)[None]
        & (key_index <= query_index + BLK)[None]
        & (key_index[None] + first_key[:, None, None] >= 0)
    )
    probs = softmax_rows(scores, allowed[:, None])
    return jnp.einsum(
        "ngqk,nkgd->ngqd", probs, window_values, preferred_element_type=jnp.float32
    )


def far_kernel(
    q_ref, k0_ref, v0_ref, bk_ref, bv_ref, k_ref, v_ref, bias_ref, near_ref, start_ref, mix_ref, o_ref
):
    pool = k_ref.shape[0]
    keys = k_ref[:, 0].reshape(pool * BLK, HD)
    values = v_ref[:, 0].reshape(pool * BLK, HD)
    mix = mix_ref[...]
    contract = (((1,), (1,)), ((), ()))
    first_query = q_ref[0:BLK, :]
    query_index = lax.broadcasted_iota(jnp.int32, (BLK, BLK), 0)
    key_index = lax.broadcasted_iota(jnp.int32, (BLK, BLK), 1)
    allow_before = (key_index > query_index) & (start_ref[...] > 0.5)
    allow_local = key_index <= query_index
    score_before = lax.dot_general(
        first_query, bk_ref[0], contract, preferred_element_type=jnp.float32
    ) * (HD ** (-0.5))
    score_local = lax.dot_general(
        first_query, k0_ref[...], contract, preferred_element_type=jnp.float32
    ) * (HD ** (-0.5))
    near_peak = jnp.maximum(
        jnp.max(jnp.where(allow_before, score_before, NEG_FILL), axis=-1, keepdims=True),
        jnp.max(jnp.where(allow_local, score_local, NEG_FILL), axis=-1, keepdims=True),
    )
    weight_before = jnp.where(allow_before, jnp.exp(score_before - near_peak), 0.0)
    weight_local = jnp.where(allow_local, jnp.exp(score_local - near_peak), 0.0)
    near_total = jnp.sum(weight_before, axis=-1, keepdims=True) + jnp.sum(
        weight_local, axis=-1, keepdims=True
    )
    first_near = jnp.dot(
        (weight_before / near_total).astype(jnp.bfloat16), bv_ref[0],
        preferred_element_type=jnp.float32,
    ) + jnp.dot(
        (weight_local / near_total).astype(jnp.bfloat16), v0_ref[...],
        preferred_element_type=jnp.float32,
    )
    for block in range(q_ref.shape[0] // BLK):
        rows = slice(block * BLK, (block + 1) * BLK)
        scores = lax.dot_general(
            q_ref[rows, :], keys, contract, preferred_element_type=jnp.float32
        ) + bias_ref[block]
        peak = jnp.max(scores, axis=-1, keepdims=True)
        weights = jnp.exp((scores - peak) * (HD ** (-0.5)))
        scale = 1.0 / jnp.sum(weights, axis=-1, keepdims=True)
        far = jnp.dot(weights.astype(jnp.bfloat16), values, preferred_element_type=jnp.float32)
        near = first_near if block == 0 else near_ref[block - 1, 0]
        o_ref[rows, :] = (mix * (far * scale) + (1.0 - mix) * near).astype(o_ref.dtype)


def far_attention(projected, before, fetched, bias, later, start, mixing):
    rows = projected.shape[0]
    blocks = rows // BLK
    pool = fetched.shape[0]
    groups = fetched.shape[3] // HD
    return pl.pallas_call(
        far_kernel,
        grid=(groups,),
        in_specs=[
            pl.BlockSpec((rows, HD), lambda h: (0, h * 3)),
            pl.BlockSpec((BLK, HD), lambda h: (0, h * 3 + 1)),
            pl.BlockSpec((BLK, HD), lambda h: (0, h * 3 + 2)),
            pl.BlockSpec((1, BLK, HD), lambda h: (0, 0, h)),
            pl.BlockSpec((1, BLK, HD), lambda h: (1, 0, h)),
            pl.BlockSpec((pool, 1, BLK, HD), lambda h: (0, 0, 0, h)),
            pl.BlockSpec((pool, 1, BLK, HD), lambda h: (0, 1, 0, h)),
            pl.BlockSpec((blocks, 1, pool * BLK), lambda h: (0, 0, 0)),
            pl.BlockSpec((blocks - 1, 1, BLK, HD), lambda h: (0, h, 0, 0)),
            pl.BlockSpec((1, BLK), lambda h: (0, 0)),
            pl.BlockSpec((1, HD), lambda h: (0, h)),
        ],
        out_specs=pl.BlockSpec((rows, HD), lambda h: (0, h)),
        out_shape=jax.ShapeDtypeStruct((rows, groups * HD), jnp.bfloat16),
        cost_estimate=pl.CostEstimate(
            flops=groups * (blocks * pool + 2) * 4 * BLK * BLK * HD,
            transcendentals=groups * (blocks * pool + 2) * BLK * BLK,
            bytes_accessed=fetched.size * 2 + rows * groups * HD * 8,
        ),
    )(projected, projected, projected, before, before, fetched, fetched, bias, later, start, mixing)

def gather_tp(part):
    count = lax.axis_size("tp")
    me = lax.axis_index("tp")
    arrived = [part] + [
        lax.ppermute(part, "tp", [(t, (t + shift) % count) for t in range(count)])
        for shift in range(1, count)
    ]
    order = (me - jnp.arange(count)) % count
    return jnp.take(jnp.stack(arrived), order, axis=0, mode="clip").reshape(
        count * part.shape[0], part.shape[1]
    )

def local(tokens, input_weight, output_weight, gate_logit, memory, retrieved, block_home):
    holder_count = lax.axis_size("mem")
    share_rows = tokens.shape[0]
    local_rows = share_rows * lax.axis_size("tp")
    groups = output_weight.shape[0] // HD
    score_scale = HD ** (-0.5)
    projected = jnp.dot(
        gather_tp(tokens),
        input_weight,
        preferred_element_type=jnp.float32,
    )
    projected_flat = projected.astype(jnp.bfloat16)
    projected = projected_flat.reshape(local_rows, groups, 3, HD)
    queries = projected[:, :, 0]
    key_rows = projected[:, :, 1]
    value_rows = projected[:, :, 2]
    last_rows = jnp.stack([key_rows[-BLK:], value_rows[-BLK:]]).reshape(2, BLK, groups * HD)
    before = from_behind(last_rows, "mem", 1)
    blocks_here = local_rows // BLK
    query_blocks = queries.reshape(blocks_here, BLK, groups, HD)
    key_blocks = key_rows.reshape(blocks_here, BLK, groups, HD)
    value_blocks = value_rows.reshape(blocks_here, BLK, groups, HD)
    first_row = lax.axis_index("mem") * local_rows + jnp.arange(blocks_here) * BLK
    later = near_part(
        query_blocks[1:],
        jnp.concatenate([key_blocks[:-1], key_blocks[1:]], axis=1),
        jnp.concatenate([value_blocks[:-1], value_blocks[1:]], axis=1),
        first_row[1:] - BLK,
    )
    blocks_here = retrieved.shape[0]
    entries = blocks_here * TOPB
    local_blocks = memory.shape[1] // BLK
    flat_blocks = retrieved.reshape(entries)
    block_index = lax.broadcasted_iota(jnp.int32, (entries, block_home.shape[0]), 1)
    home_slot = jnp.sum(
        jnp.where(block_index == flat_blocks[:, None], block_home[None, :], 0), axis=1
    )
    holder = home_slot // local_blocks
    local_block = home_slot % local_blocks
    local_store = memory.reshape(2, local_blocks, BLK, groups * HD)
    entry_order = jnp.arange(entries)
    earlier = entry_order[None, :] < entry_order[:, None]
    same_owner = holder[:, None] == holder[None, :]
    same_block = home_slot[:, None] == home_slot[None, :]
    first = jnp.sum(same_block & earlier, axis=1) == 0
    first_entry = jnp.argmax(same_block, axis=1)
    before_first = entry_order[None, :] < first_entry[:, None]
    slot_of = jnp.sum(same_owner & before_first & first[None, :], axis=1)
    slot_index = lax.broadcasted_iota(jnp.int32, (holder_count, CAP, entries), 1)
    holder_index = lax.broadcasted_iota(jnp.int32, (holder_count, CAP, entries), 0)
    wanted_ids = jnp.max(
        jnp.where(
            (holder_index == holder[None, None, :]) & (slot_index == slot_of[None, None, :]),
            local_block[None, None, :],
            0,
        ),
        axis=2,
    )
    picked = jnp.take(
        local_store,
        lax.all_to_all(wanted_ids, "mem", split_axis=0, concat_axis=0, tiled=True).reshape(
            holder_count * CAP
        ),
        axis=1,
        mode="clip",
    ).transpose(1, 0, 2, 3)
    fetched = lax.all_to_all(picked, "mem", split_axis=0, concat_axis=0, tiled=True)
    pool = holder_count * CAP
    row_of = entry_order // TOPB
    member = (
        jnp.zeros((blocks_here, pool), jnp.bool_).at[row_of, holder * CAP + slot_of].set(True)
    )
    bias = jnp.where(jnp.repeat(member, BLK, axis=1), 0.0, NEG_FILL).reshape(
        blocks_here, 1, pool * BLK
    )
    mixing = jnp.repeat(jax.nn.sigmoid(gate_logit), HD).reshape(1, groups * HD)
    attended = far_attention(
        projected_flat,
        before,
        fetched,
        bias,
        later,
        jnp.full((1, BLK), jnp.where(lax.axis_index("mem") > 0, 1.0, 0.0), jnp.float32),
        mixing,
    )
    partial = jnp.dot(attended, output_weight, preferred_element_type=jnp.float32)
    width = 4 * HD
    return jnp.concatenate(
        [
            reduce_over_tp(partial[:, k * width:(k + 1) * width])
            for k in range(partial.shape[1] // width)
        ],
        axis=1,
    ).astype(jnp.bfloat16)


def reduce_over_tp(partial):
    count = lax.axis_size("tp")
    chips = count // 2
    share = partial.shape[0] // count
    me = lax.axis_index("tp")
    core = me % 2
    chip = me // 2
    split = partial.reshape(chips, 2, share, partial.shape[1])
    mine = lax.dynamic_index_in_dim(split, core, axis=1, keepdims=False)
    other = lax.dynamic_index_in_dim(split, 1 - core, axis=1, keepdims=False)
    arrived = lax.ppermute(
        other.astype(jnp.bfloat16), "tp", [(t, t ^ 1) for t in range(count)]
    )
    chip_sum = mine + arrived.astype(jnp.float32)
    total = lax.dynamic_index_in_dim(chip_sum, chip, axis=0, keepdims=False)
    for shift in range(1, chips):
        outgoing = lax.dynamic_index_in_dim(chip_sum, (chip + shift) % chips, axis=0, keepdims=False)
        pairs = [(t, ((t // 2 + shift) % chips) * 2 + t % 2) for t in range(count)]
        total = total + lax.ppermute(outgoing.astype(jnp.bfloat16), "tp", pairs).astype(jnp.float32)
    return total

def solution(mesh):
    placed = (
        P(("mem", "tp"), None),
        P(None, "tp"),
        P("tp", None),
        P("tp"),
        P(None, "mem", "tp"),
        P("mem", None),
        P(),
    )
    return jax.shard_map(
        local, mesh=mesh, in_specs=placed, out_specs=P(("mem", "tp"), None), check_vma=False
    )
```

```python
import jax
import jax.numpy as jnp
from jax import lax
from jax.sharding import PartitionSpec as P
from jax.experimental import pallas as pl
from jax.experimental.pallas import tpu as pltpu

HD = 128
BLK = 128
TOPB = 16
CAP = 2


NEG_FILL = -1e30


def from_behind(value, axis, steps):
    count = lax.axis_size(axis)
    initial, last = (max(0, -steps), min(count, count - steps))
    return lax.ppermute(value, axis, [(source, source + steps) for source in range(initial, last)])


def softmax_rows(scores, allowed):
    row_peak = jnp.max(jnp.where(allowed, scores, NEG_FILL), axis=-1, keepdims=True)
    weights = jnp.where(allowed, jnp.exp(scores - row_peak), 0.0)
    return (weights / jnp.sum(weights, axis=-1, keepdims=True)).astype(jnp.bfloat16)


def near_part(block_queries, window_keys, window_values, first_key):
    scores = (
        jnp.einsum(
            "nqgd,nkgd->ngqk", block_queries, window_keys, preferred_element_type=jnp.float32
        )
        * (HD ** (-0.5))
    )
    query_index = lax.broadcasted_iota(jnp.int32, (BLK, 2 * BLK), 0)
    key_index = lax.broadcasted_iota(jnp.int32, (BLK, 2 * BLK), 1)
    allowed = (
        (key_index > query_index)[None]
        & (key_index <= query_index + BLK)[None]
        & (key_index[None] + first_key[:, None, None] >= 0)
    )
    probs = softmax_rows(scores, allowed[:, None])
    return jnp.einsum(
        "ngqk,nkgd->ngqd", probs, window_values, preferred_element_type=jnp.float32
    )


def far_kernel(
    q_ref, k0_ref, v0_ref, bk_ref, bv_ref, k_ref, v_ref, bias_ref, near_ref, start_ref, mix_ref, o_ref
):
    pool = k_ref.shape[0]
    keys = k_ref[:, 0].reshape(pool * BLK, HD)
    values = v_ref[:, 0].reshape(pool * BLK, HD)
    mix = mix_ref[...]
    contract = (((1,), (1,)), ((), ()))
    first_query = q_ref[0:BLK, :]
    query_index = lax.broadcasted_iota(jnp.int32, (BLK, BLK), 0)
    key_index = lax.broadcasted_iota(jnp.int32, (BLK, BLK), 1)
    allow_before = (key_index > query_index) & (start_ref[...] > 0.5)
    allow_local = key_index <= query_index
    score_before = lax.dot_general(
        first_query, bk_ref[0], contract, preferred_element_type=jnp.float32
    ) * (HD ** (-0.5))
    score_local = lax.dot_general(
        first_query, k0_ref[...], contract, preferred_element_type=jnp.float32
    ) * (HD ** (-0.5))
    near_peak = jnp.maximum(
        jnp.max(jnp.where(allow_before, score_before, NEG_FILL), axis=-1, keepdims=True),
        jnp.max(jnp.where(allow_local, score_local, NEG_FILL), axis=-1, keepdims=True),
    )
    weight_before = jnp.where(allow_before, jnp.exp(score_before - near_peak), 0.0)
    weight_local = jnp.where(allow_local, jnp.exp(score_local - near_peak), 0.0)
    near_total = jnp.sum(weight_before, axis=-1, keepdims=True) + jnp.sum(
        weight_local, axis=-1, keepdims=True
    )
    first_near = jnp.dot(
        (weight_before / near_total).astype(jnp.bfloat16), bv_ref[0],
        preferred_element_type=jnp.float32,
    ) + jnp.dot(
        (weight_local / near_total).astype(jnp.bfloat16), v0_ref[...],
        preferred_element_type=jnp.float32,
    )
    for block in range(q_ref.shape[0] // BLK):
        rows = slice(block * BLK, (block + 1) * BLK)
        scores = lax.dot_general(
            q_ref[rows, :], keys, contract, preferred_element_type=jnp.float32
        ) + bias_ref[block]
        peak = jnp.max(scores, axis=-1, keepdims=True)
        weights = jnp.exp((scores - peak) * (HD ** (-0.5)))
        scale = 1.0 / jnp.sum(weights, axis=-1, keepdims=True)
        far = jnp.dot(weights.astype(jnp.bfloat16), values, preferred_element_type=jnp.float32)
        near = first_near if block == 0 else near_ref[block - 1, 0]
        o_ref[rows, :] = (mix * (far * scale) + (1.0 - mix) * near).astype(o_ref.dtype)


def far_attention(projected, before, fetched, bias, later, start, mixing):
    rows = projected.shape[0]
    blocks = rows // BLK
    pool = fetched.shape[0]
    groups = fetched.shape[3] // HD
    return pl.pallas_call(
        far_kernel,
        grid=(groups,),
        in_specs=[
            pl.BlockSpec((rows, HD), lambda h: (0, h * 3)),
            pl.BlockSpec((BLK, HD), lambda h: (0, h * 3 + 1)),
            pl.BlockSpec((BLK, HD), lambda h: (0, h * 3 + 2)),
            pl.BlockSpec((1, BLK, HD), lambda h: (0, 0, h)),
            pl.BlockSpec((1, BLK, HD), lambda h: (1, 0, h)),
            pl.BlockSpec((pool, 1, BLK, HD), lambda h: (0, 0, 0, h)),
            pl.BlockSpec((pool, 1, BLK, HD), lambda h: (0, 1, 0, h)),
            pl.BlockSpec((blocks, 1, pool * BLK), lambda h: (0, 0, 0)),
            pl.BlockSpec((blocks - 1, 1, BLK, HD), lambda h: (0, h, 0, 0)),
            pl.BlockSpec((1, BLK), lambda h: (0, 0)),
            pl.BlockSpec((1, HD), lambda h: (0, h)),
        ],
        out_specs=pl.BlockSpec((rows, HD), lambda h: (0, h)),
        out_shape=jax.ShapeDtypeStruct((rows, groups * HD), jnp.bfloat16),
        cost_estimate=pl.CostEstimate(
            flops=groups * (blocks * pool + 2) * 4 * BLK * BLK * HD,
            transcendentals=groups * (blocks * pool + 2) * BLK * BLK,
            bytes_accessed=fetched.size * 2 + rows * groups * HD * 8,
        ),
    )(projected, projected, projected, before, before, fetched, fetched, bias, later, start, mixing)

def gather_tp(part):
    count = lax.axis_size("tp")
    me = lax.axis_index("tp")
    arrived = [part] + [
        lax.ppermute(part, "tp", [(t, (t + shift) % count) for t in range(count)])
        for shift in range(1, count)
    ]
    order = (me - jnp.arange(count)) % count
    return jnp.take(jnp.stack(arrived), order, axis=0, mode="clip").reshape(
        count * part.shape[0], part.shape[1]
    )

def local(tokens, input_weight, output_weight, gate_logit, memory, retrieved, block_home):
    holder_count = lax.axis_size("mem")
    share_rows = tokens.shape[0]
    local_rows = share_rows * lax.axis_size("tp")
    groups = output_weight.shape[0] // HD
    score_scale = HD ** (-0.5)
    projected = jnp.dot(
        gather_tp(tokens),
        input_weight,
        preferred_element_type=jnp.float32,
    )
    projected_flat = projected.astype(jnp.bfloat16)
    projected = projected_flat.reshape(local_rows, groups, 3, HD)
    queries = projected[:, :, 0]
    key_rows = projected[:, :, 1]
    value_rows = projected[:, :, 2]
    last_rows = jnp.stack([key_rows[-BLK:], value_rows[-BLK:]]).reshape(2, BLK, groups * HD)
    before = from_behind(last_rows, "mem", 1)
    blocks_here = local_rows // BLK
    query_blocks = queries.reshape(blocks_here, BLK, groups, HD)
    key_blocks = key_rows.reshape(blocks_here, BLK, groups, HD)
    value_blocks = value_rows.reshape(blocks_here, BLK, groups, HD)
    first_row = lax.axis_index("mem") * local_rows + jnp.arange(blocks_here) * BLK
    later = near_part(
        query_blocks[1:],
        jnp.concatenate([key_blocks[:-1], key_blocks[1:]], axis=1),
        jnp.concatenate([value_blocks[:-1], value_blocks[1:]], axis=1),
        first_row[1:] - BLK,
    )
    blocks_here = retrieved.shape[0]
    entries = blocks_here * TOPB
    local_blocks = memory.shape[1] // BLK
    flat_blocks = retrieved.reshape(entries)
    block_index = lax.broadcasted_iota(jnp.int32, (entries, block_home.shape[0]), 1)
    home_slot = jnp.sum(
        jnp.where(block_index == flat_blocks[:, None], block_home[None, :], 0), axis=1
    )
    holder = home_slot // local_blocks
    local_block = home_slot % local_blocks
    local_store = memory.reshape(2, local_blocks, BLK, groups * HD)
    entry_order = jnp.arange(entries)
    earlier = entry_order[None, :] < entry_order[:, None]
    same_owner = holder[:, None] == holder[None, :]
    same_block = home_slot[:, None] == home_slot[None, :]
    first = jnp.sum(same_block & earlier, axis=1) == 0
    first_entry = jnp.argmax(same_block, axis=1)
    before_first = entry_order[None, :] < first_entry[:, None]
    slot_of = jnp.sum(same_owner & before_first & first[None, :], axis=1)
    slot_index = lax.broadcasted_iota(jnp.int32, (holder_count, CAP, entries), 1)
    holder_index = lax.broadcasted_iota(jnp.int32, (holder_count, CAP, entries), 0)
    wanted_ids = jnp.max(
        jnp.where(
            (holder_index == holder[None, None, :]) & (slot_index == slot_of[None, None, :]),
            local_block[None, None, :],
            0,
        ),
        axis=2,
    )
    asked = lax.all_to_all(wanted_ids, "mem", split_axis=0, concat_axis=0, tiled=True).reshape(
        holder_count * CAP
    )
    chooser = (
        asked[:, None] == lax.broadcasted_iota(jnp.int32, (holder_count * CAP, local_blocks), 1)
    ).astype(jnp.bfloat16)
    picked = jnp.einsum(
        "sb,pbx->spx",
        chooser,
        local_store.reshape(2, local_blocks, BLK * groups * HD),
        preferred_element_type=jnp.float32,
    ).astype(jnp.bfloat16).reshape(holder_count * CAP, 2, BLK, groups * HD)
    fetched = lax.all_to_all(picked, "mem", split_axis=0, concat_axis=0, tiled=True)
    pool = holder_count * CAP
    row_of = entry_order // TOPB
    member = (
        jnp.zeros((blocks_here, pool), jnp.bool_).at[row_of, holder * CAP + slot_of].set(True)
    )
    bias = jnp.where(jnp.repeat(member, BLK, axis=1), 0.0, NEG_FILL).reshape(
        blocks_here, 1, pool * BLK
    )
    mixing = jnp.repeat(jax.nn.sigmoid(gate_logit), HD).reshape(1, groups * HD)
    attended = far_attention(
        projected_flat,
        before,
        fetched,
        bias,
        later,
        jnp.full((1, BLK), jnp.where(lax.axis_index("mem") > 0, 1.0, 0.0), jnp.float32),
        mixing,
    )
    partial = jnp.dot(attended, output_weight, preferred_element_type=jnp.float32)
    width = partial.shape[1] // 4
    return jnp.concatenate(
        [reduce_over_tp(partial[:, k * width:(k + 1) * width]) for k in range(4)], axis=1
    ).astype(jnp.bfloat16)


def reduce_over_tp(partial):
    count = lax.axis_size("tp")
    chips = count // 2
    share = partial.shape[0] // count
    me = lax.axis_index("tp")
    core = me % 2
    chip = me // 2
    split = partial.reshape(chips, 2, share, partial.shape[1])
    mine = lax.dynamic_index_in_dim(split, core, axis=1, keepdims=False)
    other = lax.dynamic_index_in_dim(split, 1 - core, axis=1, keepdims=False)
    arrived = lax.ppermute(
        other.astype(jnp.bfloat16), "tp", [(t, t ^ 1) for t in range(count)]
    )
    chip_sum = mine + arrived.astype(jnp.float32)
    total = lax.dynamic_index_in_dim(chip_sum, chip, axis=0, keepdims=False)
    for shift in range(1, chips):
        outgoing = lax.dynamic_index_in_dim(chip_sum, (chip + shift) % chips, axis=0, keepdims=False)
        pairs = [(t, ((t // 2 + shift) % chips) * 2 + t % 2) for t in range(count)]
        total = total + lax.ppermute(outgoing.astype(jnp.bfloat16), "tp", pairs).astype(jnp.float32)
    return total

def solution(mesh):
    placed = (
        P(("mem", "tp"), None),
        P(None, "tp"),
        P("tp", None),
        P("tp"),
        P(None, "mem", "tp"),
        P("mem", None),
        P(),
    )
    return jax.shard_map(
        local, mesh=mesh, in_specs=placed, out_specs=P(("mem", "tp"), None), check_vma=False
    )
```

```python
import jax
import jax.numpy as jnp
from jax import lax
from jax.sharding import PartitionSpec as P
from jax.experimental import pallas as pl
from jax.experimental.pallas import tpu as pltpu

HD = 128
BLK = 128
TOPB = 16
CAP = 2


NEG_FILL = -1e30


def from_behind(value, axis, steps):
    count = lax.axis_size(axis)
    initial, last = (max(0, -steps), min(count, count - steps))
    return lax.ppermute(value, axis, [(source, source + steps) for source in range(initial, last)])


def softmax_rows(scores, allowed):
    row_peak = jnp.max(jnp.where(allowed, scores, NEG_FILL), axis=-1, keepdims=True)
    weights = jnp.where(allowed, jnp.exp(scores - row_peak), 0.0)
    return (weights / jnp.sum(weights, axis=-1, keepdims=True)).astype(jnp.bfloat16)


def near_part(block_queries, window_keys, window_values, first_key):
    scores = (
        jnp.einsum(
            "nqgd,nkgd->ngqk", block_queries, window_keys, preferred_element_type=jnp.float32
        )
        * (HD ** (-0.5))
    )
    query_index = lax.broadcasted_iota(jnp.int32, (BLK, 2 * BLK), 0)
    key_index = lax.broadcasted_iota(jnp.int32, (BLK, 2 * BLK), 1)
    allowed = (
        (key_index > query_index)[None]
        & (key_index <= query_index + BLK)[None]
        & (key_index[None] + first_key[:, None, None] >= 0)
    )
    probs = softmax_rows(scores, allowed[:, None])
    return jnp.einsum(
        "ngqk,nkgd->ngqd", probs, window_values, preferred_element_type=jnp.float32
    )


def far_kernel(
    q_ref, k0_ref, v0_ref, bk_ref, bv_ref, k_ref, kb_ref, v_ref, vb_ref, bias_ref, near_ref, start_ref, mix_ref, o_ref
):
    span = k_ref.shape[0] * BLK
    keys = k_ref[:, 0].reshape(span, HD)
    values = v_ref[:, 0].reshape(span, HD)
    keys_b = kb_ref[:, 0].reshape(span, HD)
    values_b = vb_ref[:, 0].reshape(span, HD)
    mix = mix_ref[...]
    contract = (((1,), (1,)), ((), ()))
    first_query = q_ref[0:BLK, :]
    query_index = lax.broadcasted_iota(jnp.int32, (BLK, BLK), 0)
    key_index = lax.broadcasted_iota(jnp.int32, (BLK, BLK), 1)
    allow_before = (key_index > query_index) & (start_ref[...] > 0.5)
    allow_local = key_index <= query_index
    score_before = lax.dot_general(
        first_query, bk_ref[0], contract, preferred_element_type=jnp.float32
    ) * (HD ** (-0.5))
    score_local = lax.dot_general(
        first_query, k0_ref[...], contract, preferred_element_type=jnp.float32
    ) * (HD ** (-0.5))
    near_peak = jnp.maximum(
        jnp.max(jnp.where(allow_before, score_before, NEG_FILL), axis=-1, keepdims=True),
        jnp.max(jnp.where(allow_local, score_local, NEG_FILL), axis=-1, keepdims=True),
    )
    weight_before = jnp.where(allow_before, jnp.exp(score_before - near_peak), 0.0)
    weight_local = jnp.where(allow_local, jnp.exp(score_local - near_peak), 0.0)
    near_total = jnp.sum(weight_before, axis=-1, keepdims=True) + jnp.sum(
        weight_local, axis=-1, keepdims=True
    )
    first_near = jnp.dot(
        (weight_before / near_total).astype(jnp.bfloat16), bv_ref[0],
        preferred_element_type=jnp.float32,
    ) + jnp.dot(
        (weight_local / near_total).astype(jnp.bfloat16), v0_ref[...],
        preferred_element_type=jnp.float32,
    )
    for block in range(q_ref.shape[0] // BLK):
        rows = slice(block * BLK, (block + 1) * BLK)
        query = q_ref[rows, :]
        scores = lax.dot_general(
            query, keys, contract, preferred_element_type=jnp.float32
        ) + bias_ref[block, :, 0:span]
        scores_b = lax.dot_general(
            query, keys_b, contract, preferred_element_type=jnp.float32
        ) + bias_ref[block, :, span:2 * span]
        peak = jnp.maximum(
            jnp.max(scores, axis=-1, keepdims=True), jnp.max(scores_b, axis=-1, keepdims=True)
        )
        weights = jnp.exp((scores - peak) * (HD ** (-0.5)))
        weights_b = jnp.exp((scores_b - peak) * (HD ** (-0.5)))
        scale = 1.0 / (
            jnp.sum(weights, axis=-1, keepdims=True) + jnp.sum(weights_b, axis=-1, keepdims=True)
        )
        far = jnp.dot(
            weights.astype(jnp.bfloat16), values, preferred_element_type=jnp.float32
        ) + jnp.dot(weights_b.astype(jnp.bfloat16), values_b, preferred_element_type=jnp.float32)
        near = first_near if block == 0 else near_ref[block - 1, 0]
        o_ref[rows, :] = (mix * (far * scale) + (1.0 - mix) * near).astype(o_ref.dtype)


def far_attention(projected, before, fetched, fetched_b, bias, later, start, mixing):
    rows = projected.shape[0]
    blocks = rows // BLK
    pool = fetched.shape[0] * 2
    groups = fetched.shape[3] // HD
    return pl.pallas_call(
        far_kernel,
        grid=(groups,),
        in_specs=[
            pl.BlockSpec((rows, HD), lambda h: (0, h * 3)),
            pl.BlockSpec((BLK, HD), lambda h: (0, h * 3 + 1)),
            pl.BlockSpec((BLK, HD), lambda h: (0, h * 3 + 2)),
            pl.BlockSpec((1, BLK, HD), lambda h: (0, 0, h)),
            pl.BlockSpec((1, BLK, HD), lambda h: (1, 0, h)),
            pl.BlockSpec((pool // 2, 1, BLK, HD), lambda h: (0, 0, 0, h)),
            pl.BlockSpec((pool // 2, 1, BLK, HD), lambda h: (0, 0, 0, h)),
            pl.BlockSpec((pool // 2, 1, BLK, HD), lambda h: (0, 1, 0, h)),
            pl.BlockSpec((pool // 2, 1, BLK, HD), lambda h: (0, 1, 0, h)),
            pl.BlockSpec((blocks, 1, pool * BLK), lambda h: (0, 0, 0)),
            pl.BlockSpec((blocks - 1, 1, BLK, HD), lambda h: (0, h, 0, 0)),
            pl.BlockSpec((1, BLK), lambda h: (0, 0)),
            pl.BlockSpec((1, HD), lambda h: (0, h)),
        ],
        out_specs=pl.BlockSpec((rows, HD), lambda h: (0, h)),
        out_shape=jax.ShapeDtypeStruct((rows, groups * HD), jnp.bfloat16),
        cost_estimate=pl.CostEstimate(
            flops=groups * (blocks * pool + 2) * 4 * BLK * BLK * HD,
            transcendentals=groups * (blocks * pool + 2) * BLK * BLK,
            bytes_accessed=fetched.size * 4 + rows * groups * HD * 8,
        ),
    )(
        projected, projected, projected, before, before,
        fetched, fetched_b, fetched, fetched_b, bias, later, start, mixing,
    )

def gather_tp(part):
    count = lax.axis_size("tp")
    me = lax.axis_index("tp")
    arrived = [part] + [
        lax.ppermute(part, "tp", [(t, (t + shift) % count) for t in range(count)])
        for shift in range(1, count)
    ]
    order = (me - jnp.arange(count)) % count
    return jnp.take(jnp.stack(arrived), order, axis=0, mode="clip").reshape(
        count * part.shape[0], part.shape[1]
    )

def local(tokens, input_weight, output_weight, gate_logit, memory, retrieved, block_home):
    holder_count = lax.axis_size("mem")
    share_rows = tokens.shape[0]
    local_rows = share_rows * lax.axis_size("tp")
    groups = output_weight.shape[0] // HD
    score_scale = HD ** (-0.5)
    projected = jnp.dot(
        gather_tp(tokens),
        input_weight,
        preferred_element_type=jnp.float32,
    )
    projected_flat = projected.astype(jnp.bfloat16)
    projected = projected_flat.reshape(local_rows, groups, 3, HD)
    queries = projected[:, :, 0]
    key_rows = projected[:, :, 1]
    value_rows = projected[:, :, 2]
    last_rows = jnp.stack([key_rows[-BLK:], value_rows[-BLK:]]).reshape(2, BLK, groups * HD)
    before = from_behind(last_rows, "mem", 1)
    blocks_here = local_rows // BLK
    query_blocks = queries.reshape(blocks_here, BLK, groups, HD)
    key_blocks = key_rows.reshape(blocks_here, BLK, groups, HD)
    value_blocks = value_rows.reshape(blocks_here, BLK, groups, HD)
    first_row = lax.axis_index("mem") * local_rows + jnp.arange(blocks_here) * BLK
    later = near_part(
        query_blocks[1:],
        jnp.concatenate([key_blocks[:-1], key_blocks[1:]], axis=1),
        jnp.concatenate([value_blocks[:-1], value_blocks[1:]], axis=1),
        first_row[1:] - BLK,
    )
    blocks_here = retrieved.shape[0]
    entries = blocks_here * TOPB
    local_blocks = memory.shape[1] // BLK
    flat_blocks = retrieved.reshape(entries)
    block_index = lax.broadcasted_iota(jnp.int32, (entries, block_home.shape[0]), 1)
    home_slot = jnp.sum(
        jnp.where(block_index == flat_blocks[:, None], block_home[None, :], 0), axis=1
    )
    holder = home_slot // local_blocks
    local_block = home_slot % local_blocks
    local_store = memory.reshape(2, local_blocks, BLK, groups * HD)
    entry_order = jnp.arange(entries)
    earlier = entry_order[None, :] < entry_order[:, None]
    same_owner = holder[:, None] == holder[None, :]
    same_block = home_slot[:, None] == home_slot[None, :]
    first = jnp.sum(same_block & earlier, axis=1) == 0
    first_entry = jnp.argmax(same_block, axis=1)
    before_first = entry_order[None, :] < first_entry[:, None]
    slot_of = jnp.sum(same_owner & before_first & first[None, :], axis=1)
    slot_index = lax.broadcasted_iota(jnp.int32, (holder_count, CAP, entries), 1)
    holder_index = lax.broadcasted_iota(jnp.int32, (holder_count, CAP, entries), 0)
    wanted_ids = jnp.max(
        jnp.where(
            (holder_index == holder[None, None, :]) & (slot_index == slot_of[None, None, :]),
            local_block[None, None, :],
            0,
        ),
        axis=2,
    )
    asked = lax.all_to_all(wanted_ids, "mem", split_axis=0, concat_axis=0, tiled=True)
    halves = [
        lax.all_to_all(
            jnp.take(local_store, asked[:, part], axis=1, mode="clip").transpose(1, 0, 2, 3),
            "mem",
            split_axis=0,
            concat_axis=0,
            tiled=True,
        )
        for part in range(CAP)
    ]
    pool = holder_count * CAP
    row_of = entry_order // TOPB
    member = (
        jnp.zeros((blocks_here, pool), jnp.bool_).at[row_of, slot_of * holder_count + holder].set(True)
    )
    bias = jnp.where(jnp.repeat(member, BLK, axis=1), 0.0, NEG_FILL).reshape(
        blocks_here, 1, pool * BLK
    )
    mixing = jnp.repeat(jax.nn.sigmoid(gate_logit), HD).reshape(1, groups * HD)
    attended = far_attention(
        projected_flat,
        before,
        halves[0],
        halves[1],
        bias,
        later,
        jnp.full((1, BLK), jnp.where(lax.axis_index("mem") > 0, 1.0, 0.0), jnp.float32),
        mixing,
    )
    partial = jnp.dot(attended, output_weight, preferred_element_type=jnp.float32)
    width = partial.shape[1] // 4
    return jnp.concatenate(
        [reduce_over_tp(partial[:, k * width:(k + 1) * width]) for k in range(4)], axis=1
    ).astype(jnp.bfloat16)


def reduce_over_tp(partial):
    count = lax.axis_size("tp")
    chips = count // 2
    share = partial.shape[0] // count
    me = lax.axis_index("tp")
    core = me % 2
    chip = me // 2
    split = partial.reshape(chips, 2, share, partial.shape[1])
    mine = lax.dynamic_index_in_dim(split, core, axis=1, keepdims=False)
    other = lax.dynamic_index_in_dim(split, 1 - core, axis=1, keepdims=False)
    arrived = lax.ppermute(
        other.astype(jnp.bfloat16), "tp", [(t, t ^ 1) for t in range(count)]
    )
    chip_sum = mine + arrived.astype(jnp.float32)
    total = lax.dynamic_index_in_dim(chip_sum, chip, axis=0, keepdims=False)
    for shift in range(1, chips):
        outgoing = lax.dynamic_index_in_dim(chip_sum, (chip + shift) % chips, axis=0, keepdims=False)
        pairs = [(t, ((t // 2 + shift) % chips) * 2 + t % 2) for t in range(count)]
        total = total + lax.ppermute(outgoing.astype(jnp.bfloat16), "tp", pairs).astype(jnp.float32)
    return total

def solution(mesh):
    placed = (
        P(("mem", "tp"), None),
        P(None, "tp"),
        P("tp", None),
        P("tp"),
        P(None, "mem", "tp"),
        P("mem", None),
        P(),
    )
    return jax.shard_map(
        local, mesh=mesh, in_specs=placed, out_specs=P(("mem", "tp"), None), check_vma=False
    )
```

```python
import jax
import jax.numpy as jnp
from jax import lax
from jax.sharding import PartitionSpec as P
from jax.experimental import pallas as pl
from jax.experimental.pallas import tpu as pltpu

HD = 128
BLK = 128
TOPB = 16
CAP = 2


NEG_FILL = -1e30


def from_behind(value, axis, steps):
    count = lax.axis_size(axis)
    initial, last = (max(0, -steps), min(count, count - steps))
    return lax.ppermute(value, axis, [(source, source + steps) for source in range(initial, last)])


def softmax_rows(scores, allowed):
    row_peak = jnp.max(jnp.where(allowed, scores, NEG_FILL), axis=-1, keepdims=True)
    weights = jnp.where(allowed, jnp.exp(scores - row_peak), 0.0)
    return (weights / jnp.sum(weights, axis=-1, keepdims=True)).astype(jnp.bfloat16)


def near_part(block_queries, window_keys, window_values, first_key):
    scores = (
        jnp.einsum(
            "nqgd,nkgd->ngqk", block_queries, window_keys, preferred_element_type=jnp.float32
        )
        * (HD ** (-0.5))
    )
    query_index = lax.broadcasted_iota(jnp.int32, (BLK, 2 * BLK), 0)
    key_index = lax.broadcasted_iota(jnp.int32, (BLK, 2 * BLK), 1)
    allowed = (
        (key_index > query_index)[None]
        & (key_index <= query_index + BLK)[None]
        & (key_index[None] + first_key[:, None, None] >= 0)
    )
    probs = softmax_rows(scores, allowed[:, None])
    return jnp.einsum(
        "ngqk,nkgd->ngqd", probs, window_values, preferred_element_type=jnp.float32
    )


def far_kernel(
    q_ref, k0_ref, v0_ref, bk_ref, bv_ref, k_ref, v_ref, bias_ref, near_ref, start_ref, mix_ref, o_ref
):
    pool = k_ref.shape[0]
    keys = k_ref[:, 0].reshape(pool * BLK, HD)
    values = v_ref[:, 0].reshape(pool * BLK, HD)
    mix = mix_ref[...]
    contract = (((1,), (1,)), ((), ()))
    first_query = q_ref[0:BLK, :]
    query_index = lax.broadcasted_iota(jnp.int32, (BLK, BLK), 0)
    key_index = lax.broadcasted_iota(jnp.int32, (BLK, BLK), 1)
    allow_before = (key_index > query_index) & (start_ref[...] > 0.5)
    allow_local = key_index <= query_index
    score_before = lax.dot_general(
        first_query, bk_ref[0], contract, preferred_element_type=jnp.float32
    ) * (HD ** (-0.5))
    score_local = lax.dot_general(
        first_query, k0_ref[...], contract, preferred_element_type=jnp.float32
    ) * (HD ** (-0.5))
    near_peak = jnp.maximum(
        jnp.max(jnp.where(allow_before, score_before, NEG_FILL), axis=-1, keepdims=True),
        jnp.max(jnp.where(allow_local, score_local, NEG_FILL), axis=-1, keepdims=True),
    )
    weight_before = jnp.where(allow_before, jnp.exp(score_before - near_peak), 0.0)
    weight_local = jnp.where(allow_local, jnp.exp(score_local - near_peak), 0.0)
    near_total = jnp.sum(weight_before, axis=-1, keepdims=True) + jnp.sum(
        weight_local, axis=-1, keepdims=True
    )
    first_near = jnp.dot(
        (weight_before / near_total).astype(jnp.bfloat16), bv_ref[0],
        preferred_element_type=jnp.float32,
    ) + jnp.dot(
        (weight_local / near_total).astype(jnp.bfloat16), v0_ref[...],
        preferred_element_type=jnp.float32,
    )
    for block in range(q_ref.shape[0] // BLK):
        rows = slice(block * BLK, (block + 1) * BLK)
        scores = lax.dot_general(
            q_ref[rows, :], keys, contract, preferred_element_type=jnp.float32
        ) + bias_ref[block]
        peak = jnp.max(scores, axis=-1, keepdims=True)
        weights = jnp.exp((scores - peak) * (HD ** (-0.5)))
        scale = 1.0 / jnp.sum(weights, axis=-1, keepdims=True)
        far = jnp.dot(weights.astype(jnp.bfloat16), values, preferred_element_type=jnp.float32)
        near = first_near if block == 0 else near_ref[block - 1, 0]
        o_ref[rows, :] = (mix * (far * scale) + (1.0 - mix) * near).astype(o_ref.dtype)


def far_attention(projected, before, fetched, bias, later, start, mixing):
    rows = projected.shape[0]
    blocks = rows // BLK
    pool = fetched.shape[0]
    groups = fetched.shape[3] // HD
    return pl.pallas_call(
        far_kernel,
        grid=(groups,),
        in_specs=[
            pl.BlockSpec((rows, HD), lambda h: (0, h * 3)),
            pl.BlockSpec((BLK, HD), lambda h: (0, h * 3 + 1)),
            pl.BlockSpec((BLK, HD), lambda h: (0, h * 3 + 2)),
            pl.BlockSpec((1, BLK, HD), lambda h: (0, 0, h)),
            pl.BlockSpec((1, BLK, HD), lambda h: (1, 0, h)),
            pl.BlockSpec((pool, 1, BLK, HD), lambda h: (0, 0, 0, h)),
            pl.BlockSpec((pool, 1, BLK, HD), lambda h: (0, 1, 0, h)),
            pl.BlockSpec((blocks, 1, pool * BLK), lambda h: (0, 0, 0)),
            pl.BlockSpec((blocks - 1, 1, BLK, HD), lambda h: (0, h, 0, 0)),
            pl.BlockSpec((1, BLK), lambda h: (0, 0)),
            pl.BlockSpec((1, HD), lambda h: (0, h)),
        ],
        out_specs=pl.BlockSpec((rows, HD), lambda h: (0, h)),
        out_shape=jax.ShapeDtypeStruct((rows, groups * HD), jnp.bfloat16),
        cost_estimate=pl.CostEstimate(
            flops=groups * (blocks * pool + 2) * 4 * BLK * BLK * HD,
            transcendentals=groups * (blocks * pool + 2) * BLK * BLK,
            bytes_accessed=fetched.size * 2 + rows * groups * HD * 8,
        ),
    )(projected, projected, projected, before, before, fetched, fetched, bias, later, start, mixing)

def gather_tp(part):
    count = lax.axis_size("tp")
    me = lax.axis_index("tp")
    arrived = [part] + [
        lax.ppermute(part, "tp", [(t, (t + shift) % count) for t in range(count)])
        for shift in range(1, count)
    ]
    order = (me - jnp.arange(count)) % count
    return jnp.take(jnp.stack(arrived), order, axis=0, mode="clip").reshape(
        count * part.shape[0], part.shape[1]
    )

def local(tokens, input_weight, output_weight, gate_logit, memory, retrieved, block_home):
    holder_count = lax.axis_size("mem")
    share_rows = tokens.shape[0]
    local_rows = share_rows * lax.axis_size("tp")
    groups = output_weight.shape[0] // HD
    score_scale = HD ** (-0.5)
    projected = jnp.dot(
        gather_tp(tokens),
        input_weight,
        preferred_element_type=jnp.float32,
    )
    projected_flat = projected.astype(jnp.bfloat16)
    projected = projected_flat.reshape(local_rows, groups, 3, HD)
    queries = projected[:, :, 0]
    key_rows = projected[:, :, 1]
    value_rows = projected[:, :, 2]
    last_rows = jnp.stack([key_rows[-BLK:], value_rows[-BLK:]]).reshape(2, BLK, groups * HD)
    before = from_behind(last_rows, "mem", 1)
    blocks_here = local_rows // BLK
    query_blocks = queries.reshape(blocks_here, BLK, groups, HD)
    key_blocks = key_rows.reshape(blocks_here, BLK, groups, HD)
    value_blocks = value_rows.reshape(blocks_here, BLK, groups, HD)
    first_row = lax.axis_index("mem") * local_rows + jnp.arange(blocks_here) * BLK
    later = near_part(
        query_blocks[1:],
        jnp.concatenate([key_blocks[:-1], key_blocks[1:]], axis=1),
        jnp.concatenate([value_blocks[:-1], value_blocks[1:]], axis=1),
        first_row[1:] - BLK,
    )
    blocks_here = retrieved.shape[0]
    entries = blocks_here * TOPB
    local_blocks = memory.shape[1] // BLK
    flat_blocks = retrieved.reshape(entries)
    block_index = lax.broadcasted_iota(jnp.int32, (entries, block_home.shape[0]), 1)
    home_slot = jnp.sum(
        jnp.where(block_index == flat_blocks[:, None], block_home[None, :], 0), axis=1
    )
    holder = home_slot // local_blocks
    local_block = home_slot % local_blocks
    local_store = memory.reshape(2, local_blocks, BLK, groups * HD)
    entry_order = jnp.arange(entries)
    earlier = entry_order[None, :] < entry_order[:, None]
    same_owner = holder[:, None] == holder[None, :]
    same_block = home_slot[:, None] == home_slot[None, :]
    first = jnp.sum(same_block & earlier, axis=1) == 0
    first_entry = jnp.argmax(same_block, axis=1)
    before_first = entry_order[None, :] < first_entry[:, None]
    slot_of = jnp.sum(same_owner & before_first & first[None, :], axis=1)
    slot_index = lax.broadcasted_iota(jnp.int32, (holder_count, CAP, entries), 1)
    holder_index = lax.broadcasted_iota(jnp.int32, (holder_count, CAP, entries), 0)
    wanted_ids = jnp.max(
        jnp.where(
            (holder_index == holder[None, None, :]) & (slot_index == slot_of[None, None, :]),
            local_block[None, None, :],
            0,
        ),
        axis=2,
    )
    picked = jnp.take(
        local_store,
        lax.all_to_all(wanted_ids, "mem", split_axis=0, concat_axis=0, tiled=True).reshape(
            holder_count * CAP
        ),
        axis=1,
        mode="clip",
    ).transpose(1, 0, 2, 3)
    fetched = lax.all_to_all(picked, "mem", split_axis=0, concat_axis=0, tiled=True)
    pool = holder_count * CAP
    row_of = entry_order // TOPB
    member = (
        jnp.zeros((blocks_here, pool), jnp.bool_).at[row_of, holder * CAP + slot_of].set(True)
    )
    bias = jnp.where(jnp.repeat(member, BLK, axis=1), 0.0, NEG_FILL).reshape(
        blocks_here, 1, pool * BLK
    )
    mixing = jnp.repeat(jax.nn.sigmoid(gate_logit), HD).reshape(1, groups * HD)
    attended = far_attention(
        projected_flat,
        before,
        fetched,
        bias,
        later,
        jnp.full((1, BLK), jnp.where(lax.axis_index("mem") > 0, 1.0, 0.0), jnp.float32),
        mixing,
    )
    width = output_weight.shape[1] // 4
    return jnp.concatenate(
        [
            reduce_over_tp(
                jnp.dot(
                    attended,
                    output_weight[:, k * width:(k + 1) * width],
                    preferred_element_type=jnp.float32,
                )
            )
            for k in range(4)
        ],
        axis=1,
    ).astype(jnp.bfloat16)


def reduce_over_tp(partial):
    count = lax.axis_size("tp")
    chips = count // 2
    share = partial.shape[0] // count
    me = lax.axis_index("tp")
    core = me % 2
    chip = me // 2
    split = partial.reshape(chips, 2, share, partial.shape[1])
    mine = lax.dynamic_index_in_dim(split, core, axis=1, keepdims=False)
    other = lax.dynamic_index_in_dim(split, 1 - core, axis=1, keepdims=False)
    arrived = lax.ppermute(
        other.astype(jnp.bfloat16), "tp", [(t, t ^ 1) for t in range(count)]
    )
    chip_sum = mine + arrived.astype(jnp.float32)
    total = lax.dynamic_index_in_dim(chip_sum, chip, axis=0, keepdims=False)
    for shift in range(1, chips):
        outgoing = lax.dynamic_index_in_dim(chip_sum, (chip + shift) % chips, axis=0, keepdims=False)
        pairs = [(t, ((t // 2 + shift) % chips) * 2 + t % 2) for t in range(count)]
        total = total + lax.ppermute(outgoing.astype(jnp.bfloat16), "tp", pairs).astype(jnp.float32)
    return total

def solution(mesh):
    placed = (
        P(("mem", "tp"), None),
        P(None, "tp"),
        P("tp", None),
        P("tp"),
        P(None, "mem", "tp"),
        P("mem", None),
        P(),
    )
    return jax.shard_map(
        local, mesh=mesh, in_specs=placed, out_specs=P(("mem", "tp"), None), check_vma=False
    )
```

```python
import jax
import jax.numpy as jnp
from jax import lax
from jax.sharding import PartitionSpec as P
from jax.experimental import pallas as pl
from jax.experimental.pallas import tpu as pltpu

HD = 128
BLK = 128
TOPB = 16
CAP = 2


NEG_FILL = -1e30


def from_behind(value, axis, steps):
    count = lax.axis_size(axis)
    initial, last = (max(0, -steps), min(count, count - steps))
    return lax.ppermute(value, axis, [(source, source + steps) for source in range(initial, last)])


def softmax_rows(scores, allowed):
    row_peak = jnp.max(jnp.where(allowed, scores, NEG_FILL), axis=-1, keepdims=True)
    weights = jnp.where(allowed, jnp.exp(scores - row_peak), 0.0)
    return (weights / jnp.sum(weights, axis=-1, keepdims=True)).astype(jnp.bfloat16)


def near_part(block_queries, window_keys, window_values, first_key):
    scores = (
        jnp.einsum(
            "nqgd,nkgd->ngqk", block_queries, window_keys, preferred_element_type=jnp.float32
        )
        * (HD ** (-0.5))
    )
    query_index = lax.broadcasted_iota(jnp.int32, (BLK, 2 * BLK), 0)
    key_index = lax.broadcasted_iota(jnp.int32, (BLK, 2 * BLK), 1)
    allowed = (
        (key_index > query_index)[None]
        & (key_index <= query_index + BLK)[None]
        & (key_index[None] + first_key[:, None, None] >= 0)
    )
    probs = softmax_rows(scores, allowed[:, None])
    return jnp.einsum(
        "ngqk,nkgd->ngqd", probs, window_values, preferred_element_type=jnp.float32
    )


def far_kernel(
    q_ref, k0_ref, v0_ref, bk_ref, bv_ref, k_ref, v_ref, bias_ref, near_ref, start_ref, mix_ref, o_ref
):
    pool = k_ref.shape[0]
    keys = k_ref[:, 0].reshape(pool * BLK, HD)
    values = v_ref[:, 0].reshape(pool * BLK, HD)
    mix = mix_ref[...]
    contract = (((1,), (1,)), ((), ()))
    first_query = q_ref[0:BLK, :]
    query_index = lax.broadcasted_iota(jnp.int32, (BLK, BLK), 0)
    key_index = lax.broadcasted_iota(jnp.int32, (BLK, BLK), 1)
    allow_before = (key_index > query_index) & (start_ref[...] > 0.5)
    allow_local = key_index <= query_index
    score_before = lax.dot_general(
        first_query, bk_ref[0], contract, preferred_element_type=jnp.float32
    ) * (HD ** (-0.5))
    score_local = lax.dot_general(
        first_query, k0_ref[...], contract, preferred_element_type=jnp.float32
    ) * (HD ** (-0.5))
    near_peak = jnp.maximum(
        jnp.max(jnp.where(allow_before, score_before, NEG_FILL), axis=-1, keepdims=True),
        jnp.max(jnp.where(allow_local, score_local, NEG_FILL), axis=-1, keepdims=True),
    )
    weight_before = jnp.where(allow_before, jnp.exp(score_before - near_peak), 0.0)
    weight_local = jnp.where(allow_local, jnp.exp(score_local - near_peak), 0.0)
    near_total = jnp.sum(weight_before, axis=-1, keepdims=True) + jnp.sum(
        weight_local, axis=-1, keepdims=True
    )
    first_near = jnp.dot(
        (weight_before / near_total).astype(jnp.bfloat16), bv_ref[0],
        preferred_element_type=jnp.float32,
    ) + jnp.dot(
        (weight_local / near_total).astype(jnp.bfloat16), v0_ref[...],
        preferred_element_type=jnp.float32,
    )
    for block in range(q_ref.shape[0] // BLK):
        rows = slice(block * BLK, (block + 1) * BLK)
        scores = lax.dot_general(
            q_ref[rows, :], keys, contract, preferred_element_type=jnp.float32
        ) + bias_ref[block]
        peak = jnp.max(scores, axis=-1, keepdims=True)
        weights = jnp.exp((scores - peak) * (HD ** (-0.5)))
        scale = 1.0 / jnp.sum(weights, axis=-1, keepdims=True)
        far = jnp.dot(weights.astype(jnp.bfloat16), values, preferred_element_type=jnp.float32)
        near = first_near if block == 0 else near_ref[block - 1, 0]
        o_ref[rows, :] = (mix * (far * scale) + (1.0 - mix) * near).astype(o_ref.dtype)


def far_attention(projected, before, fetched, bias, later, start, mixing):
    rows = projected.shape[0]
    blocks = rows // BLK
    pool = fetched.shape[0]
    groups = fetched.shape[3] // HD
    return pl.pallas_call(
        far_kernel,
        grid=(groups,),
        in_specs=[
            pl.BlockSpec((rows, HD), lambda h: (0, h * 3)),
            pl.BlockSpec((BLK, HD), lambda h: (0, h * 3 + 1)),
            pl.BlockSpec((BLK, HD), lambda h: (0, h * 3 + 2)),
            pl.BlockSpec((1, BLK, HD), lambda h: (0, 0, h)),
            pl.BlockSpec((1, BLK, HD), lambda h: (1, 0, h)),
            pl.BlockSpec((pool, 1, BLK, HD), lambda h: (0, 0, 0, h)),
            pl.BlockSpec((pool, 1, BLK, HD), lambda h: (0, 1, 0, h)),
            pl.BlockSpec((blocks, 1, pool * BLK), lambda h: (0, 0, 0)),
            pl.BlockSpec((blocks - 1, 1, BLK, HD), lambda h: (0, h, 0, 0)),
            pl.BlockSpec((1, BLK), lambda h: (0, 0)),
            pl.BlockSpec((1, HD), lambda h: (0, h)),
        ],
        out_specs=pl.BlockSpec((rows, HD), lambda h: (0, h)),
        out_shape=jax.ShapeDtypeStruct((rows, groups * HD), jnp.bfloat16),
        cost_estimate=pl.CostEstimate(
            flops=groups * (blocks * pool + 2) * 4 * BLK * BLK * HD,
            transcendentals=groups * (blocks * pool + 2) * BLK * BLK,
            bytes_accessed=fetched.size * 2 + rows * groups * HD * 8,
        ),
    )(projected, projected, projected, before, before, fetched, fetched, bias, later, start, mixing)

def gather_tp(part):
    count = lax.axis_size("tp")
    me = lax.axis_index("tp")
    arrived = [part] + [
        lax.ppermute(part, "tp", [(t, (t + shift) % count) for t in range(count)])
        for shift in range(1, count)
    ]
    order = (me - jnp.arange(count)) % count
    return jnp.take(jnp.stack(arrived), order, axis=0, mode="clip").reshape(
        count * part.shape[0], part.shape[1]
    )

def local(tokens, input_weight, output_weight, gate_logit, memory, retrieved, block_home):
    holder_count = lax.axis_size("mem")
    share_rows = tokens.shape[0]
    local_rows = share_rows * lax.axis_size("tp")
    groups = output_weight.shape[0] // HD
    score_scale = HD ** (-0.5)
    projected = jnp.dot(
        gather_tp(tokens),
        input_weight,
        preferred_element_type=jnp.float32,
    )
    projected_flat = projected.astype(jnp.bfloat16)
    projected = projected_flat.reshape(local_rows, groups, 3, HD)
    queries = projected[:, :, 0]
    key_rows = projected[:, :, 1]
    value_rows = projected[:, :, 2]
    last_rows = jnp.stack([key_rows[-BLK:], value_rows[-BLK:]]).reshape(2, BLK, groups * HD)
    before = from_behind(last_rows, "mem", 1)
    blocks_here = local_rows // BLK
    query_blocks = queries.reshape(blocks_here, BLK, groups, HD)
    key_blocks = key_rows.reshape(blocks_here, BLK, groups, HD)
    value_blocks = value_rows.reshape(blocks_here, BLK, groups, HD)
    first_row = lax.axis_index("mem") * local_rows + jnp.arange(blocks_here) * BLK
    later = near_part(
        query_blocks[1:],
        jnp.concatenate([key_blocks[:-1], key_blocks[1:]], axis=1),
        jnp.concatenate([value_blocks[:-1], value_blocks[1:]], axis=1),
        first_row[1:] - BLK,
    )
    blocks_here = retrieved.shape[0]
    entries = blocks_here * TOPB
    local_blocks = memory.shape[1] // BLK
    flat_blocks = retrieved.reshape(entries)
    block_index = lax.broadcasted_iota(jnp.int32, (entries, block_home.shape[0]), 1)
    home_slot = jnp.sum(
        jnp.where(block_index == flat_blocks[:, None], block_home[None, :], 0), axis=1
    )
    holder = home_slot // local_blocks
    local_block = home_slot % local_blocks
    local_store = memory.reshape(2, local_blocks, BLK, groups * HD)
    entry_order = jnp.arange(entries)
    earlier = entry_order[None, :] < entry_order[:, None]
    same_owner = holder[:, None] == holder[None, :]
    same_block = home_slot[:, None] == home_slot[None, :]
    first = jnp.sum(same_block & earlier, axis=1) == 0
    first_entry = jnp.argmax(same_block, axis=1)
    before_first = entry_order[None, :] < first_entry[:, None]
    slot_of = jnp.sum(same_owner & before_first & first[None, :], axis=1)
    slot_index = lax.broadcasted_iota(jnp.int32, (holder_count, CAP, entries), 1)
    holder_index = lax.broadcasted_iota(jnp.int32, (holder_count, CAP, entries), 0)
    wanted_ids = jnp.max(
        jnp.where(
            (holder_index == holder[None, None, :]) & (slot_index == slot_of[None, None, :]),
            local_block[None, None, :],
            0,
        ),
        axis=2,
    )
    asked = lax.all_to_all(wanted_ids, "mem", split_axis=0, concat_axis=0, tiled=True).reshape(
        holder_count * CAP
    )
    rows_wanted = jnp.stack([asked, asked + local_blocks], axis=1).reshape(holder_count * CAP * 2)
    picked = jnp.take(
        memory.reshape(2 * local_blocks, BLK, groups * HD), rows_wanted, axis=0, mode="clip"
    ).reshape(holder_count * CAP, 2, BLK, groups * HD)
    fetched = lax.all_to_all(picked, "mem", split_axis=0, concat_axis=0, tiled=True)
    pool = holder_count * CAP
    row_of = entry_order // TOPB
    member = (
        jnp.zeros((blocks_here, pool), jnp.bool_).at[row_of, holder * CAP + slot_of].set(True)
    )
    bias = jnp.where(jnp.repeat(member, BLK, axis=1), 0.0, NEG_FILL).reshape(
        blocks_here, 1, pool * BLK
    )
    mixing = jnp.repeat(jax.nn.sigmoid(gate_logit), HD).reshape(1, groups * HD)
    attended = far_attention(
        projected_flat,
        before,
        fetched,
        bias,
        later,
        jnp.full((1, BLK), jnp.where(lax.axis_index("mem") > 0, 1.0, 0.0), jnp.float32),
        mixing,
    )
    partial = jnp.dot(attended, output_weight, preferred_element_type=jnp.float32)
    width = partial.shape[1] // 4
    return jnp.concatenate(
        [reduce_over_tp(partial[:, k * width:(k + 1) * width]) for k in range(4)], axis=1
    ).astype(jnp.bfloat16)


def reduce_over_tp(partial):
    count = lax.axis_size("tp")
    chips = count // 2
    share = partial.shape[0] // count
    me = lax.axis_index("tp")
    core = me % 2
    chip = me // 2
    split = partial.reshape(chips, 2, share, partial.shape[1])
    mine = lax.dynamic_index_in_dim(split, core, axis=1, keepdims=False)
    other = lax.dynamic_index_in_dim(split, 1 - core, axis=1, keepdims=False)
    arrived = lax.ppermute(
        other.astype(jnp.bfloat16), "tp", [(t, t ^ 1) for t in range(count)]
    )
    chip_sum = mine + arrived.astype(jnp.float32)
    total = lax.dynamic_index_in_dim(chip_sum, chip, axis=0, keepdims=False)
    for shift in range(1, chips):
        outgoing = lax.dynamic_index_in_dim(chip_sum, (chip + shift) % chips, axis=0, keepdims=False)
        pairs = [(t, ((t // 2 + shift) % chips) * 2 + t % 2) for t in range(count)]
        total = total + lax.ppermute(outgoing.astype(jnp.bfloat16), "tp", pairs).astype(jnp.float32)
    return total

def solution(mesh):
    placed = (
        P(("mem", "tp"), None),
        P(None, "tp"),
        P("tp", None),
        P("tp"),
        P(None, "mem", "tp"),
        P("mem", None),
        P(),
    )
    return jax.shard_map(
        local, mesh=mesh, in_specs=placed, out_specs=P(("mem", "tp"), None), check_vma=False
    )
```

```python
import jax
import jax.numpy as jnp
from jax import lax
from jax.sharding import PartitionSpec as P
from jax.experimental import pallas as pl
from jax.experimental.pallas import tpu as pltpu

HD = 128
BLK = 128
TOPB = 16
CAP = 2


NEG_FILL = -1e30


def from_behind(value, axis, steps):
    count = lax.axis_size(axis)
    initial, last = (max(0, -steps), min(count, count - steps))
    return lax.ppermute(value, axis, [(source, source + steps) for source in range(initial, last)])


def softmax_rows(scores, allowed):
    row_peak = jnp.max(jnp.where(allowed, scores, NEG_FILL), axis=-1, keepdims=True)
    weights = jnp.where(allowed, jnp.exp(scores - row_peak), 0.0)
    return (weights / jnp.sum(weights, axis=-1, keepdims=True)).astype(jnp.bfloat16)


def near_part(block_queries, window_keys, window_values, first_key):
    scores = (
        jnp.einsum(
            "nqgd,nkgd->ngqk", block_queries, window_keys, preferred_element_type=jnp.float32
        )
        * (HD ** (-0.5))
    )
    query_index = lax.broadcasted_iota(jnp.int32, (BLK, 2 * BLK), 0)
    key_index = lax.broadcasted_iota(jnp.int32, (BLK, 2 * BLK), 1)
    allowed = (
        (key_index > query_index)[None]
        & (key_index <= query_index + BLK)[None]
        & (key_index[None] + first_key[:, None, None] >= 0)
    )
    probs = softmax_rows(scores, allowed[:, None])
    return jnp.einsum(
        "ngqk,nkgd->ngqd", probs, window_values, preferred_element_type=jnp.float32
    )


def far_kernel(
    q_ref, k0_ref, v0_ref, bk_ref, bv_ref, k_ref, v_ref, bias_ref, near_ref, start_ref, mix_ref, o_ref
):
    pool = k_ref.shape[0]
    keys = k_ref[:, 0].reshape(pool * BLK, HD)
    values = v_ref[:, 0].reshape(pool * BLK, HD)
    mix = mix_ref[...]
    contract = (((1,), (1,)), ((), ()))
    first_query = q_ref[0:BLK, :]
    query_index = lax.broadcasted_iota(jnp.int32, (BLK, BLK), 0)
    key_index = lax.broadcasted_iota(jnp.int32, (BLK, BLK), 1)
    allow_before = (key_index > query_index) & (start_ref[...] > 0.5)
    allow_local = key_index <= query_index
    score_before = lax.dot_general(
        first_query, bk_ref[0], contract, preferred_element_type=jnp.float32
    ) * (HD ** (-0.5))
    score_local = lax.dot_general(
        first_query, k0_ref[...], contract, preferred_element_type=jnp.float32
    ) * (HD ** (-0.5))
    near_peak = jnp.maximum(
        jnp.max(jnp.where(allow_before, score_before, NEG_FILL), axis=-1, keepdims=True),
        jnp.max(jnp.where(allow_local, score_local, NEG_FILL), axis=-1, keepdims=True),
    )
    weight_before = jnp.where(allow_before, jnp.exp(score_before - near_peak), 0.0)
    weight_local = jnp.where(allow_local, jnp.exp(score_local - near_peak), 0.0)
    near_total = jnp.sum(weight_before, axis=-1, keepdims=True) + jnp.sum(
        weight_local, axis=-1, keepdims=True
    )
    first_near = jnp.dot(
        (weight_before / near_total).astype(jnp.bfloat16), bv_ref[0],
        preferred_element_type=jnp.float32,
    ) + jnp.dot(
        (weight_local / near_total).astype(jnp.bfloat16), v0_ref[...],
        preferred_element_type=jnp.float32,
    )
    for block in range(q_ref.shape[0] // BLK):
        rows = slice(block * BLK, (block + 1) * BLK)
        scores = lax.dot_general(
            q_ref[rows, :], keys, contract, preferred_element_type=jnp.float32
        ) + bias_ref[block]
        peak = jnp.max(scores, axis=-1, keepdims=True)
        weights = jnp.exp((scores - peak) * (HD ** (-0.5)))
        scale = 1.0 / jnp.sum(weights, axis=-1, keepdims=True)
        far = jnp.dot(weights.astype(jnp.bfloat16), values, preferred_element_type=jnp.float32)
        near = first_near if block == 0 else near_ref[block - 1, 0]
        o_ref[rows, :] = (mix * (far * scale) + (1.0 - mix) * near).astype(o_ref.dtype)


def far_attention(projected, before, fetched, bias, later, start, mixing):
    rows = projected.shape[0]
    blocks = rows // BLK
    pool = fetched.shape[0]
    groups = fetched.shape[3] // HD
    return pl.pallas_call(
        far_kernel,
        grid=(groups,),
        in_specs=[
            pl.BlockSpec((rows, HD), lambda h: (0, h * 3)),
            pl.BlockSpec((BLK, HD), lambda h: (0, h * 3 + 1)),
            pl.BlockSpec((BLK, HD), lambda h: (0, h * 3 + 2)),
            pl.BlockSpec((1, BLK, HD), lambda h: (0, 0, h)),
            pl.BlockSpec((1, BLK, HD), lambda h: (1, 0, h)),
            pl.BlockSpec((pool, 1, BLK, HD), lambda h: (0, 0, 0, h)),
            pl.BlockSpec((pool, 1, BLK, HD), lambda h: (0, 1, 0, h)),
            pl.BlockSpec((blocks, 1, pool * BLK), lambda h: (0, 0, 0)),
            pl.BlockSpec((blocks - 1, 1, BLK, HD), lambda h: (0, h, 0, 0)),
            pl.BlockSpec((1, BLK), lambda h: (0, 0)),
            pl.BlockSpec((1, HD), lambda h: (0, h)),
        ],
        out_specs=pl.BlockSpec((rows, HD), lambda h: (0, h)),
        out_shape=jax.ShapeDtypeStruct((rows, groups * HD), jnp.bfloat16),
        cost_estimate=pl.CostEstimate(
            flops=groups * (blocks * pool + 2) * 4 * BLK * BLK * HD,
            transcendentals=groups * (blocks * pool + 2) * BLK * BLK,
            bytes_accessed=fetched.size * 2 + rows * groups * HD * 8,
        ),
    )(projected, projected, projected, before, before, fetched, fetched, bias, later, start, mixing)

def pick_kernel(ids_ref, mem_ref, out_ref, sems):
    copies = []
    for slot in range(out_ref.shape[0]):
        for part in range(2):
            copy = pltpu.make_async_copy(
                mem_ref.at[part, pl.ds(ids_ref[slot] * BLK, BLK)],
                out_ref.at[slot, part],
                sems.at[slot, part],
            )
            copy.start()
            copies.append(copy)
    for copy in copies:
        copy.wait()


def pick_blocks(ids, memory):
    count = ids.shape[0]
    return pl.pallas_call(
        pick_kernel,
        grid_spec=pltpu.PrefetchScalarGridSpec(
            num_scalar_prefetch=1,
            grid=(1,),
            in_specs=[pl.BlockSpec(memory_space=pl.ANY)],
            out_specs=pl.BlockSpec(memory_space=pl.ANY),
            scratch_shapes=[pltpu.SemaphoreType.DMA((count, 2))],
        ),
        out_shape=jax.ShapeDtypeStruct((count, 2, BLK, memory.shape[2]), memory.dtype),
    )(ids, memory)


def gather_tp(part):
    count = lax.axis_size("tp")
    me = lax.axis_index("tp")
    arrived = [part] + [
        lax.ppermute(part, "tp", [(t, (t + shift) % count) for t in range(count)])
        for shift in range(1, count)
    ]
    order = (me - jnp.arange(count)) % count
    return jnp.take(jnp.stack(arrived), order, axis=0, mode="clip").reshape(
        count * part.shape[0], part.shape[1]
    )

def local(tokens, input_weight, output_weight, gate_logit, memory, retrieved, block_home):
    holder_count = lax.axis_size("mem")
    share_rows = tokens.shape[0]
    local_rows = share_rows * lax.axis_size("tp")
    groups = output_weight.shape[0] // HD
    score_scale = HD ** (-0.5)
    projected = jnp.dot(
        gather_tp(tokens),
        input_weight,
        preferred_element_type=jnp.float32,
    )
    projected_flat = projected.astype(jnp.bfloat16)
    projected = projected_flat.reshape(local_rows, groups, 3, HD)
    queries = projected[:, :, 0]
    key_rows = projected[:, :, 1]
    value_rows = projected[:, :, 2]
    last_rows = jnp.stack([key_rows[-BLK:], value_rows[-BLK:]]).reshape(2, BLK, groups * HD)
    before = from_behind(last_rows, "mem", 1)
    blocks_here = local_rows // BLK
    query_blocks = queries.reshape(blocks_here, BLK, groups, HD)
    key_blocks = key_rows.reshape(blocks_here, BLK, groups, HD)
    value_blocks = value_rows.reshape(blocks_here, BLK, groups, HD)
    first_row = lax.axis_index("mem") * local_rows + jnp.arange(blocks_here) * BLK
    later = near_part(
        query_blocks[1:],
        jnp.concatenate([key_blocks[:-1], key_blocks[1:]], axis=1),
        jnp.concatenate([value_blocks[:-1], value_blocks[1:]], axis=1),
        first_row[1:] - BLK,
    )
    blocks_here = retrieved.shape[0]
    entries = blocks_here * TOPB
    local_blocks = memory.shape[1] // BLK
    flat_blocks = retrieved.reshape(entries)
    block_index = lax.broadcasted_iota(jnp.int32, (entries, block_home.shape[0]), 1)
    home_slot = jnp.sum(
        jnp.where(block_index == flat_blocks[:, None], block_home[None, :], 0), axis=1
    )
    holder = home_slot // local_blocks
    local_block = home_slot % local_blocks
    local_store = memory.reshape(2, local_blocks, BLK, groups * HD)
    entry_order = jnp.arange(entries)
    earlier = entry_order[None, :] < entry_order[:, None]
    same_owner = holder[:, None] == holder[None, :]
    same_block = home_slot[:, None] == home_slot[None, :]
    first = jnp.sum(same_block & earlier, axis=1) == 0
    first_entry = jnp.argmax(same_block, axis=1)
    before_first = entry_order[None, :] < first_entry[:, None]
    slot_of = jnp.sum(same_owner & before_first & first[None, :], axis=1)
    slot_index = lax.broadcasted_iota(jnp.int32, (holder_count, CAP, entries), 1)
    holder_index = lax.broadcasted_iota(jnp.int32, (holder_count, CAP, entries), 0)
    wanted_ids = jnp.max(
        jnp.where(
            (holder_index == holder[None, None, :]) & (slot_index == slot_of[None, None, :]),
            local_block[None, None, :],
            0,
        ),
        axis=2,
    )
    asked = lax.all_to_all(wanted_ids, "mem", split_axis=0, concat_axis=0, tiled=True).reshape(
        holder_count * CAP
    )
    picked = pick_blocks(jnp.clip(asked, 0, local_blocks - 1), memory)
    fetched = lax.all_to_all(picked, "mem", split_axis=0, concat_axis=0, tiled=True)
    pool = holder_count * CAP
    row_of = entry_order // TOPB
    member = (
        jnp.zeros((blocks_here, pool), jnp.bool_).at[row_of, holder * CAP + slot_of].set(True)
    )
    bias = jnp.where(jnp.repeat(member, BLK, axis=1), 0.0, NEG_FILL).reshape(
        blocks_here, 1, pool * BLK
    )
    mixing = jnp.repeat(jax.nn.sigmoid(gate_logit), HD).reshape(1, groups * HD)
    attended = far_attention(
        projected_flat,
        before,
        fetched,
        bias,
        later,
        jnp.full((1, BLK), jnp.where(lax.axis_index("mem") > 0, 1.0, 0.0), jnp.float32),
        mixing,
    )
    partial = jnp.dot(attended, output_weight, preferred_element_type=jnp.float32)
    width = partial.shape[1] // 4
    return jnp.concatenate(
        [reduce_over_tp(partial[:, k * width:(k + 1) * width]) for k in range(4)], axis=1
    ).astype(jnp.bfloat16)


def reduce_over_tp(partial):
    count = lax.axis_size("tp")
    chips = count // 2
    share = partial.shape[0] // count
    me = lax.axis_index("tp")
    core = me % 2
    chip = me // 2
    split = partial.reshape(chips, 2, share, partial.shape[1])
    mine = lax.dynamic_index_in_dim(split, core, axis=1, keepdims=False)
    other = lax.dynamic_index_in_dim(split, 1 - core, axis=1, keepdims=False)
    arrived = lax.ppermute(
        other.astype(jnp.bfloat16), "tp", [(t, t ^ 1) for t in range(count)]
    )
    chip_sum = mine + arrived.astype(jnp.float32)
    total = lax.dynamic_index_in_dim(chip_sum, chip, axis=0, keepdims=False)
    for shift in range(1, chips):
        outgoing = lax.dynamic_index_in_dim(chip_sum, (chip + shift) % chips, axis=0, keepdims=False)
        pairs = [(t, ((t // 2 + shift) % chips) * 2 + t % 2) for t in range(count)]
        total = total + lax.ppermute(outgoing.astype(jnp.bfloat16), "tp", pairs).astype(jnp.float32)
    return total

def solution(mesh):
    placed = (
        P(("mem", "tp"), None),
        P(None, "tp"),
        P("tp", None),
        P("tp"),
        P(None, "mem", "tp"),
        P("mem", None),
        P(),
    )
    return jax.shard_map(
        local, mesh=mesh, in_specs=placed, out_specs=P(("mem", "tp"), None), check_vma=False
    )
```
